32 devices in a mesh: groups: 2 (over x), dp: 8 (over z, y), ctx: 2 (over core).
Axes of the slice: x: 2, y: 2, z: 4, core: 2. Of those that a mesh axis runs over, the one named last changes fastest.
Arguments:
- queries: bfloat16 [16, 768, 2048], P(('groups', 'dp'), 'ctx'), parts along dimension 0, may hold values from -8 to 8
- keys: bfloat16 [16, 768, 512], P(('groups', 'dp'), 'ctx'), parts along dimension 0, may hold values from -8 to 8
- values: bfloat16 [16, 768, 512], P(('groups', 'dp'), 'ctx'), parts along dimension 0, may hold values from -6 to 6
- out_grad: bfloat16 [16, 768, 2048], P(('groups', 'dp'), 'ctx'), parts along dimension 0, may hold values from -6 to 6
- key_weight: bfloat16 [4096, 512], P('ctx'), may hold values from -0.09375 to 0.09375
- value_weight: bfloat16 [4096, 512], P('ctx'), may hold values from -0.09375 to 0.09375
- suffix_embed: bfloat16 [32, 8, 4096], P(('groups', 'dp'), None, 'ctx'), parts along dimension 0, may hold values from -6 to 6
- class_ids: int32 [16], P(('groups', 'dp')), parts along dimension 0, may hold values from 0 to 15
- class_slot: int32 [32], P('groups'), parts along dimension 0, may hold values from 0 to 15, each once
- pad_offset: int32 [16], P(('groups', 'dp')), parts along dimension 0, may hold values from 0 to 384, as said below
- suffix_pos: int32 [16, 8], P(('groups', 'dp')), parts along dimension 0, may hold values from 0 to 767, as said below
Outputs:
- query_grad: bfloat16 [16, 768, 2048], P(('groups', 'dp'), 'ctx'), parts along dimension 0
- key_grad: bfloat16 [16, 768, 512], P(('groups', 'dp'), 'ctx'), parts along dimension 0
- value_grad: bfloat16 [16, 768, 512], P(('groups', 'dp'), 'ctx'), parts along dimension 0
- suffix_grad: float32 [32, 8, 4096], P(('groups', 'dp'), None, 'ctx'), parts along dimension 0
The draws below stay inside these ranges and needn't reach their ends.
There are 2 independent parts, one for each index of `groups`. The reference program is written for one: setup_inputs(seed, part) draws one part's arguments, and reference() takes and returns one part's arrays. A program takes and returns all parts, laid end to end along the dimension named above; an argument that names none is the same for every part. Nothing has to cross between parts.
Inputs may be any that keep to these rules, and one draw needn't show every extreme that they name: `class_slot`: each class gets a distinct slot. `pad_offset`: reached by some prompt. `suffix_pos`: every suffix position of a prompt is at least its pad_offset; the smallest and the largest are reached.
All inputs are finite; a program needn't handle non-finite values.
Results may differ from the reference program's by a relative error of at most 0.039.
Values may be sent and summed in bfloat16 or wider, within the bound.
No kernel may reach another device: no remote copies, remote signals or barrier semaphores. Data moves between devices by JAX's collectives and lax.ppermute only.
A program may use at most 128 MiB of HBM per device.

```python
import jax
import jax.numpy as jnp
from jax import lax

D = 4096
HEADS = 16
KV_HEADS = 4
HEAD_DIM = 128
SUFFIX = 8
GROUP = 4
LENGTH = 768
SAMPLES = 8
CLASSES = 16


def draw_queries(key, part):
    base = jnp.clip(jax.random.normal(jax.random.fold_in(key, 1), (SAMPLES, LENGTH, HEADS * HEAD_DIM), jnp.float32), -6.0, 6.0)
    return base.astype(jnp.bfloat16)


def draw_keys(key, part):
    base = jnp.clip(jax.random.normal(jax.random.fold_in(key, 2), (SAMPLES, LENGTH, KV_HEADS * HEAD_DIM), jnp.float32), -6.0, 6.0)
    return base.astype(jnp.bfloat16)


def offsets_of(key):
    raw_offset = jax.random.randint(jax.random.fold_in(key, 21), (SAMPLES,), 0, LENGTH // 2 + 1)
    chosen = jax.random.randint(jax.random.fold_in(key, 23), (), 0, SAMPLES)
    raw_offset = raw_offset.at[chosen].set(LENGTH // 2)
    return raw_offset.at[(chosen + 1) % SAMPLES].set(0).astype(jnp.int32)


def draw_pad_offset(key, part):
    return offsets_of(key)


def draw_suffix_pos(key, part):
    offsets = offsets_of(key)
    span_left = LENGTH - offsets
    raw_pos = jax.random.randint(jax.random.fold_in(key, 22), (SAMPLES, SUFFIX), 0, LENGTH)
    placed = offsets[:, None] + raw_pos % span_left[:, None]
    chosen = jax.random.randint(jax.random.fold_in(key, 24), (), 0, SAMPLES)
    placed = placed.at[chosen, 0].set(LENGTH - 1)
    unpadded = jnp.argmin(offsets)
    placed = placed.at[unpadded, SUFFIX - 1].set(0)
    return placed.astype(jnp.int32)


def place_ends(result, stream_key, low, largest):
    extent = result.shape
    spot = [jax.random.randint(jax.random.fold_in(stream_key, axis), (), 0, extent[axis]) for axis in range(len(extent))]
    result = result.at[tuple(spot)].set(low)
    longest = extent.index(max(extent))
    spot[longest] = (spot[longest] + 1) % extent[longest]
    return result.at[tuple(spot)].set(largest)


def block_scale(stream_key, shape, shards, low, top_value):
    def one(axis_at, parts):
        draws = jax.random.uniform(jax.random.fold_in(jax.random.fold_in(stream_key, 6), axis_at), (parts,), jnp.float32, low / len(shards), top_value / len(shards))
        return jnp.repeat(jnp.exp(draws), shape[axis_at] // parts).reshape((-1,) + (1,) * (len(shape) - axis_at - 1))

    loudness = one(*shards[0])
    for cut in shards[1:]:
        loudness = loudness * one(*cut)
    return loudness


def normal_values(key, extent, width, bound, pieces=(), kind=jnp.bfloat16):
    level = block_scale(key, extent, pieces, -0.22, 0.18) if pieces else 1.0
    values = jax.random.normal(key, extent, jnp.float32) * width * level
    return jnp.minimum(jnp.maximum(values, -bound), bound).astype(kind)


def setup_inputs(seed: int = 0, part: int = 0) -> dict:
    splits = jax.random.split(jax.random.key(seed), 12)
    own_keys = jax.random.split(jax.random.fold_in(splits[11], part), 12)
    queries = draw_queries(jax.random.fold_in(jax.random.fold_in(splits[11], part), 71), part)
    keys = draw_keys(jax.random.fold_in(jax.random.fold_in(splits[11], part), 71), part)
    values = normal_values(own_keys[2], (SAMPLES, LENGTH, KV_HEADS * HEAD_DIM), 1.0, 6.0, ((0, 8), (1, 2)))
    out_grad = normal_values(own_keys[3], (SAMPLES, LENGTH, HEADS * HEAD_DIM), 1.0, 6.0, ((0, 8), (1, 2)))
    key_weight = normal_values(splits[4], (D, KV_HEADS * HEAD_DIM), D ** -0.5, 0.09375, ((0, 2),))
    value_weight = normal_values(splits[5], (D, KV_HEADS * HEAD_DIM), D ** -0.5, 0.09375, ((0, 2),))
    suffix_embed = normal_values(own_keys[6], (CLASSES, SUFFIX, D), 1.0, 6.0, ((0, 8), (2, 2)))
    class_ids = place_ends(jax.random.randint(own_keys[7], (SAMPLES,), 0, CLASSES), jax.random.fold_in(own_keys[7], 1), 0, CLASSES - 1).astype(jnp.int32)
    class_slot = jax.random.permutation(own_keys[8], CLASSES).astype(jnp.int32)
    pad_offset = draw_pad_offset(jax.random.fold_in(jax.random.fold_in(splits[11], part), 71), part)
    suffix_pos = draw_suffix_pos(jax.random.fold_in(jax.random.fold_in(splits[11], part), 71), part)
    return {"queries": queries, "keys": keys, "values": values, "out_grad": out_grad, "key_weight": key_weight, "value_weight": value_weight, "suffix_embed": suffix_embed, "class_ids": class_ids, "class_slot": class_slot, "pad_offset": pad_offset, "suffix_pos": suffix_pos}


masked_fill = -1.0e30


def round_half(value):
    return lax.optimization_barrier(value.astype(jnp.bfloat16)).astype(jnp.float32)


def attend_one(operands):
    queries_one, kv_one, grads_one, suffix_one, offset, positions = operands
    scale = HEAD_DIM ** -0.5
    kv_width = KV_HEADS * HEAD_DIM
    token_pos = jnp.arange(LENGTH, dtype=jnp.int32)
    earlier = token_pos[None, :] <= token_pos[:, None]
    kept = (token_pos[None, :] >= offset) | (token_pos[None, :] == token_pos[:, None])
    suffix_seen = positions[None, :] <= token_pos[:, None]
    visible = jnp.concatenate([earlier & kept, suffix_seen], axis=1)
    every_kv = jnp.concatenate([kv_one, suffix_one], axis=0).astype(jnp.float32)
    dq_list = []
    dk_list = []
    dv_list = []
    for kv_head in range(KV_HEADS):
        low = kv_head * GROUP * HEAD_DIM
        high = (kv_head + 1) * GROUP * HEAD_DIM
        query_part = queries_one[:, low:high].reshape(LENGTH, GROUP, HEAD_DIM).astype(jnp.float32)
        grad_part = grads_one[:, low:high].reshape(LENGTH, GROUP, HEAD_DIM).astype(jnp.float32)
        keys_part = every_kv[:, kv_head * HEAD_DIM:(kv_head + 1) * HEAD_DIM]
        values_part = every_kv[:, kv_width + kv_head * HEAD_DIM:kv_width + (kv_head + 1) * HEAD_DIM]
        scores = jnp.einsum("pgd,jd->gpj", query_part, keys_part, precision=lax.Precision.HIGHEST) * scale
        scores = jnp.where(visible[None], scores, masked_fill)
        row_max = jnp.max(scores, axis=2)
        expo = jnp.exp(scores - row_max[:, :, None])
        total = jnp.sum(expo, axis=2)
        mixed = jnp.einsum("gpj,jd->pgd", round_half(expo), values_part, precision=lax.Precision.HIGHEST)
        attended = round_half(mixed / total.T[:, :, None])
        delta = jnp.sum(grad_part * attended, axis=2).T
        probs = expo / total[:, :, None]
        prob_grad = jnp.einsum("pgd,jd->gpj", grad_part, values_part, precision=lax.Precision.HIGHEST)
        score_grad = round_half(probs * (prob_grad - delta[:, :, None]))
        query_piece = jnp.einsum("gpj,jd->pgd", score_grad, keys_part, precision=lax.Precision.HIGHEST)
        dq_list.append(query_piece.reshape(LENGTH, GROUP * HEAD_DIM) * scale)
        dk_list.append(jnp.einsum("gpj,pgd->jd", score_grad, query_part, precision=lax.Precision.HIGHEST) * scale)
        dv_list.append(jnp.einsum("gpj,pgd->jd", round_half(probs), grad_part, precision=lax.Precision.HIGHEST))
    query_grad = jnp.concatenate(dq_list, axis=1).astype(jnp.bfloat16)
    every_grad = jnp.concatenate(dk_list + dv_list, axis=1)
    return query_grad, every_grad[:LENGTH], every_grad[LENGTH:]


def reference(queries, keys, values, out_grad, key_weight, value_weight, suffix_embed, class_ids, class_slot, pad_offset, suffix_pos):
    kv_width = KV_HEADS * HEAD_DIM
    slots = class_slot[class_ids]
    chosen = suffix_embed[slots].astype(jnp.float32)
    key_full = key_weight.astype(jnp.float32)
    value_full = value_weight.astype(jnp.float32)
    suffix_keys = jnp.einsum("bsd,dk->bsk", chosen, key_full, precision=lax.Precision.HIGHEST)
    suffix_values = jnp.einsum("bsd,dk->bsk", chosen, value_full, precision=lax.Precision.HIGHEST)
    suffix_kv = jnp.concatenate([suffix_keys, suffix_values], axis=2).astype(jnp.bfloat16)
    every_kv = jnp.concatenate([keys, values], axis=2)
    query_grad, prompt_grad, suffix_grads = lax.map(attend_one, (queries, every_kv, out_grad, suffix_kv, pad_offset, suffix_pos))
    contrib = jnp.einsum("bsk,dk->bsd", suffix_grads[:, :, :kv_width], key_full, precision=lax.Precision.HIGHEST)
    contrib = contrib + jnp.einsum("bsk,dk->bsd", suffix_grads[:, :, kv_width:], value_full, precision=lax.Precision.HIGHEST)
    suffix_grad = jnp.zeros((CLASSES, SUFFIX, D), jnp.float32).at[slots].add(contrib)
    key_grad = prompt_grad[:, :, :kv_width].astype(jnp.bfloat16)
    value_grad = prompt_grad[:, :, kv_width:].astype(jnp.bfloat16)
    return (query_grad, key_grad, value_grad, suffix_grad)
```

```python
import functools
import jax
import jax.numpy as jnp
from jax import lax
from jax.experimental import pallas as pl
from jax.experimental.pallas import tpu as pltpu
from jax.sharding import PartitionSpec as P

HEAD_DIM = 128
masked_fill = -1e30


def passed_along(block, axis, distance):
    devices = range(lax.axis_size(axis))
    route = [(i - distance, i) for i in devices if i - distance in devices]
    return lax.ppermute(block, axis, route)


def attention_kernel(q_ref, do_ref, k_ref, v_ref, keep_ref, dq_ref, dk_ref, dv_ref, *, scale):
    member = pl.program_id(1)
    q = q_ref[...]
    grad = do_ref[...]
    k = k_ref[...]
    v = v_ref[...]
    nt = (((1,), (1,)), ((), ()))
    tn = (((0,), (0,)), ((), ()))
    scores = lax.dot_general(q, k, nt, preferred_element_type=jnp.float32) * scale
    scores = jnp.where(keep_ref[...] > 0.5, scores, masked_fill)
    row_max = jnp.max(scores, axis=1, keepdims=True)
    expo = jnp.exp(scores - row_max)
    total = jnp.sum(expo, axis=1, keepdims=True)
    mixed = jnp.dot(expo.astype(jnp.bfloat16), v, preferred_element_type=jnp.float32)
    attended = (mixed / total).astype(jnp.bfloat16)
    delta = jnp.sum(grad.astype(jnp.float32) * attended.astype(jnp.float32), axis=1, keepdims=True)
    probs = expo / total
    prob_grad = lax.dot_general(grad, v, nt, preferred_element_type=jnp.float32)
    score_grad = (probs * (prob_grad - delta)).astype(jnp.bfloat16)
    query_piece = jnp.dot(score_grad, k, preferred_element_type=jnp.float32)
    dq_ref[...] = (query_piece * scale).astype(dq_ref.dtype)
    key_piece = lax.dot_general(score_grad, q, tn, preferred_element_type=jnp.float32) * scale
    value_piece = lax.dot_general(probs.astype(jnp.bfloat16), grad, tn, preferred_element_type=jnp.float32)

    @pl.when(member == 0)
    def _():
        dk_ref[...] = key_piece
        dv_ref[...] = value_piece

    @pl.when(member > 0)
    def _():
        dk_ref[...] += key_piece
        dv_ref[...] += value_piece


def attend(queries2d, grads2d, every_kv, keep, kv_heads, group):
    tok_rows = queries2d.shape[0]
    n_keys = every_kv.shape[0]
    scale = HEAD_DIM ** (-0.5)
    kernel = functools.partial(attention_kernel, scale=scale)
    row_spec = pl.BlockSpec((tok_rows, HEAD_DIM), lambda h, g: (0, h * group + g))
    return pl.pallas_call(
        kernel,
        grid=(kv_heads, group),
        in_specs=[
            row_spec,
            row_spec,
            pl.BlockSpec((n_keys, HEAD_DIM), lambda h, g: (0, h)),
            pl.BlockSpec((n_keys, HEAD_DIM), lambda h, g: (0, kv_heads + h)),
            pl.BlockSpec((tok_rows, n_keys), lambda h, g: (0, 0)),
        ],
        out_specs=[
            row_spec,
            pl.BlockSpec((n_keys, HEAD_DIM), lambda h, g: (0, h)),
            pl.BlockSpec((n_keys, HEAD_DIM), lambda h, g: (0, h)),
        ],
        out_shape=[
            jax.ShapeDtypeStruct(queries2d.shape, jnp.bfloat16),
            jax.ShapeDtypeStruct((n_keys, kv_heads * HEAD_DIM), jnp.float32),
            jax.ShapeDtypeStruct((n_keys, kv_heads * HEAD_DIM), jnp.float32),
        ],
        compiler_params=pltpu.CompilerParams(dimension_semantics=("arbitrary", "arbitrary")),
    )(queries2d, grads2d, every_kv, every_kv, keep)


def per_device(
    queries,
    keys,
    values,
    out_grad,
    key_weight,
    value_weight,
    suffix_embed,
    class_ids,
    class_slot,
    pad_offset,
    suffix_pos,
):
    cycle_size = lax.axis_size("ctx")
    cycle_rank = lax.axis_index("ctx")
    tok_rows = queries.shape[1]
    kv_width = keys.shape[2]
    kv_heads = kv_width // HEAD_DIM
    group = queries.shape[2] // kv_width
    suffix_len = suffix_embed.shape[1]
    classes = class_slot.shape[0]
    slot_ids = jnp.arange(classes, dtype=jnp.int32)
    picked = jnp.sum(jnp.where(slot_ids == class_ids[0], class_slot, 0))
    slot_onehot = (slot_ids == picked).astype(jnp.float32)
    table = lax.all_gather(suffix_embed, "dp", axis=0, tiled=True)
    chosen = lax.dynamic_index_in_dim(table, picked, 0, keepdims=False)
    partial_kv = jnp.concatenate(
        [
            jnp.dot(chosen, key_weight, preferred_element_type=jnp.float32),
            jnp.dot(chosen, value_weight, preferred_element_type=jnp.float32),
        ],
        axis=1,
    )
    suffix_kv = lax.psum(partial_kv, "ctx").astype(jnp.bfloat16)
    query_pos = cycle_rank * tok_rows + jnp.arange(tok_rows, dtype=jnp.int32)
    offset = pad_offset[0]
    local_kv = jnp.concatenate([keys[0], values[0]], axis=1)
    prev_kv = passed_along(local_kv, "ctx", 1)
    pad_rows = (-(2 * tok_rows + suffix_len)) % 128
    every_kv = jnp.concatenate(
        [local_kv, prev_kv, suffix_kv, jnp.zeros((pad_rows, 2 * kv_width), jnp.bfloat16)], axis=0
    )
    rows = jnp.arange(tok_rows, dtype=jnp.int32)
    far = jnp.full((pad_rows,), 1 << 30, jnp.int32)
    key_pos = jnp.concatenate(
        [
            cycle_rank * tok_rows + rows,
            ((cycle_rank - 1) % cycle_size) * tok_rows + rows,
            suffix_pos[0],
            far,
        ]
    )
    earlier = key_pos[None, :] <= query_pos[:, None]
    kept = (key_pos[None, :] >= offset) | (key_pos[None, :] == query_pos[:, None])
    keep = (earlier & kept).astype(jnp.float32)
    dq, dk, dv = attend(queries[0], out_grad[0], every_kv, keep, kv_heads, group)
    suffix_dkv = jnp.concatenate(
        [dk[2 * tok_rows : 2 * tok_rows + suffix_len], dv[2 * tok_rows : 2 * tok_rows + suffix_len]], axis=1
    )
    key_full = key_weight.astype(jnp.float32)
    value_full = value_weight.astype(jnp.float32)
    summed_dkv = lax.psum(suffix_dkv, "ctx")
    contrib = jnp.einsum(
        "sk,dk->sd", summed_dkv[:, :kv_width], key_full, precision=lax.Precision.HIGHEST
    )
    contrib = contrib + jnp.einsum(
        "sk,dk->sd", summed_dkv[:, kv_width:], value_full, precision=lax.Precision.HIGHEST
    )
    bucket = slot_onehot[:, None, None] * contrib[None]
    suffix_grad = lax.psum_scatter(bucket, "dp", scatter_dimension=0, tiled=True)
    back_k = passed_along(dk[tok_rows : 2 * tok_rows], "ctx", -1)
    back_v = passed_along(dv[tok_rows : 2 * tok_rows], "ctx", -1)
    key_grad = (dk[:tok_rows] + back_k).astype(jnp.bfloat16)[None]
    value_grad = (dv[:tok_rows] + back_v).astype(jnp.bfloat16)[None]
    return (dq[None], key_grad, value_grad, suffix_grad)


def solution(mesh):
    return jax.shard_map(
        per_device,
        mesh=mesh,
        in_specs=(
            P(("groups", "dp"), "ctx", None),
            P(("groups", "dp"), "ctx", None),
            P(("groups", "dp"), "ctx", None),
            P(("groups", "dp"), "ctx", None),
            P("ctx", None),
            P("ctx", None),
            P(("groups", "dp"), None, "ctx"),
            P(("groups", "dp")),
            P("groups"),
            P(("groups", "dp")),
            P(("groups", "dp"), None),
        ),
        out_specs=(
            P(("groups", "dp"), "ctx", None),
            P(("groups", "dp"), "ctx", None),
            P(("groups", "dp"), "ctx", None),
            P(("groups", "dp"), None, "ctx"),
        ),
        check_vma=False,
    )
```

```python
import functools
import jax
import jax.numpy as jnp
from jax import lax
from jax.experimental import pallas as pl
from jax.experimental.pallas import tpu as pltpu
from jax.sharding import PartitionSpec as P

HEAD_DIM = 128
masked_fill = -1e30


def passed_along(block, axis, distance):
    devices = range(lax.axis_size(axis))
    route = [(i - distance, i) for i in devices if i - distance in devices]
    return lax.ppermute(block, axis, route)


def attention_kernel(q_ref, do_ref, k_ref, v_ref, keep_ref, dq_ref, dk_ref, dv_ref, *, scale):
    member = pl.program_id(1)
    q = q_ref[...]
    grad = do_ref[...]
    k = k_ref[...]
    v = v_ref[...]
    nt = (((1,), (1,)), ((), ()))
    tn = (((0,), (0,)), ((), ()))
    scores = lax.dot_general(q, k, nt, preferred_element_type=jnp.float32) * scale
    scores = jnp.where(keep_ref[...] > 0.5, scores, masked_fill)
    row_max = jnp.max(scores, axis=1, keepdims=True)
    expo = jnp.exp(scores - row_max)
    total = jnp.sum(expo, axis=1, keepdims=True)
    mixed = jnp.dot(expo.astype(jnp.bfloat16), v, preferred_element_type=jnp.float32)
    attended = (mixed / total).astype(jnp.bfloat16)
    delta = jnp.sum(grad.astype(jnp.float32) * attended.astype(jnp.float32), axis=1, keepdims=True)
    probs = expo / total
    prob_grad = lax.dot_general(grad, v, nt, preferred_element_type=jnp.float32)
    score_grad = (probs * (prob_grad - delta)).astype(jnp.bfloat16)
    query_piece = jnp.dot(score_grad, k, preferred_element_type=jnp.float32)
    dq_ref[...] = (query_piece * scale).astype(dq_ref.dtype)
    key_piece = lax.dot_general(score_grad, q, tn, preferred_element_type=jnp.float32) * scale
    value_piece = lax.dot_general(probs.astype(jnp.bfloat16), grad, tn, preferred_element_type=jnp.float32)

    @pl.when(member == 0)
    def _():
        dk_ref[...] = key_piece
        dv_ref[...] = value_piece

    @pl.when(member > 0)
    def _():
        dk_ref[...] += key_piece
        dv_ref[...] += value_piece


def attend(queries2d, grads2d, every_kv, keep, kv_heads, group):
    tok_rows = queries2d.shape[0]
    n_keys = every_kv.shape[0]
    scale = HEAD_DIM ** (-0.5)
    kernel = functools.partial(attention_kernel, scale=scale)
    row_spec = pl.BlockSpec((tok_rows, HEAD_DIM), lambda h, g: (0, h * group + g))
    return pl.pallas_call(
        kernel,
        grid=(kv_heads, group),
        in_specs=[
            row_spec,
            row_spec,
            pl.BlockSpec((n_keys, HEAD_DIM), lambda h, g: (0, h)),
            pl.BlockSpec((n_keys, HEAD_DIM), lambda h, g: (0, kv_heads + h)),
            pl.BlockSpec((tok_rows, n_keys), lambda h, g: (0, 0)),
        ],
        out_specs=[
            row_spec,
            pl.BlockSpec((n_keys, HEAD_DIM), lambda h, g: (0, h)),
            pl.BlockSpec((n_keys, HEAD_DIM), lambda h, g: (0, h)),
        ],
        out_shape=[
            jax.ShapeDtypeStruct(queries2d.shape, jnp.bfloat16),
            jax.ShapeDtypeStruct((n_keys, kv_heads * HEAD_DIM), jnp.float32),
            jax.ShapeDtypeStruct((n_keys, kv_heads * HEAD_DIM), jnp.float32),
        ],
        compiler_params=pltpu.CompilerParams(dimension_semantics=("arbitrary", "arbitrary")),
    )(queries2d, grads2d, every_kv, every_kv, keep)


def swapped(block, axis):
    devices = range(lax.axis_size(axis))
    route = [(i, i ^ 1) for i in devices]
    return lax.ppermute(block, axis, route)


def shifted(block, axis, distance):
    devices = range(lax.axis_size(axis))
    route = [(i, (i + distance) % len(devices)) for i in devices]
    return lax.ppermute(block, axis, route)


def per_device(
    queries,
    keys,
    values,
    out_grad,
    key_weight,
    value_weight,
    suffix_embed,
    class_ids,
    class_slot,
    pad_offset,
    suffix_pos,
):
    cycle_size = lax.axis_size("ctx")
    cycle_rank = lax.axis_index("ctx")
    owners = lax.axis_size("dp")
    owner_rank = lax.axis_index("dp")
    tok_rows = queries.shape[1]
    kv_width = keys.shape[2]
    kv_heads = kv_width // HEAD_DIM
    group = queries.shape[2] // kv_width
    own_slots = suffix_embed.shape[0]
    suffix_len = suffix_embed.shape[1]
    classes = class_slot.shape[0]
    slot_ids = jnp.arange(classes, dtype=jnp.int32)
    picked = jnp.sum(jnp.where(slot_ids == class_ids[0], class_slot, 0))
    owned_kv = jnp.concatenate(
        [
            jnp.einsum("sld,dk->slk", suffix_embed, key_weight, preferred_element_type=jnp.float32),
            jnp.einsum("sld,dk->slk", suffix_embed, value_weight, preferred_element_type=jnp.float32),
        ],
        axis=2,
    )
    owned_kv = (owned_kv + swapped(owned_kv, "ctx")).astype(jnp.bfloat16)
    arrived = [owned_kv] + [shifted(owned_kv, "dp", step) for step in range(1, owners)]
    source_step = (owner_rank - picked // own_slots) % owners
    suffix_kv = jnp.stack(arrived)[source_step, picked % own_slots]
    query_pos = cycle_rank * tok_rows + jnp.arange(tok_rows, dtype=jnp.int32)
    offset = pad_offset[0]
    local_kv = jnp.concatenate([keys[0], values[0]], axis=1)
    prev_kv = passed_along(local_kv, "ctx", 1)
    pad_rows = (-(2 * tok_rows + suffix_len)) % 128
    every_kv = jnp.concatenate(
        [local_kv, prev_kv, suffix_kv, jnp.zeros((pad_rows, 2 * kv_width), jnp.bfloat16)], axis=0
    )
    rows = jnp.arange(tok_rows, dtype=jnp.int32)
    far = jnp.full((pad_rows,), 1 << 30, jnp.int32)
    key_pos = jnp.concatenate(
        [
            cycle_rank * tok_rows + rows,
            ((cycle_rank - 1) % cycle_size) * tok_rows + rows,
            suffix_pos[0],
            far,
        ]
    )
    earlier = key_pos[None, :] <= query_pos[:, None]
    kept = (key_pos[None, :] >= offset) | (key_pos[None, :] == query_pos[:, None])
    keep = (earlier & kept).astype(jnp.float32)
    dq, dk, dv = attend(queries[0], out_grad[0], every_kv, keep, kv_heads, group)
    suffix_dkv = jnp.concatenate(
        [dk[2 * tok_rows : 2 * tok_rows + suffix_len], dv[2 * tok_rows : 2 * tok_rows + suffix_len]], axis=1
    )
    summed_dkv = suffix_dkv + swapped(suffix_dkv, "ctx")
    local_ids = jnp.arange(own_slots, dtype=jnp.int32)
    slot_total = None
    for step in range(owners):
        target = (owner_rank + step) % owners
        wanted = (picked == target * own_slots + local_ids)[:, None, None]
        sent = jnp.where(wanted, summed_dkv[None], 0.0)
        if step:
            sent = shifted(sent, "dp", step)
        slot_total = sent if slot_total is None else slot_total + sent
    key_full = key_weight.astype(jnp.float32)
    value_full = value_weight.astype(jnp.float32)
    suffix_grad = jnp.einsum(
        "slk,dk->sld", slot_total[:, :, :kv_width], key_full, precision=lax.Precision.HIGHEST
    )
    suffix_grad = suffix_grad + jnp.einsum(
        "slk,dk->sld", slot_total[:, :, kv_width:], value_full, precision=lax.Precision.HIGHEST
    )
    back_k = passed_along(dk[tok_rows : 2 * tok_rows], "ctx", -1)
    back_v = passed_along(dv[tok_rows : 2 * tok_rows], "ctx", -1)
    key_grad = (dk[:tok_rows] + back_k).astype(jnp.bfloat16)[None]
    value_grad = (dv[:tok_rows] + back_v).astype(jnp.bfloat16)[None]
    return (dq[None], key_grad, value_grad, suffix_grad)


def solution(mesh):
    return jax.shard_map(
        per_device,
        mesh=mesh,
        in_specs=(
            P(("groups", "dp"), "ctx", None),
            P(("groups", "dp"), "ctx", None),
            P(("groups", "dp"), "ctx", None),
            P(("groups", "dp"), "ctx", None),
            P("ctx", None),
            P("ctx", None),
            P(("groups", "dp"), None, "ctx"),
            P(("groups", "dp")),
            P("groups"),
            P(("groups", "dp")),
            P(("groups", "dp"), None),
        ),
        out_specs=(
            P(("groups", "dp"), "ctx", None),
            P(("groups", "dp"), "ctx", None),
            P(("groups", "dp"), "ctx", None),
            P(("groups", "dp"), None, "ctx"),
        ),
        check_vma=False,
    )
```

```python
import functools
import jax
import jax.numpy as jnp
from jax import lax
from jax.experimental import pallas as pl
from jax.experimental.pallas import tpu as pltpu
from jax.sharding import PartitionSpec as P

HEAD_DIM = 128
masked_fill = -1e30


def passed_along(block, axis, distance):
    devices = range(lax.axis_size(axis))
    route = [(i - distance, i) for i in devices if i - distance in devices]
    return lax.ppermute(block, axis, route)


def swapped(block, axis):
    devices = range(lax.axis_size(axis))
    route = [(i, i ^ 1) for i in devices]
    return lax.ppermute(block, axis, route)


def shifted(block, axis, distance):
    devices = range(lax.axis_size(axis))
    route = [(i, (i + distance) % len(devices)) for i in devices]
    return lax.ppermute(block, axis, route)


def gathered(block, axis):
    size = lax.axis_size(axis)
    held = block[None]
    if size & (size - 1):
        return jnp.stack([block] + [shifted(block, axis, step) for step in range(1, size)])
    distance = 1
    while distance < size:
        held = jnp.concatenate([held, shifted(held, axis, distance)], axis=0)
        distance *= 2
    return held


def attention_kernel(
    q_ref, do_ref, k_ref, v_ref, bias_ref,
    dq_ref, dk_local_ref, dv_local_ref, dk_prev_ref, dv_prev_ref, dk_suffix_ref, dv_suffix_ref,
    *, scale, tok_rows, suffix_len,
):
    member = pl.program_id(1)
    q = q_ref[...]
    grad = do_ref[...]
    k = k_ref[...]
    v = v_ref[...]
    nt = (((1,), (1,)), ((), ()))
    tn = (((0,), (0,)), ((), ()))
    scores = lax.dot_general(q, k, nt, preferred_element_type=jnp.float32) * scale + bias_ref[...]
    row_max = jnp.max(scores, axis=1, keepdims=True)
    expo = jnp.exp(scores - row_max)
    total = jnp.sum(expo, axis=1, keepdims=True)
    inverse = 1.0 / total
    mixed = jnp.dot(expo.astype(jnp.bfloat16), v, preferred_element_type=jnp.float32)
    attended = (mixed * inverse).astype(jnp.bfloat16)
    delta = jnp.sum(grad.astype(jnp.float32) * attended.astype(jnp.float32), axis=1, keepdims=True)
    probs = expo * inverse
    prob_grad = lax.dot_general(grad, v, nt, preferred_element_type=jnp.float32)
    score_grad = (probs * (prob_grad - delta)).astype(jnp.bfloat16)
    query_piece = jnp.dot(score_grad, k, preferred_element_type=jnp.float32)
    dq_ref[...] = (query_piece * scale).astype(dq_ref.dtype)
    key_piece = lax.dot_general(score_grad, q, tn, preferred_element_type=jnp.float32) * scale
    value_piece = lax.dot_general(probs.astype(jnp.bfloat16), grad, tn, preferred_element_type=jnp.float32)
    pieces = [
        (dk_local_ref, key_piece[:tok_rows]),
        (dv_local_ref, value_piece[:tok_rows]),
        (dk_prev_ref, key_piece[tok_rows : 2 * tok_rows]),
        (dv_prev_ref, value_piece[tok_rows : 2 * tok_rows]),
        (dk_suffix_ref, key_piece[2 * tok_rows : 2 * tok_rows + suffix_len]),
        (dv_suffix_ref, value_piece[2 * tok_rows : 2 * tok_rows + suffix_len]),
    ]

    @pl.when(member == 0)
    def _():
        for ref, piece in pieces:
            ref[...] = piece

    @pl.when(member > 0)
    def _():
        for ref, piece in pieces:
            ref[...] += piece


def attend(queries2d, grads2d, every_kv, bias, kv_heads, group, suffix_len):
    tok_rows = queries2d.shape[0]
    n_keys = every_kv.shape[0]
    scale = HEAD_DIM ** (-0.5)
    kernel = functools.partial(attention_kernel, scale=scale, tok_rows=tok_rows, suffix_len=suffix_len)
    row_spec = pl.BlockSpec((tok_rows, HEAD_DIM), lambda h, g: (0, h * group + g))
    head_spec = pl.BlockSpec((tok_rows, HEAD_DIM), lambda h, g: (0, h))
    suffix_spec = pl.BlockSpec((suffix_len, HEAD_DIM), lambda h, g: (0, h))
    width = kv_heads * HEAD_DIM
    return pl.pallas_call(
        kernel,
        grid=(kv_heads, group),
        in_specs=[
            row_spec,
            row_spec,
            pl.BlockSpec((n_keys, HEAD_DIM), lambda h, g: (0, h)),
            pl.BlockSpec((n_keys, HEAD_DIM), lambda h, g: (0, kv_heads + h)),
            pl.BlockSpec((tok_rows, n_keys), lambda h, g: (0, 0)),
        ],
        out_specs=[row_spec, head_spec, head_spec, head_spec, head_spec, suffix_spec, suffix_spec],
        out_shape=[jax.ShapeDtypeStruct(queries2d.shape, jnp.bfloat16)]
        + [jax.ShapeDtypeStruct((tok_rows, width), jnp.float32)] * 4
        + [jax.ShapeDtypeStruct((suffix_len, width), jnp.float32)] * 2,
        compiler_params=pltpu.CompilerParams(dimension_semantics=("arbitrary", "arbitrary")),
    )(queries2d, grads2d, every_kv, every_kv, bias)


def per_device(
    queries,
    keys,
    values,
    out_grad,
    key_weight,
    value_weight,
    suffix_embed,
    class_ids,
    class_slot,
    pad_offset,
    suffix_pos,
):
    cycle_size = lax.axis_size("ctx")
    cycle_rank = lax.axis_index("ctx")
    owners = lax.axis_size("dp")
    owner_rank = lax.axis_index("dp")
    tok_rows = queries.shape[1]
    kv_width = keys.shape[2]
    kv_heads = kv_width // HEAD_DIM
    group = queries.shape[2] // kv_width
    own_slots = suffix_embed.shape[0]
    suffix_len = suffix_embed.shape[1]
    classes = class_slot.shape[0]
    slot_ids = jnp.arange(classes, dtype=jnp.int32)
    picked = jnp.sum(jnp.where(slot_ids == class_ids[0], class_slot, 0))
    owned_kv = jnp.concatenate(
        [
            jnp.einsum("sld,dk->slk", suffix_embed, key_weight, preferred_element_type=jnp.float32),
            jnp.einsum("sld,dk->slk", suffix_embed, value_weight, preferred_element_type=jnp.float32),
        ],
        axis=2,
    )
    owned_kv = (owned_kv + swapped(owned_kv, "ctx")).astype(jnp.bfloat16)
    source_step = (owner_rank - picked // own_slots) % owners
    suffix_kv = gathered(owned_kv, "dp")[source_step, picked % own_slots]
    query_pos = cycle_rank * tok_rows + jnp.arange(tok_rows, dtype=jnp.int32)
    offset = pad_offset[0]
    local_kv = jnp.concatenate([keys[0], values[0]], axis=1)
    prev_kv = passed_along(local_kv, "ctx", 1)
    pad_rows = (-(2 * tok_rows + suffix_len)) % 128
    every_kv = jnp.concatenate(
        [local_kv, prev_kv, suffix_kv, jnp.zeros((pad_rows, 2 * kv_width), jnp.bfloat16)], axis=0
    )
    rows = jnp.arange(tok_rows, dtype=jnp.int32)
    far = jnp.full((pad_rows,), 1 << 30, jnp.int32)
    key_pos = jnp.concatenate(
        [
            cycle_rank * tok_rows + rows,
            ((cycle_rank - 1) % cycle_size) * tok_rows + rows,
            suffix_pos[0],
            far,
        ]
    )
    earlier = key_pos[None, :] <= query_pos[:, None]
    kept = (key_pos[None, :] >= offset) | (key_pos[None, :] == query_pos[:, None])
    bias = jnp.where(earlier & kept, 0.0, masked_fill).astype(jnp.float32)
    dq, dk_local, dv_local, dk_prev, dv_prev, dk_suffix, dv_suffix = attend(
        queries[0], out_grad[0], every_kv, bias, kv_heads, group, suffix_len
    )
    back_k = passed_along(dk_prev, "ctx", -1)
    back_v = passed_along(dv_prev, "ctx", -1)
    suffix_dkv = jnp.concatenate([dk_suffix, dv_suffix], axis=1)
    summed_dkv = suffix_dkv + swapped(suffix_dkv, "ctx")
    tagged = jnp.concatenate(
        [summed_dkv, jnp.full((1, 2 * kv_width), picked.astype(jnp.float32))], axis=0
    )
    arrived = gathered(tagged, "dp")
    local_ids = owner_rank * own_slots + jnp.arange(own_slots, dtype=jnp.int32)
    wanted = arrived[:, suffix_len, 0][:, None] == local_ids.astype(jnp.float32)[None, :]
    slot_total = jnp.sum(
        jnp.where(wanted[:, :, None, None], arrived[:, None, :suffix_len], 0.0), axis=0
    )
    key_full = key_weight.astype(jnp.float32)
    value_full = value_weight.astype(jnp.float32)
    suffix_grad = jnp.einsum(
        "slk,dk->sld", slot_total[:, :, :kv_width], key_full, precision=lax.Precision.HIGHEST
    )
    suffix_grad = suffix_grad + jnp.einsum(
        "slk,dk->sld", slot_total[:, :, kv_width:], value_full, precision=lax.Precision.HIGHEST
    )
    key_grad = (dk_local + back_k).astype(jnp.bfloat16)[None]
    value_grad = (dv_local + back_v).astype(jnp.bfloat16)[None]
    return (dq[None], key_grad, value_grad, suffix_grad)


def solution(mesh):
    return jax.shard_map(
        per_device,
        mesh=mesh,
        in_specs=(
            P(("groups", "dp"), "ctx", None),
            P(("groups", "dp"), "ctx", None),
            P(("groups", "dp"), "ctx", None),
            P(("groups", "dp"), "ctx", None),
            P("ctx", None),
            P("ctx", None),
            P(("groups", "dp"), None, "ctx"),
            P(("groups", "dp")),
            P("groups"),
            P(("groups", "dp")),
            P(("groups", "dp"), None),
        ),
        out_specs=(
            P(("groups", "dp"), "ctx", None),
            P(("groups", "dp"), "ctx", None),
            P(("groups", "dp"), "ctx", None),
            P(("groups", "dp"), None, "ctx"),
        ),
        check_vma=False,
    )
```

```python
import functools
import jax
import jax.numpy as jnp
from jax import lax
from jax.experimental import pallas as pl
from jax.experimental.pallas import tpu as pltpu
from jax.sharding import PartitionSpec as P

HEAD_DIM = 128
masked_fill = -1e30


def passed_along(block, axis, distance):
    devices = range(lax.axis_size(axis))
    route = [(i - distance, i) for i in devices if i - distance in devices]
    return lax.ppermute(block, axis, route)


def swapped(block, axis):
    devices = range(lax.axis_size(axis))
    route = [(i, i ^ 1) for i in devices]
    return lax.ppermute(block, axis, route)


def shifted(block, axis, distance):
    devices = range(lax.axis_size(axis))
    route = [(i, (i + distance) % len(devices)) for i in devices]
    return lax.ppermute(block, axis, route)


def gathered(block, axis):
    size = lax.axis_size(axis)
    held = block[None]
    if size & (size - 1):
        return jnp.stack([block] + [shifted(block, axis, step) for step in range(1, size)])
    distance = 1
    while distance < size:
        held = jnp.concatenate([held, shifted(held, axis, distance)], axis=0)
        distance *= 2
    return held


def column_of(ref, lane):
    return jnp.sum(jnp.where(lane, ref[...], 0.0), axis=1, keepdims=True)


def prompt_kernel(q_ref, k_ref, v_ref, bias_ref, mixed_ref, max_ref, total_ref, *, scale, group):
    head = pl.program_id(0) * group + pl.program_id(1)

    @pl.when(head == 0)
    def _():
        max_ref[...] = jnp.zeros_like(max_ref)
        total_ref[...] = jnp.zeros_like(total_ref)

    nt = (((1,), (1,)), ((), ()))
    scores = lax.dot_general(q_ref[...], k_ref[...], nt, preferred_element_type=jnp.float32) * scale
    scores = scores + bias_ref[...]
    row_max = jnp.max(scores, axis=1, keepdims=True)
    expo = jnp.exp(scores - row_max)
    total = jnp.sum(expo, axis=1, keepdims=True)
    mixed_ref[...] = jnp.dot(expo.astype(jnp.bfloat16), v_ref[...], preferred_element_type=jnp.float32)
    lane = lax.broadcasted_iota(jnp.int32, max_ref.shape, 1) == head
    max_ref[...] = jnp.where(lane, row_max, max_ref[...])
    total_ref[...] = jnp.where(lane, total, total_ref[...])


def backward_kernel(
    q_ref, do_ref, k_ref, v_ref, bias_ref, max_ref, inverse_ref, delta_ref,
    dq_ref, dk_local_ref, dv_local_ref, dk_prev_ref, dv_prev_ref,
    *, scale, tok_rows, group,
):
    member = pl.program_id(1)
    head = pl.program_id(0) * group + member
    lane = lax.broadcasted_iota(jnp.int32, max_ref.shape, 1) == head
    row_max = column_of(max_ref, lane)
    inverse = column_of(inverse_ref, lane)
    delta = column_of(delta_ref, lane)
    q = q_ref[...]
    grad = do_ref[...]
    k = k_ref[...]
    v = v_ref[...]
    nt = (((1,), (1,)), ((), ()))
    tn = (((0,), (0,)), ((), ()))
    scores = lax.dot_general(q, k, nt, preferred_element_type=jnp.float32) * scale + bias_ref[...]
    probs = jnp.exp(scores - row_max) * inverse
    prob_grad = lax.dot_general(grad, v, nt, preferred_element_type=jnp.float32)
    score_grad = (probs * (prob_grad - delta)).astype(jnp.bfloat16)
    query_piece = jnp.dot(score_grad, k, preferred_element_type=jnp.float32)
    dq_ref[...] = (query_piece * scale).astype(dq_ref.dtype)
    key_piece = lax.dot_general(score_grad, q, tn, preferred_element_type=jnp.float32) * scale
    value_piece = lax.dot_general(probs.astype(jnp.bfloat16), grad, tn, preferred_element_type=jnp.float32)
    pieces = [
        (dk_local_ref, key_piece[:tok_rows]),
        (dv_local_ref, value_piece[:tok_rows]),
        (dk_prev_ref, key_piece[tok_rows : 2 * tok_rows]),
        (dv_prev_ref, value_piece[tok_rows : 2 * tok_rows]),
    ]

    @pl.when(member == 0)
    def _():
        for ref, piece in pieces:
            ref[...] = piece

    @pl.when(member > 0)
    def _():
        for ref, piece in pieces:
            ref[...] += piece


def attend_prompt(queries2d, prompt_kv, bias, kv_heads, group):
    tok_rows = queries2d.shape[0]
    n_keys = prompt_kv.shape[0]
    heads = kv_heads * group
    kernel = functools.partial(prompt_kernel, scale=HEAD_DIM ** (-0.5), group=group)
    row_spec = pl.BlockSpec((tok_rows, HEAD_DIM), lambda h, g: (0, h * group + g))
    stat_spec = pl.BlockSpec((tok_rows, heads), lambda h, g: (0, 0))
    return pl.pallas_call(
        kernel,
        grid=(kv_heads, group),
        in_specs=[
            row_spec,
            pl.BlockSpec((n_keys, HEAD_DIM), lambda h, g: (0, h)),
            pl.BlockSpec((n_keys, HEAD_DIM), lambda h, g: (0, kv_heads + h)),
            pl.BlockSpec((tok_rows, n_keys), lambda h, g: (0, 0)),
        ],
        out_specs=[row_spec, stat_spec, stat_spec],
        out_shape=[
            jax.ShapeDtypeStruct(queries2d.shape, jnp.float32),
            jax.ShapeDtypeStruct((tok_rows, heads), jnp.float32),
            jax.ShapeDtypeStruct((tok_rows, heads), jnp.float32),
        ],
        compiler_params=pltpu.CompilerParams(dimension_semantics=("arbitrary", "arbitrary")),
        cost_estimate=pl.CostEstimate(
            flops=4 * tok_rows * n_keys * HEAD_DIM * heads,
            transcendentals=tok_rows * n_keys * heads,
            bytes_accessed=2 * queries2d.size + 2 * prompt_kv.size + 4 * bias.size + 4 * queries2d.size,
        ),
    )(queries2d, prompt_kv, prompt_kv, bias)


def attend_backward(queries2d, grads2d, every_kv, bias, row_max, inverse, delta, kv_heads, group):
    tok_rows = queries2d.shape[0]
    n_keys = every_kv.shape[0]
    heads = kv_heads * group
    kernel = functools.partial(backward_kernel, scale=HEAD_DIM ** (-0.5), tok_rows=tok_rows, group=group)
    row_spec = pl.BlockSpec((tok_rows, HEAD_DIM), lambda h, g: (0, h * group + g))
    head_spec = pl.BlockSpec((tok_rows, HEAD_DIM), lambda h, g: (0, h))
    stat_spec = pl.BlockSpec((tok_rows, heads), lambda h, g: (0, 0))
    width = kv_heads * HEAD_DIM
    return pl.pallas_call(
        kernel,
        grid=(kv_heads, group),
        in_specs=[
            row_spec,
            row_spec,
            pl.BlockSpec((n_keys, HEAD_DIM), lambda h, g: (0, h)),
            pl.BlockSpec((n_keys, HEAD_DIM), lambda h, g: (0, kv_heads + h)),
            pl.BlockSpec((tok_rows, n_keys), lambda h, g: (0, 0)),
            stat_spec,
            stat_spec,
            stat_spec,
        ],
        out_specs=[row_spec, head_spec, head_spec, head_spec, head_spec],
        out_shape=[jax.ShapeDtypeStruct(queries2d.shape, jnp.bfloat16)]
        + [jax.ShapeDtypeStruct((tok_rows, width), jnp.float32)] * 4,
        compiler_params=pltpu.CompilerParams(dimension_semantics=("arbitrary", "arbitrary")),
        cost_estimate=pl.CostEstimate(
            flops=10 * tok_rows * n_keys * HEAD_DIM * heads,
            transcendentals=tok_rows * n_keys * heads,
            bytes_accessed=6 * queries2d.size + 2 * every_kv.size + 4 * bias.size + 16 * tok_rows * width,
        ),
    )(queries2d, grads2d, every_kv, every_kv, bias, row_max, inverse, delta)


def per_device(
    queries,
    keys,
    values,
    out_grad,
    key_weight,
    value_weight,
    suffix_embed,
    class_ids,
    class_slot,
    pad_offset,
    suffix_pos,
):
    cycle_size = lax.axis_size("ctx")
    cycle_rank = lax.axis_index("ctx")
    owners = lax.axis_size("dp")
    owner_rank = lax.axis_index("dp")
    tok_rows = queries.shape[1]
    kv_width = keys.shape[2]
    kv_heads = kv_width // HEAD_DIM
    group = queries.shape[2] // kv_width
    own_slots = suffix_embed.shape[0]
    suffix_len = suffix_embed.shape[1]
    classes = class_slot.shape[0]
    slot_ids = jnp.arange(classes, dtype=jnp.int32)
    picked = jnp.sum(jnp.where(slot_ids == class_ids[0], class_slot, 0))
    owned_kv = jnp.concatenate(
        [
            jnp.einsum("sld,dk->slk", suffix_embed, key_weight, preferred_element_type=jnp.float32),
            jnp.einsum("sld,dk->slk", suffix_embed, value_weight, preferred_element_type=jnp.float32),
        ],
        axis=2,
    )
    owned_kv = (owned_kv + swapped(owned_kv, "ctx")).astype(jnp.bfloat16)
    source_step = (owner_rank - picked // own_slots) % owners
    arrived = [owned_kv] + [shifted(owned_kv, "dp", step) for step in range(1, owners)]
    suffix_kv = jnp.stack(arrived)[source_step, picked % own_slots]
    query_pos = cycle_rank * tok_rows + jnp.arange(tok_rows, dtype=jnp.int32)
    offset = pad_offset[0]
    scale = HEAD_DIM ** (-0.5)
    heads = kv_heads * group
    local_kv = jnp.concatenate([keys[0], values[0]], axis=1)
    prev_kv = passed_along(local_kv, "ctx", 1)
    prompt_kv = jnp.concatenate([local_kv, prev_kv], axis=0)
    pad_rows = (-(2 * tok_rows + suffix_len)) % 128
    rows = jnp.arange(tok_rows, dtype=jnp.int32)
    far = jnp.full((pad_rows,), 1 << 30, jnp.int32)
    key_pos = jnp.concatenate(
        [
            cycle_rank * tok_rows + rows,
            ((cycle_rank - 1) % cycle_size) * tok_rows + rows,
            suffix_pos[0],
            far,
        ]
    )
    earlier = key_pos[None, :] <= query_pos[:, None]
    kept = (key_pos[None, :] >= offset) | (key_pos[None, :] == query_pos[:, None])
    seen = earlier & kept
    bias = jnp.where(seen, 0.0, masked_fill).astype(jnp.float32)
    prompt_mixed, prompt_max, prompt_total = attend_prompt(
        queries[0], prompt_kv, bias[:, : 2 * tok_rows], kv_heads, group
    )
    query_heads = queries[0].reshape(tok_rows, heads, HEAD_DIM)
    grad_heads = out_grad[0].reshape(tok_rows, heads, HEAD_DIM)
    suffix_keys = jnp.repeat(suffix_kv[:, :kv_width].reshape(suffix_len, kv_heads, HEAD_DIM), group, axis=1)
    suffix_values = jnp.repeat(suffix_kv[:, kv_width:].reshape(suffix_len, kv_heads, HEAD_DIM), group, axis=1)
    suffix_scores = (
        jnp.einsum("phd,thd->pht", query_heads, suffix_keys, preferred_element_type=jnp.float32) * scale
    )
    suffix_seen = seen[:, 2 * tok_rows : 2 * tok_rows + suffix_len]
    suffix_scores = jnp.where(suffix_seen[:, None, :], suffix_scores, masked_fill)
    row_max = jnp.maximum(prompt_max, jnp.max(suffix_scores, axis=2))
    rescale = jnp.exp(prompt_max - row_max)
    suffix_expo = jnp.exp(suffix_scores - row_max[:, :, None])
    total = prompt_total * rescale + jnp.sum(suffix_expo, axis=2)
    inverse = 1.0 / total
    mixed = prompt_mixed.reshape(tok_rows, heads, HEAD_DIM) * rescale[:, :, None] + jnp.einsum(
        "pht,thd->phd", suffix_expo.astype(jnp.bfloat16), suffix_values, preferred_element_type=jnp.float32
    )
    attended = (mixed * inverse[:, :, None]).astype(jnp.bfloat16)
    delta = jnp.sum(grad_heads.astype(jnp.float32) * attended.astype(jnp.float32), axis=2)
    suffix_probs = suffix_expo * inverse[:, :, None]
    suffix_prob_grad = jnp.einsum(
        "phd,thd->pht", grad_heads, suffix_values, preferred_element_type=jnp.float32
    )
    suffix_score_grad = (suffix_probs * (suffix_prob_grad - delta[:, :, None])).astype(jnp.bfloat16)
    dk_suffix = jnp.einsum(
        "pkgt,pkgd->tkd",
        suffix_score_grad.reshape(tok_rows, kv_heads, group, suffix_len),
        query_heads.reshape(tok_rows, kv_heads, group, HEAD_DIM),
        preferred_element_type=jnp.float32,
    ).reshape(suffix_len, kv_width) * scale
    dv_suffix = jnp.einsum(
        "pkgt,pkgd->tkd",
        suffix_probs.astype(jnp.bfloat16).reshape(tok_rows, kv_heads, group, suffix_len),
        grad_heads.reshape(tok_rows, kv_heads, group, HEAD_DIM),
        preferred_element_type=jnp.float32,
    ).reshape(suffix_len, kv_width)
    every_kv = jnp.concatenate(
        [prompt_kv, suffix_kv, jnp.zeros((pad_rows, 2 * kv_width), jnp.bfloat16)], axis=0
    )
    dq, dk_local, dv_local, dk_prev, dv_prev = attend_backward(
        queries[0], out_grad[0], every_kv, bias, row_max, inverse, delta, kv_heads, group
    )
    back_k = passed_along(dk_prev, "ctx", -1)
    back_v = passed_along(dv_prev, "ctx", -1)
    suffix_dkv = jnp.concatenate([dk_suffix, dv_suffix], axis=1)
    summed_dkv = suffix_dkv + swapped(suffix_dkv, "ctx")
    local_ids = jnp.arange(own_slots, dtype=jnp.int32)
    slot_total = None
    for step in range(owners):
        target = (owner_rank + step) % owners
        wanted = (picked == target * own_slots + local_ids)[:, None, None]
        sent = jnp.where(wanted, summed_dkv[None], 0.0)
        if step:
            sent = shifted(sent, "dp", step)
        slot_total = sent if slot_total is None else slot_total + sent
    key_full = key_weight.astype(jnp.float32)
    value_full = value_weight.astype(jnp.float32)
    suffix_grad = jnp.einsum(
        "slk,dk->sld", slot_total[:, :, :kv_width], key_full, precision=lax.Precision.HIGHEST
    )
    suffix_grad = suffix_grad + jnp.einsum(
        "slk,dk->sld", slot_total[:, :, kv_width:], value_full, precision=lax.Precision.HIGHEST
    )
    key_grad = (dk_local + back_k).astype(jnp.bfloat16)[None]
    value_grad = (dv_local + back_v).astype(jnp.bfloat16)[None]
    return (dq[None], key_grad, value_grad, suffix_grad)


def solution(mesh):
    return jax.shard_map(
        per_device,
        mesh=mesh,
        in_specs=(
            P(("groups", "dp"), "ctx", None),
            P(("groups", "dp"), "ctx", None),
            P(("groups", "dp"), "ctx", None),
            P(("groups", "dp"), "ctx", None),
            P("ctx", None),
            P("ctx", None),
            P(("groups", "dp"), None, "ctx"),
            P(("groups", "dp")),
            P("groups"),
            P(("groups", "dp")),
            P(("groups", "dp"), None),
        ),
        out_specs=(
            P(("groups", "dp"), "ctx", None),
            P(("groups", "dp"), "ctx", None),
            P(("groups", "dp"), "ctx", None),
            P(("groups", "dp"), None, "ctx"),
        ),
        check_vma=False,
    )
```

```python
import functools
import jax
import jax.numpy as jnp
from jax import lax
from jax.experimental import pallas as pl
from jax.experimental.pallas import tpu as pltpu
from jax.sharding import PartitionSpec as P

HEAD_DIM = 128
masked_fill = -1e30


def passed_along(block, axis, distance):
    devices = range(lax.axis_size(axis))
    route = [(i - distance, i) for i in devices if i - distance in devices]
    return lax.ppermute(block, axis, route)


def swapped(block, axis):
    devices = range(lax.axis_size(axis))
    route = [(i, i ^ 1) for i in devices]
    return lax.ppermute(block, axis, route)


def shifted(block, axis, distance):
    devices = range(lax.axis_size(axis))
    route = [(i, (i + distance) % len(devices)) for i in devices]
    return lax.ppermute(block, axis, route)


def paired_gather(block, axis):
    size = lax.axis_size(axis)
    pair = jnp.stack([block, swapped(block, axis)])
    return jnp.stack([pair] + [shifted(pair, axis, 2 * step) for step in range(1, size // 2)])


def attention_kernel(
    q_ref, do_ref, k_ref, v_ref, bias_ref,
    dq_ref, dk_local_ref, dv_local_ref, dk_prev_ref, dv_prev_ref, dk_suffix_ref, dv_suffix_ref,
    *, scale, tok_rows, suffix_len,
):
    member = pl.program_id(1)
    q = q_ref[...]
    grad = do_ref[...]
    k = k_ref[...]
    v = v_ref[...]
    nt = (((1,), (1,)), ((), ()))
    tn = (((0,), (0,)), ((), ()))
    scores = lax.dot_general(q, k, nt, preferred_element_type=jnp.float32) * scale + bias_ref[...]
    row_max = jnp.max(scores, axis=1, keepdims=True)
    expo = jnp.exp(scores - row_max)
    total = jnp.sum(expo, axis=1, keepdims=True)
    inverse = 1.0 / total
    mixed = jnp.dot(expo.astype(jnp.bfloat16), v, preferred_element_type=jnp.float32)
    attended = (mixed * inverse).astype(jnp.bfloat16)
    delta = jnp.sum(grad.astype(jnp.float32) * attended.astype(jnp.float32), axis=1, keepdims=True)
    probs = expo * inverse
    prob_grad = lax.dot_general(grad, v, nt, preferred_element_type=jnp.float32)
    score_grad = (probs * (prob_grad - delta)).astype(jnp.bfloat16)
    query_piece = jnp.dot(score_grad, k, preferred_element_type=jnp.float32)
    dq_ref[...] = (query_piece * scale).astype(dq_ref.dtype)
    key_piece = lax.dot_general(score_grad, q, tn, preferred_element_type=jnp.float32) * scale
    value_piece = lax.dot_general(probs.astype(jnp.bfloat16), grad, tn, preferred_element_type=jnp.float32)
    pieces = [
        (dk_local_ref, key_piece[:tok_rows]),
        (dv_local_ref, value_piece[:tok_rows]),
        (dk_prev_ref, key_piece[tok_rows : 2 * tok_rows]),
        (dv_prev_ref, value_piece[tok_rows : 2 * tok_rows]),
        (dk_suffix_ref, key_piece[2 * tok_rows : 2 * tok_rows + suffix_len]),
        (dv_suffix_ref, value_piece[2 * tok_rows : 2 * tok_rows + suffix_len]),
    ]

    @pl.when(member == 0)
    def _():
        for ref, piece in pieces:
            ref[...] = piece

    @pl.when(member > 0)
    def _():
        for ref, piece in pieces:
            ref[...] += piece


def attend(queries2d, grads2d, every_kv, bias, kv_heads, group, suffix_len):
    tok_rows = queries2d.shape[0]
    n_keys = every_kv.shape[0]
    scale = HEAD_DIM ** (-0.5)
    kernel = functools.partial(attention_kernel, scale=scale, tok_rows=tok_rows, suffix_len=suffix_len)
    row_spec = pl.BlockSpec((tok_rows, HEAD_DIM), lambda h, g: (0, h * group + g))
    head_spec = pl.BlockSpec((tok_rows, HEAD_DIM), lambda h, g: (0, h))
    suffix_spec = pl.BlockSpec((suffix_len, HEAD_DIM), lambda h, g: (0, h))
    width = kv_heads * HEAD_DIM
    return pl.pallas_call(
        kernel,
        grid=(kv_heads, group),
        in_specs=[
            row_spec,
            row_spec,
            pl.BlockSpec((n_keys, HEAD_DIM), lambda h, g: (0, h)),
            pl.BlockSpec((n_keys, HEAD_DIM), lambda h, g: (0, kv_heads + h)),
            pl.BlockSpec((tok_rows, n_keys), lambda h, g: (0, 0)),
        ],
        out_specs=[row_spec, head_spec, head_spec, head_spec, head_spec, suffix_spec, suffix_spec],
        out_shape=[jax.ShapeDtypeStruct(queries2d.shape, jnp.bfloat16)]
        + [jax.ShapeDtypeStruct((tok_rows, width), jnp.float32)] * 4
        + [jax.ShapeDtypeStruct((suffix_len, width), jnp.float32)] * 2,
        compiler_params=pltpu.CompilerParams(dimension_semantics=("arbitrary", "arbitrary")),
        cost_estimate=pl.CostEstimate(
            flops=12 * tok_rows * n_keys * HEAD_DIM * kv_heads * group,
            transcendentals=tok_rows * n_keys * kv_heads * group,
            bytes_accessed=6 * queries2d.size + 2 * every_kv.size + 4 * bias.size + 16 * tok_rows * width,
        ),
    )(queries2d, grads2d, every_kv, every_kv, bias)


def per_device(
    queries,
    keys,
    values,
    out_grad,
    key_weight,
    value_weight,
    suffix_embed,
    class_ids,
    class_slot,
    pad_offset,
    suffix_pos,
):
    cycle_size = lax.axis_size("ctx")
    cycle_rank = lax.axis_index("ctx")
    owners = lax.axis_size("dp")
    owner_rank = lax.axis_index("dp")
    tok_rows = queries.shape[1]
    kv_width = keys.shape[2]
    kv_heads = kv_width // HEAD_DIM
    group = queries.shape[2] // kv_width
    own_slots = suffix_embed.shape[0]
    suffix_len = suffix_embed.shape[1]
    classes = class_slot.shape[0]
    slot_ids = jnp.arange(classes, dtype=jnp.int32)
    picked = jnp.sum(jnp.where(slot_ids == class_ids[0], class_slot, 0))
    owned_kv = jnp.concatenate(
        [
            jnp.einsum("sld,dk->slk", suffix_embed, key_weight, preferred_element_type=jnp.float32),
            jnp.einsum("sld,dk->slk", suffix_embed, value_weight, preferred_element_type=jnp.float32),
        ],
        axis=2,
    )
    owned_kv = (owned_kv + swapped(owned_kv, "ctx")).astype(jnp.bfloat16)
    owner = picked // own_slots
    partner = (owner_rank ^ owner) & 1
    source_step = ((owner_rank - (owner ^ partner)) % owners) // 2
    suffix_kv = paired_gather(owned_kv, "dp")[source_step, partner, picked % own_slots]
    query_pos = cycle_rank * tok_rows + jnp.arange(tok_rows, dtype=jnp.int32)
    offset = pad_offset[0]
    local_kv = jnp.concatenate([keys[0], values[0]], axis=1)
    prev_kv = passed_along(local_kv, "ctx", 1)
    pad_rows = (-(2 * tok_rows + suffix_len)) % 128
    every_kv = jnp.concatenate(
        [local_kv, prev_kv, suffix_kv, jnp.zeros((pad_rows, 2 * kv_width), jnp.bfloat16)], axis=0
    )
    rows = jnp.arange(tok_rows, dtype=jnp.int32)
    far = jnp.full((pad_rows,), 1 << 30, jnp.int32)
    key_pos = jnp.concatenate(
        [
            cycle_rank * tok_rows + rows,
            ((cycle_rank - 1) % cycle_size) * tok_rows + rows,
            suffix_pos[0],
            far,
        ]
    )
    earlier = key_pos[None, :] <= query_pos[:, None]
    kept = (key_pos[None, :] >= offset) | (key_pos[None, :] == query_pos[:, None])
    bias = jnp.where(earlier & kept, 0.0, masked_fill).astype(jnp.float32)
    dq, dk_local, dv_local, dk_prev, dv_prev, dk_suffix, dv_suffix = attend(
        queries[0], out_grad[0], every_kv, bias, kv_heads, group, suffix_len
    )
    back_k = passed_along(dk_prev, "ctx", -1)
    back_v = passed_along(dv_prev, "ctx", -1)
    suffix_dkv = jnp.concatenate([dk_suffix, dv_suffix], axis=1)
    summed_dkv = suffix_dkv + swapped(suffix_dkv, "ctx")
    local_ids = jnp.arange(own_slots, dtype=jnp.int32)
    pair_ids = jnp.arange(2, dtype=jnp.int32)
    collected = None
    for step in range(owners // 2):
        target = (owner_rank + 2 * step) % owners
        wanted = picked == ((target ^ pair_ids)[:, None] * own_slots + local_ids[None, :])
        sent = jnp.where(wanted[:, :, None, None], summed_dkv[None, None], 0.0)
        if step:
            sent = shifted(sent, "dp", 2 * step)
        collected = sent if collected is None else collected + sent
    slot_total = collected[0] + swapped(collected[1], "dp")
    key_full = key_weight.astype(jnp.float32)
    value_full = value_weight.astype(jnp.float32)
    suffix_grad = jnp.einsum(
        "slk,dk->sld", slot_total[:, :, :kv_width], key_full, precision=lax.Precision.HIGHEST
    )
    suffix_grad = suffix_grad + jnp.einsum(
        "slk,dk->sld", slot_total[:, :, kv_width:], value_full, precision=lax.Precision.HIGHEST
    )
    key_grad = (dk_local + back_k).astype(jnp.bfloat16)[None]
    value_grad = (dv_local + back_v).astype(jnp.bfloat16)[None]
    return (dq[None], key_grad, value_grad, suffix_grad)


def solution(mesh):
    return jax.shard_map(
        per_device,
        mesh=mesh,
        in_specs=(
            P(("groups", "dp"), "ctx", None),
            P(("groups", "dp"), "ctx", None),
            P(("groups", "dp"), "ctx", None),
            P(("groups", "dp"), "ctx", None),
            P("ctx", None),
            P("ctx", None),
            P(("groups", "dp"), None, "ctx"),
            P(("groups", "dp")),
            P("groups"),
            P(("groups", "dp")),
            P(("groups", "dp"), None),
        ),
        out_specs=(
            P(("groups", "dp"), "ctx", None),
            P(("groups", "dp"), "ctx", None),
            P(("groups", "dp"), "ctx", None),
            P(("groups", "dp"), None, "ctx"),
        ),
        check_vma=False,
    )
```

```python
import functools
import jax
import jax.numpy as jnp
from jax import lax
from jax.experimental import pallas as pl
from jax.experimental.pallas import tpu as pltpu
from jax.sharding import PartitionSpec as P

HEAD_DIM = 128
masked_fill = -1e30


def passed_along(block, axis, distance):
    devices = range(lax.axis_size(axis))
    route = [(i - distance, i) for i in devices if i - distance in devices]
    return lax.ppermute(block, axis, route)


def swapped(block, axis):
    devices = range(lax.axis_size(axis))
    route = [(i, i ^ 1) for i in devices]
    return lax.ppermute(block, axis, route)


def shifted(block, axis, distance):
    devices = range(lax.axis_size(axis))
    route = [(i, (i + distance) % len(devices)) for i in devices]
    return lax.ppermute(block, axis, route)


def paired_gather(block, axis):
    size = lax.axis_size(axis)
    pair = jnp.stack([block, swapped(block, axis)])
    return jnp.stack([pair] + [shifted(pair, axis, 2 * step) for step in range(1, size // 2)])


def attention_kernel(
    q_ref, do_ref, kl_ref, vl_ref, kp_ref, vp_ref, ks_ref, vs_ref, bias_ref,
    dq_ref, dk_local_ref, dv_local_ref, dk_prev_ref, dv_prev_ref, dk_suffix_ref, dv_suffix_ref,
    *, scale, suffix_len,
):
    member = pl.program_id(1)
    q = q_ref[...]
    grad = do_ref[...]
    nt = (((1,), (1,)), ((), ()))
    tn = (((0,), (0,)), ((), ()))
    blocks = [(kl_ref[...], vl_ref[...]), (kp_ref[...], vp_ref[...]), (ks_ref[...], vs_ref[...])]
    scores = []
    low = 0
    for k, _ in blocks:
        high = low + k.shape[0]
        part = lax.dot_general(q, k, nt, preferred_element_type=jnp.float32) * scale
        scores.append(part + bias_ref[:, low:high])
        low = high
    row_max = scores[0].max(axis=1, keepdims=True)
    for part in scores[1:]:
        row_max = jnp.maximum(row_max, part.max(axis=1, keepdims=True))
    expos = [jnp.exp(part - row_max) for part in scores]
    total = sum(jnp.sum(e, axis=1, keepdims=True) for e in expos)
    inverse = 1.0 / total
    mixed = sum(
        jnp.dot(e.astype(jnp.bfloat16), v, preferred_element_type=jnp.float32)
        for e, (_, v) in zip(expos, blocks)
    )
    attended = (mixed * inverse).astype(jnp.bfloat16)
    delta = jnp.sum(grad.astype(jnp.float32) * attended.astype(jnp.float32), axis=1, keepdims=True)
    query_piece = None
    pieces = []
    for e, (k, v) in zip(expos, blocks):
        probs = e * inverse
        prob_grad = lax.dot_general(grad, v, nt, preferred_element_type=jnp.float32)
        score_grad = (probs * (prob_grad - delta)).astype(jnp.bfloat16)
        term = jnp.dot(score_grad, k, preferred_element_type=jnp.float32)
        query_piece = term if query_piece is None else query_piece + term
        key_piece = lax.dot_general(score_grad, q, tn, preferred_element_type=jnp.float32) * scale
        value_piece = lax.dot_general(probs.astype(jnp.bfloat16), grad, tn, preferred_element_type=jnp.float32)
        pieces.append((key_piece, value_piece))
    dq_ref[...] = (query_piece * scale).astype(dq_ref.dtype)
    writes = [
        (dk_local_ref, pieces[0][0]),
        (dv_local_ref, pieces[0][1]),
        (dk_prev_ref, pieces[1][0]),
        (dv_prev_ref, pieces[1][1]),
        (dk_suffix_ref, pieces[2][0][:suffix_len]),
        (dv_suffix_ref, pieces[2][1][:suffix_len]),
    ]

    @pl.when(member == 0)
    def _():
        for ref, piece in writes:
            ref[...] = piece

    @pl.when(member > 0)
    def _():
        for ref, piece in writes:
            ref[...] += piece


def attend(queries2d, grads2d, local_kv, prev_kv, suffix_block, bias, kv_heads, group, suffix_len):
    tok_rows = queries2d.shape[0]
    n_keys = bias.shape[1]
    scale = HEAD_DIM ** (-0.5)
    kernel = functools.partial(attention_kernel, scale=scale, suffix_len=suffix_len)
    row_spec = pl.BlockSpec((tok_rows, HEAD_DIM), lambda h, g: (0, h * group + g))
    head_spec = pl.BlockSpec((tok_rows, HEAD_DIM), lambda h, g: (0, h))
    suffix_spec = pl.BlockSpec((suffix_len, HEAD_DIM), lambda h, g: (0, h))
    width = kv_heads * HEAD_DIM

    def key_specs(block):
        rows = block.shape[0]
        return [
            pl.BlockSpec((rows, HEAD_DIM), lambda h, g: (0, h)),
            pl.BlockSpec((rows, HEAD_DIM), lambda h, g: (0, kv_heads + h)),
        ]

    return pl.pallas_call(
        kernel,
        grid=(kv_heads, group),
        in_specs=[row_spec, row_spec]
        + key_specs(local_kv)
        + key_specs(prev_kv)
        + key_specs(suffix_block)
        + [pl.BlockSpec((tok_rows, n_keys), lambda h, g: (0, 0))],
        out_specs=[row_spec, head_spec, head_spec, head_spec, head_spec, suffix_spec, suffix_spec],
        out_shape=[jax.ShapeDtypeStruct(queries2d.shape, jnp.bfloat16)]
        + [jax.ShapeDtypeStruct((tok_rows, width), jnp.float32)] * 4
        + [jax.ShapeDtypeStruct((suffix_len, width), jnp.float32)] * 2,
        compiler_params=pltpu.CompilerParams(dimension_semantics=("arbitrary", "arbitrary")),
        cost_estimate=pl.CostEstimate(
            flops=12 * tok_rows * n_keys * HEAD_DIM * kv_heads * group,
            transcendentals=tok_rows * n_keys * kv_heads * group,
            bytes_accessed=6 * queries2d.size + 2 * n_keys * 2 * width + 4 * bias.size + 16 * tok_rows * width,
        ),
    )(queries2d, grads2d, local_kv, local_kv, prev_kv, prev_kv, suffix_block, suffix_block, bias)


def per_device(
    queries,
    keys,
    values,
    out_grad,
    key_weight,
    value_weight,
    suffix_embed,
    class_ids,
    class_slot,
    pad_offset,
    suffix_pos,
):
    cycle_size = lax.axis_size("ctx")
    cycle_rank = lax.axis_index("ctx")
    owners = lax.axis_size("dp")
    owner_rank = lax.axis_index("dp")
    tok_rows = queries.shape[1]
    kv_width = keys.shape[2]
    kv_heads = kv_width // HEAD_DIM
    group = queries.shape[2] // kv_width
    own_slots = suffix_embed.shape[0]
    suffix_len = suffix_embed.shape[1]
    classes = class_slot.shape[0]
    slot_ids = jnp.arange(classes, dtype=jnp.int32)
    picked = jnp.sum(jnp.where(slot_ids == class_ids[0], class_slot, 0))
    owned_kv = jnp.concatenate(
        [
            jnp.einsum("sld,dk->slk", suffix_embed, key_weight, preferred_element_type=jnp.float32),
            jnp.einsum("sld,dk->slk", suffix_embed, value_weight, preferred_element_type=jnp.float32),
        ],
        axis=2,
    )
    owner = picked // own_slots
    partner = (owner_rank ^ owner) & 1
    source_step = ((owner_rank - (owner ^ partner)) % owners) // 2
    half_kv = paired_gather(owned_kv, "dp")[source_step, partner, picked % own_slots]
    suffix_kv = (half_kv + swapped(half_kv, "ctx")).astype(jnp.bfloat16)
    query_pos = cycle_rank * tok_rows + jnp.arange(tok_rows, dtype=jnp.int32)
    offset = pad_offset[0]
    local_kv = jnp.concatenate([keys[0], values[0]], axis=1)
    prev_kv = passed_along(local_kv, "ctx", 1)
    pad_rows = (-(2 * tok_rows + suffix_len)) % 128
    suffix_block = jnp.concatenate(
        [suffix_kv, jnp.zeros((pad_rows, 2 * kv_width), jnp.bfloat16)], axis=0
    )
    rows = jnp.arange(tok_rows, dtype=jnp.int32)
    far = jnp.full((pad_rows,), 1 << 30, jnp.int32)
    key_pos = jnp.concatenate(
        [
            cycle_rank * tok_rows + rows,
            ((cycle_rank - 1) % cycle_size) * tok_rows + rows,
            suffix_pos[0],
            far,
        ]
    )
    earlier = key_pos[None, :] <= query_pos[:, None]
    kept = (key_pos[None, :] >= offset) | (key_pos[None, :] == query_pos[:, None])
    bias = jnp.where(earlier & kept, 0.0, masked_fill).astype(jnp.float32)
    dq, dk_local, dv_local, dk_prev, dv_prev, dk_suffix, dv_suffix = attend(
        queries[0], out_grad[0], local_kv, prev_kv, suffix_block, bias, kv_heads, group, suffix_len
    )
    back_k = passed_along(dk_prev, "ctx", -1)
    back_v = passed_along(dv_prev, "ctx", -1)
    suffix_dkv = jnp.concatenate([dk_suffix, dv_suffix], axis=1)
    summed_dkv = suffix_dkv + swapped(suffix_dkv, "ctx")
    local_ids = jnp.arange(own_slots, dtype=jnp.int32)
    pair_ids = jnp.arange(2, dtype=jnp.int32)
    collected = None
    for step in range(owners // 2):
        target = (owner_rank + 2 * step) % owners
        wanted = picked == ((target ^ pair_ids)[:, None] * own_slots + local_ids[None, :])
        sent = jnp.where(wanted[:, :, None, None], summed_dkv[None, None], 0.0)
        if step:
            sent = shifted(sent, "dp", 2 * step)
        collected = sent if collected is None else collected + sent
    slot_total = collected[0] + swapped(collected[1], "dp")
    key_full = key_weight.astype(jnp.float32)
    value_full = value_weight.astype(jnp.float32)
    suffix_grad = jnp.einsum(
        "slk,dk->sld", slot_total[:, :, :kv_width], key_full, precision=lax.Precision.HIGHEST
    )
    suffix_grad = suffix_grad + jnp.einsum(
        "slk,dk->sld", slot_total[:, :, kv_width:], value_full, precision=lax.Precision.HIGHEST
    )
    key_grad = (dk_local + back_k).astype(jnp.bfloat16)[None]
    value_grad = (dv_local + back_v).astype(jnp.bfloat16)[None]
    return (dq[None], key_grad, value_grad, suffix_grad)


def solution(mesh):
    return jax.shard_map(
        per_device,
        mesh=mesh,
        in_specs=(
            P(("groups", "dp"), "ctx", None),
            P(("groups", "dp"), "ctx", None),
            P(("groups", "dp"), "ctx", None),
            P(("groups", "dp"), "ctx", None),
            P("ctx", None),
            P("ctx", None),
            P(("groups", "dp"), None, "ctx"),
            P(("groups", "dp")),
            P("groups"),
            P(("groups", "dp")),
            P(("groups", "dp"), None),
        ),
        out_specs=(
            P(("groups", "dp"), "ctx", None),
            P(("groups", "dp"), "ctx", None),
            P(("groups", "dp"), "ctx", None),
            P(("groups", "dp"), None, "ctx"),
        ),
        check_vma=False,
    )
```

```python
import functools
import jax
import jax.numpy as jnp
from jax import lax
from jax.experimental import pallas as pl
from jax.experimental.pallas import tpu as pltpu
from jax.sharding import PartitionSpec as P

HEAD_DIM = 128
masked_fill = -1e30


def passed_along(block, axis, distance):
    devices = range(lax.axis_size(axis))
    route = [(i - distance, i) for i in devices if i - distance in devices]
    return lax.ppermute(block, axis, route)


def swapped(block, axis):
    devices = range(lax.axis_size(axis))
    route = [(i, i ^ 1) for i in devices]
    return lax.ppermute(block, axis, route)


def shifted(block, axis, distance):
    devices = range(lax.axis_size(axis))
    route = [(i, (i + distance) % len(devices)) for i in devices]
    return lax.ppermute(block, axis, route)


def paired_gather(block, axis):
    size = lax.axis_size(axis)
    pair = jnp.stack([block, swapped(block, axis)])
    return jnp.stack([pair] + [shifted(pair, axis, 2 * step) for step in range(1, size // 2)])


def attention_kernel(
    q_ref, do_ref, k_ref, v_ref, bias_ref,
    dq_ref, dk_local_ref, dv_local_ref, dk_prev_ref, dv_prev_ref, dk_suffix_ref, dv_suffix_ref,
    *, scale, tok_rows, suffix_len,
):
    member = pl.program_id(1)
    q = q_ref[...]
    grad = do_ref[...]
    k = k_ref[...]
    v = v_ref[...]
    nt = (((1,), (1,)), ((), ()))
    tn = (((0,), (0,)), ((), ()))
    scores = lax.dot_general(q, k, nt, preferred_element_type=jnp.float32) * scale + bias_ref[...]
    row_max = jnp.max(scores, axis=1, keepdims=True)
    expo = jnp.exp(scores - row_max)
    total = jnp.sum(expo, axis=1, keepdims=True)
    inverse = 1.0 / total
    mixed = jnp.dot(expo.astype(jnp.bfloat16), v, preferred_element_type=jnp.float32)
    attended = (mixed * inverse).astype(jnp.bfloat16)
    delta = jnp.sum(grad.astype(jnp.float32) * attended.astype(jnp.float32), axis=1, keepdims=True)
    probs = expo * inverse
    prob_grad = lax.dot_general(grad, v, nt, preferred_element_type=jnp.float32)
    score_grad = (probs * (prob_grad - delta)).astype(jnp.bfloat16)
    query_piece = jnp.dot(score_grad, k, preferred_element_type=jnp.float32)
    dq_ref[...] = (query_piece * scale).astype(dq_ref.dtype)
    key_piece = lax.dot_general(score_grad, q, tn, preferred_element_type=jnp.float32) * scale
    value_piece = lax.dot_general(probs.astype(jnp.bfloat16), grad, tn, preferred_element_type=jnp.float32)
    pieces = [
        (dk_local_ref, key_piece[:tok_rows]),
        (dv_local_ref, value_piece[:tok_rows]),
        (dk_prev_ref, key_piece[tok_rows : 2 * tok_rows]),
        (dv_prev_ref, value_piece[tok_rows : 2 * tok_rows]),
        (dk_suffix_ref, key_piece[2 * tok_rows : 2 * tok_rows + suffix_len]),
        (dv_suffix_ref, value_piece[2 * tok_rows : 2 * tok_rows + suffix_len]),
    ]

    @pl.when(member == 0)
    def _():
        for ref, piece in pieces:
            ref[...] = piece

    @pl.when(member > 0)
    def _():
        for ref, piece in pieces:
            ref[...] += piece


def attend(queries2d, grads2d, every_kv, bias, kv_heads, group, suffix_len):
    tok_rows = queries2d.shape[0]
    n_keys = every_kv.shape[0]
    scale = HEAD_DIM ** (-0.5)
    kernel = functools.partial(attention_kernel, scale=scale, tok_rows=tok_rows, suffix_len=suffix_len)
    row_spec = pl.BlockSpec((tok_rows, HEAD_DIM), lambda h, g: (0, h * group + g))
    head_spec = pl.BlockSpec((tok_rows, HEAD_DIM), lambda h, g: (0, h))
    suffix_spec = pl.BlockSpec((suffix_len, HEAD_DIM), lambda h, g: (0, h))
    width = kv_heads * HEAD_DIM
    return pl.pallas_call(
        kernel,
        grid=(kv_heads, group),
        in_specs=[
            row_spec,
            row_spec,
            pl.BlockSpec((n_keys, HEAD_DIM), lambda h, g: (0, h)),
            pl.BlockSpec((n_keys, HEAD_DIM), lambda h, g: (0, kv_heads + h)),
            pl.BlockSpec((tok_rows, n_keys), lambda h, g: (0, 0)),
        ],
        out_specs=[row_spec, head_spec, head_spec, head_spec, head_spec, suffix_spec, suffix_spec],
        out_shape=[jax.ShapeDtypeStruct(queries2d.shape, jnp.bfloat16)]
        + [jax.ShapeDtypeStruct((tok_rows, width), jnp.float32)] * 4
        + [jax.ShapeDtypeStruct((suffix_len, width), jnp.float32)] * 2,
        compiler_params=pltpu.CompilerParams(dimension_semantics=("arbitrary", "arbitrary")),
        cost_estimate=pl.CostEstimate(
            flops=12 * tok_rows * n_keys * HEAD_DIM * kv_heads * group,
            transcendentals=tok_rows * n_keys * kv_heads * group,
            bytes_accessed=6 * queries2d.size + 2 * every_kv.size + 4 * bias.size + 16 * tok_rows * width,
        ),
    )(queries2d, grads2d, every_kv, every_kv, bias)


def per_device(
    queries,
    keys,
    values,
    out_grad,
    key_weight,
    value_weight,
    suffix_embed,
    class_ids,
    class_slot,
    pad_offset,
    suffix_pos,
):
    cycle_size = lax.axis_size("ctx")
    cycle_rank = lax.axis_index("ctx")
    owners = lax.axis_size("dp")
    owner_rank = lax.axis_index("dp")
    tok_rows = queries.shape[1]
    kv_width = keys.shape[2]
    kv_heads = kv_width // HEAD_DIM
    group = queries.shape[2] // kv_width
    own_slots = suffix_embed.shape[0]
    suffix_len = suffix_embed.shape[1]
    classes = class_slot.shape[0]
    slot_ids = jnp.arange(classes, dtype=jnp.int32)
    picked = jnp.sum(jnp.where(slot_ids == class_ids[0], class_slot, 0))
    owned_kv = jnp.concatenate(
        [
            jnp.einsum("sld,dk->slk", suffix_embed, key_weight, preferred_element_type=jnp.float32),
            jnp.einsum("sld,dk->slk", suffix_embed, value_weight, preferred_element_type=jnp.float32),
        ],
        axis=2,
    )
    owner = picked // own_slots
    partner = (owner_rank ^ owner) & 1
    source_step = ((owner_rank - (owner ^ partner)) % owners) // 2
    half_kv = paired_gather(owned_kv, "dp")[source_step, partner, picked % own_slots]
    suffix_kv = (half_kv + swapped(half_kv, "ctx")).astype(jnp.bfloat16)
    query_pos = cycle_rank * tok_rows + jnp.arange(tok_rows, dtype=jnp.int32)
    offset = pad_offset[0]
    local_kv = jnp.concatenate([keys[0], values[0]], axis=1)
    prev_kv = passed_along(local_kv, "ctx", 1)
    pad_rows = (-(2 * tok_rows + suffix_len)) % 128
    every_kv = jnp.concatenate(
        [local_kv, prev_kv, suffix_kv, jnp.zeros((pad_rows, 2 * kv_width), jnp.bfloat16)], axis=0
    )
    rows = jnp.arange(tok_rows, dtype=jnp.int32)
    far = jnp.full((pad_rows,), 1 << 30, jnp.int32)
    key_pos = jnp.concatenate(
        [
            cycle_rank * tok_rows + rows,
            ((cycle_rank - 1) % cycle_size) * tok_rows + rows,
            suffix_pos[0],
            far,
        ]
    )
    earlier = key_pos[None, :] <= query_pos[:, None]
    kept = (key_pos[None, :] >= offset) | (key_pos[None, :] == query_pos[:, None])
    bias = jnp.where(earlier & kept, 0.0, masked_fill).astype(jnp.float32)
    dq, dk_local, dv_local, dk_prev, dv_prev, dk_suffix, dv_suffix = attend(
        queries[0], out_grad[0], every_kv, bias, kv_heads, group, suffix_len
    )
    back_k = passed_along(dk_prev, "ctx", -1)
    back_v = passed_along(dv_prev, "ctx", -1)
    suffix_dkv = jnp.concatenate([dk_suffix, dv_suffix], axis=1)
    summed_dkv = suffix_dkv + swapped(suffix_dkv, "ctx")
    local_ids = jnp.arange(own_slots, dtype=jnp.int32)
    pair_ids = jnp.arange(2, dtype=jnp.int32)
    collected = None
    for step in range(owners // 2):
        target = (owner_rank + 2 * step) % owners
        wanted = picked == ((target ^ pair_ids)[:, None] * own_slots + local_ids[None, :])
        sent = jnp.where(wanted[:, :, None, None], summed_dkv[None, None], 0.0)
        if step:
            sent = shifted(sent, "dp", 2 * step)
        collected = sent if collected is None else collected + sent
    slot_total = collected[0] + swapped(collected[1], "dp")
    key_full = key_weight.astype(jnp.float32)
    value_full = value_weight.astype(jnp.float32)
    suffix_grad = jnp.einsum(
        "slk,dk->sld", slot_total[:, :, :kv_width], key_full, precision=lax.Precision.HIGHEST
    )
    suffix_grad = suffix_grad + jnp.einsum(
        "slk,dk->sld", slot_total[:, :, kv_width:], value_full, precision=lax.Precision.HIGHEST
    )
    key_grad = (dk_local + back_k).astype(jnp.bfloat16)[None]
    value_grad = (dv_local + back_v).astype(jnp.bfloat16)[None]
    return (dq[None], key_grad, value_grad, suffix_grad)


def solution(mesh):
    return jax.shard_map(
        per_device,
        mesh=mesh,
        in_specs=(
            P(("groups", "dp"), "ctx", None),
            P(("groups", "dp"), "ctx", None),
            P(("groups", "dp"), "ctx", None),
            P(("groups", "dp"), "ctx", None),
            P("ctx", None),
            P("ctx", None),
            P(("groups", "dp"), None, "ctx"),
            P(("groups", "dp")),
            P("groups"),
            P(("groups", "dp")),
            P(("groups", "dp"), None),
        ),
        out_specs=(
            P(("groups", "dp"), "ctx", None),
            P(("groups", "dp"), "ctx", None),
            P(("groups", "dp"), "ctx", None),
            P(("groups", "dp"), None, "ctx"),
        ),
        check_vma=False,
    )
```

```python
import functools
import jax
import jax.numpy as jnp
from jax import lax
from jax.experimental import pallas as pl
from jax.experimental.pallas import tpu as pltpu
from jax.sharding import PartitionSpec as P

HEAD_DIM = 128
masked_fill = -1e30


def passed_along(block, axis, distance):
    devices = range(lax.axis_size(axis))
    route = [(i - distance, i) for i in devices if i - distance in devices]
    return lax.ppermute(block, axis, route)


def swapped(block, axis):
    devices = range(lax.axis_size(axis))
    route = [(i, i ^ 1) for i in devices]
    return lax.ppermute(block, axis, route)


def shifted(block, axis, distance):
    devices = range(lax.axis_size(axis))
    route = [(i, (i + distance) % len(devices)) for i in devices]
    return lax.ppermute(block, axis, route)


def paired_gather(block, axis):
    size = lax.axis_size(axis)
    pair = jnp.stack([block, swapped(block, axis)])
    return jnp.stack([pair] + [shifted(pair, axis, 2 * step) for step in range(1, size // 2)])


def attention_kernel(
    q_ref, do_ref, k_ref, v_ref, bias_ref,
    dq_ref, dk_local_ref, dv_local_ref, dk_prev_ref, dv_prev_ref, dk_suffix_ref, dv_suffix_ref,
    *, scale, tok_rows, suffix_len,
):
    member = pl.program_id(1)
    q = q_ref[...]
    grad = do_ref[...]
    k = k_ref[...]
    v = v_ref[...]
    nt = (((1,), (1,)), ((), ()))
    tn = (((0,), (0,)), ((), ()))
    scores = lax.dot_general(k, q, nt, preferred_element_type=jnp.float32) * scale + bias_ref[...]
    row_max = jnp.max(scores, axis=0, keepdims=True)
    expo = jnp.exp(scores - row_max)
    total = jnp.sum(expo, axis=0, keepdims=True)
    inverse = 1.0 / total
    mixed = lax.dot_general(v, expo.astype(jnp.bfloat16), tn, preferred_element_type=jnp.float32)
    attended = (mixed * inverse).astype(jnp.bfloat16)
    grad_t = grad.astype(jnp.float32).T
    delta = jnp.sum(grad_t * attended.astype(jnp.float32), axis=0, keepdims=True)
    probs = expo * inverse
    prob_grad = lax.dot_general(v, grad, nt, preferred_element_type=jnp.float32)
    score_grad = (probs * (prob_grad - delta)).astype(jnp.bfloat16)
    query_piece = lax.dot_general(k, score_grad, tn, preferred_element_type=jnp.float32)
    dq_ref[...] = (query_piece.T * scale).astype(dq_ref.dtype)
    key_piece = jnp.dot(score_grad, q, preferred_element_type=jnp.float32) * scale
    value_piece = jnp.dot(probs.astype(jnp.bfloat16), grad, preferred_element_type=jnp.float32)
    pieces = [
        (dk_local_ref, key_piece[:tok_rows]),
        (dv_local_ref, value_piece[:tok_rows]),
        (dk_prev_ref, key_piece[tok_rows : 2 * tok_rows]),
        (dv_prev_ref, value_piece[tok_rows : 2 * tok_rows]),
        (dk_suffix_ref, key_piece[2 * tok_rows : 2 * tok_rows + suffix_len]),
        (dv_suffix_ref, value_piece[2 * tok_rows : 2 * tok_rows + suffix_len]),
    ]

    @pl.when(member == 0)
    def _():
        for ref, piece in pieces:
            ref[...] = piece

    @pl.when(member > 0)
    def _():
        for ref, piece in pieces:
            ref[...] += piece


def attend(queries2d, grads2d, every_kv, bias, kv_heads, group, suffix_len):
    tok_rows = queries2d.shape[0]
    n_keys = every_kv.shape[0]
    scale = HEAD_DIM ** (-0.5)
    kernel = functools.partial(attention_kernel, scale=scale, tok_rows=tok_rows, suffix_len=suffix_len)
    row_spec = pl.BlockSpec((tok_rows, HEAD_DIM), lambda h, g: (0, h * group + g))
    head_spec = pl.BlockSpec((tok_rows, HEAD_DIM), lambda h, g: (0, h))
    suffix_spec = pl.BlockSpec((suffix_len, HEAD_DIM), lambda h, g: (0, h))
    width = kv_heads * HEAD_DIM
    return pl.pallas_call(
        kernel,
        grid=(kv_heads, group),
        in_specs=[
            row_spec,
            row_spec,
            pl.BlockSpec((n_keys, HEAD_DIM), lambda h, g: (0, h)),
            pl.BlockSpec((n_keys, HEAD_DIM), lambda h, g: (0, kv_heads + h)),
            pl.BlockSpec((n_keys, tok_rows), lambda h, g: (0, 0)),
        ],
        out_specs=[row_spec, head_spec, head_spec, head_spec, head_spec, suffix_spec, suffix_spec],
        out_shape=[jax.ShapeDtypeStruct(queries2d.shape, jnp.bfloat16)]
        + [jax.ShapeDtypeStruct((tok_rows, width), jnp.float32)] * 4
        + [jax.ShapeDtypeStruct((suffix_len, width), jnp.float32)] * 2,
        compiler_params=pltpu.CompilerParams(dimension_semantics=("arbitrary", "arbitrary")),
        cost_estimate=pl.CostEstimate(
            flops=12 * tok_rows * n_keys * HEAD_DIM * kv_heads * group,
            transcendentals=tok_rows * n_keys * kv_heads * group,
            bytes_accessed=6 * queries2d.size + 2 * every_kv.size + 4 * bias.size + 16 * tok_rows * width,
        ),
    )(queries2d, grads2d, every_kv, every_kv, bias)


def per_device(
    queries,
    keys,
    values,
    out_grad,
    key_weight,
    value_weight,
    suffix_embed,
    class_ids,
    class_slot,
    pad_offset,
    suffix_pos,
):
    cycle_size = lax.axis_size("ctx")
    cycle_rank = lax.axis_index("ctx")
    owners = lax.axis_size("dp")
    owner_rank = lax.axis_index("dp")
    tok_rows = queries.shape[1]
    kv_width = keys.shape[2]
    kv_heads = kv_width // HEAD_DIM
    group = queries.shape[2] // kv_width
    own_slots = suffix_embed.shape[0]
    suffix_len = suffix_embed.shape[1]
    classes = class_slot.shape[0]
    slot_ids = jnp.arange(classes, dtype=jnp.int32)
    picked = jnp.sum(jnp.where(slot_ids == class_ids[0], class_slot, 0))
    owned_kv = jnp.concatenate(
        [
            jnp.einsum("sld,dk->slk", suffix_embed, key_weight, preferred_element_type=jnp.float32),
            jnp.einsum("sld,dk->slk", suffix_embed, value_weight, preferred_element_type=jnp.float32),
        ],
        axis=2,
    )
    owner = picked // own_slots
    partner = (owner_rank ^ owner) & 1
    source_step = ((owner_rank - (owner ^ partner)) % owners) // 2
    half_kv = paired_gather(owned_kv, "dp")[source_step, partner, picked % own_slots]
    suffix_kv = (half_kv + swapped(half_kv, "ctx")).astype(jnp.bfloat16)
    query_pos = cycle_rank * tok_rows + jnp.arange(tok_rows, dtype=jnp.int32)
    offset = pad_offset[0]
    local_kv = jnp.concatenate([keys[0], values[0]], axis=1)
    prev_kv = passed_along(local_kv, "ctx", 1)
    pad_rows = (-(2 * tok_rows + suffix_len)) % 128
    every_kv = jnp.concatenate(
        [local_kv, prev_kv, suffix_kv, jnp.zeros((pad_rows, 2 * kv_width), jnp.bfloat16)], axis=0
    )
    rows = jnp.arange(tok_rows, dtype=jnp.int32)
    far = jnp.full((pad_rows,), 1 << 30, jnp.int32)
    key_pos = jnp.concatenate(
        [
            cycle_rank * tok_rows + rows,
            ((cycle_rank - 1) % cycle_size) * tok_rows + rows,
            suffix_pos[0],
            far,
        ]
    )
    earlier = key_pos[None, :] <= query_pos[:, None]
    kept = (key_pos[None, :] >= offset) | (key_pos[None, :] == query_pos[:, None])
    bias = jnp.where(earlier & kept, 0.0, masked_fill).astype(jnp.float32).T
    dq, dk_local, dv_local, dk_prev, dv_prev, dk_suffix, dv_suffix = attend(
        queries[0], out_grad[0], every_kv, bias, kv_heads, group, suffix_len
    )
    back_k = passed_along(dk_prev, "ctx", -1)
    back_v = passed_along(dv_prev, "ctx", -1)
    suffix_dkv = jnp.concatenate([dk_suffix, dv_suffix], axis=1)
    summed_dkv = suffix_dkv + swapped(suffix_dkv, "ctx")
    local_ids = jnp.arange(own_slots, dtype=jnp.int32)
    pair_ids = jnp.arange(2, dtype=jnp.int32)
    collected = None
    for step in range(owners // 2):
        target = (owner_rank + 2 * step) % owners
        wanted = picked == ((target ^ pair_ids)[:, None] * own_slots + local_ids[None, :])
        sent = jnp.where(wanted[:, :, None, None], summed_dkv[None, None], 0.0)
        if step:
            sent = shifted(sent, "dp", 2 * step)
        collected = sent if collected is None else collected + sent
    slot_total = collected[0] + swapped(collected[1], "dp")
    key_full = key_weight.astype(jnp.float32)
    value_full = value_weight.astype(jnp.float32)
    suffix_grad = jnp.einsum(
        "slk,dk->sld", slot_total[:, :, :kv_width], key_full, precision=lax.Precision.HIGHEST
    )
    suffix_grad = suffix_grad + jnp.einsum(
        "slk,dk->sld", slot_total[:, :, kv_width:], value_full, precision=lax.Precision.HIGHEST
    )
    key_grad = (dk_local + back_k).astype(jnp.bfloat16)[None]
    value_grad = (dv_local + back_v).astype(jnp.bfloat16)[None]
    return (dq[None], key_grad, value_grad, suffix_grad)


def solution(mesh):
    return jax.shard_map(
        per_device,
        mesh=mesh,
        in_specs=(
            P(("groups", "dp"), "ctx", None),
            P(("groups", "dp"), "ctx", None),
            P(("groups", "dp"), "ctx", None),
            P(("groups", "dp"), "ctx", None),
            P("ctx", None),
            P("ctx", None),
            P(("groups", "dp"), None, "ctx"),
            P(("groups", "dp")),
            P("groups"),
            P(("groups", "dp")),
            P(("groups", "dp"), None),
        ),
        out_specs=(
            P(("groups", "dp"), "ctx", None),
            P(("groups", "dp"), "ctx", None),
            P(("groups", "dp"), "ctx", None),
            P(("groups", "dp"), None, "ctx"),
        ),
        check_vma=False,
    )
```

```python
import functools
import jax
import jax.numpy as jnp
from jax import lax
from jax.experimental import pallas as pl
from jax.experimental.pallas import tpu as pltpu
from jax.sharding import PartitionSpec as P

HEAD_DIM = 128
masked_fill = -1e30


def passed_along(block, axis, distance):
    devices = range(lax.axis_size(axis))
    route = [(i - distance, i) for i in devices if i - distance in devices]
    return lax.ppermute(block, axis, route)


def swapped(block, axis):
    devices = range(lax.axis_size(axis))
    route = [(i, i ^ 1) for i in devices]
    return lax.ppermute(block, axis, route)


def shifted(block, axis, distance):
    devices = range(lax.axis_size(axis))
    route = [(i, (i + distance) % len(devices)) for i in devices]
    return lax.ppermute(block, axis, route)


def paired_gather(block, axis):
    size = lax.axis_size(axis)
    pair = jnp.stack([block, swapped(block, axis)])
    return jnp.stack([pair] + [shifted(pair, axis, 2 * step) for step in range(1, size // 2)])


def attention_kernel(
    q_ref, do_ref, k_ref, v_ref, bias_ref,
    dq_ref, dk_local_ref, dv_local_ref, dk_prev_ref, dv_prev_ref, dk_suffix_ref, dv_suffix_ref,
    *, scale, tok_rows, suffix_len,
):
    member = pl.program_id(1)
    q = q_ref[...]
    grad = do_ref[...]
    k = k_ref[...]
    v = v_ref[...]
    nt = (((1,), (1,)), ((), ()))
    tn = (((0,), (0,)), ((), ()))
    scores = lax.dot_general(k, q, nt, preferred_element_type=jnp.float32) * scale + bias_ref[...]
    row_max = jnp.max(scores, axis=0, keepdims=True)
    expo = jnp.exp(scores - row_max)
    total = jnp.sum(expo, axis=0, keepdims=True)
    inverse = 1.0 / total
    mixed = lax.dot_general(v, expo.astype(jnp.bfloat16), tn, preferred_element_type=jnp.float32)
    attended = (mixed * inverse).astype(jnp.bfloat16)
    grad_t = grad.astype(jnp.float32).T
    delta = jnp.sum(grad_t * attended.astype(jnp.float32), axis=0, keepdims=True)
    probs = expo * inverse
    prob_grad = lax.dot_general(v, grad, nt, preferred_element_type=jnp.float32)
    score_grad = (probs * (prob_grad - delta)).astype(jnp.bfloat16)
    query_piece = lax.dot_general(k, score_grad, tn, preferred_element_type=jnp.float32)
    dq_ref[...] = (query_piece.T * scale).astype(dq_ref.dtype)
    key_piece = jnp.dot(score_grad, q, preferred_element_type=jnp.float32) * scale
    value_piece = jnp.dot(probs.astype(jnp.bfloat16), grad, preferred_element_type=jnp.float32)
    pieces = [
        (dk_local_ref, key_piece[:tok_rows]),
        (dv_local_ref, value_piece[:tok_rows]),
        (dk_prev_ref, key_piece[tok_rows : 2 * tok_rows]),
        (dv_prev_ref, value_piece[tok_rows : 2 * tok_rows]),
        (dk_suffix_ref, key_piece[2 * tok_rows : 2 * tok_rows + suffix_len]),
        (dv_suffix_ref, value_piece[2 * tok_rows : 2 * tok_rows + suffix_len]),
    ]

    @pl.when(member == 0)
    def _():
        for ref, piece in pieces:
            ref[...] = piece

    @pl.when(member > 0)
    def _():
        for ref, piece in pieces:
            ref[...] += piece


def attend(queries2d, grads2d, every_kv, bias, kv_heads, group, suffix_len):
    tok_rows = queries2d.shape[0]
    n_keys = every_kv.shape[0]
    scale = HEAD_DIM ** (-0.5)
    kernel = functools.partial(attention_kernel, scale=scale, tok_rows=tok_rows, suffix_len=suffix_len)
    row_spec = pl.BlockSpec((tok_rows, HEAD_DIM), lambda h, g: (0, h * group + g))
    head_spec = pl.BlockSpec((tok_rows, HEAD_DIM), lambda h, g: (0, h))
    suffix_spec = pl.BlockSpec((suffix_len, HEAD_DIM), lambda h, g: (0, h))
    width = kv_heads * HEAD_DIM
    return pl.pallas_call(
        kernel,
        grid=(kv_heads, group),
        in_specs=[
            row_spec,
            row_spec,
            pl.BlockSpec((n_keys, HEAD_DIM), lambda h, g: (0, h)),
            pl.BlockSpec((n_keys, HEAD_DIM), lambda h, g: (0, kv_heads + h)),
            pl.BlockSpec((n_keys, tok_rows), lambda h, g: (0, 0)),
        ],
        out_specs=[row_spec, head_spec, head_spec, head_spec, head_spec, suffix_spec, suffix_spec],
        out_shape=[jax.ShapeDtypeStruct(queries2d.shape, jnp.bfloat16)]
        + [jax.ShapeDtypeStruct((tok_rows, width), jnp.float32)] * 4
        + [jax.ShapeDtypeStruct((suffix_len, width), jnp.float32)] * 2,
        compiler_params=pltpu.CompilerParams(dimension_semantics=("arbitrary", "arbitrary")),
        cost_estimate=pl.CostEstimate(
            flops=12 * tok_rows * n_keys * HEAD_DIM * kv_heads * group,
            transcendentals=tok_rows * n_keys * kv_heads * group,
            bytes_accessed=6 * queries2d.size + 2 * every_kv.size + 4 * bias.size + 16 * tok_rows * width,
        ),
    )(queries2d, grads2d, every_kv, every_kv, bias)


def per_device(
    queries,
    keys,
    values,
    out_grad,
    key_weight,
    value_weight,
    suffix_embed,
    class_ids,
    class_slot,
    pad_offset,
    suffix_pos,
):
    cycle_size = lax.axis_size("ctx")
    cycle_rank = lax.axis_index("ctx")
    owners = lax.axis_size("dp")
    owner_rank = lax.axis_index("dp")
    tok_rows = queries.shape[1]
    kv_width = keys.shape[2]
    kv_heads = kv_width // HEAD_DIM
    group = queries.shape[2] // kv_width
    own_slots = suffix_embed.shape[0]
    suffix_len = suffix_embed.shape[1]
    classes = class_slot.shape[0]
    slot_ids = jnp.arange(classes, dtype=jnp.int32)
    picked = jnp.sum(jnp.where(slot_ids == class_ids[0], class_slot, 0))
    owned_kv = jnp.concatenate(
        [
            jnp.einsum("sld,dk->slk", suffix_embed, key_weight, preferred_element_type=jnp.float32),
            jnp.einsum("sld,dk->slk", suffix_embed, value_weight, preferred_element_type=jnp.float32),
        ],
        axis=2,
    )
    owner = picked // own_slots
    partner = (owner_rank ^ owner) & 1
    source_step = ((owner_rank - (owner ^ partner)) % owners) // 2
    half_kv = paired_gather(owned_kv, "dp")[source_step, partner, picked % own_slots]
    suffix_kv = (half_kv + swapped(half_kv, "ctx")).astype(jnp.bfloat16)
    query_pos = cycle_rank * tok_rows + jnp.arange(tok_rows, dtype=jnp.int32)
    offset = pad_offset[0]
    local_kv = jnp.concatenate([keys[0], values[0]], axis=1)
    prev_kv = passed_along(local_kv, "ctx", 1)
    pad_rows = (-(2 * tok_rows + suffix_len)) % 128
    every_kv = jnp.concatenate(
        [local_kv, prev_kv, suffix_kv, jnp.zeros((pad_rows, 2 * kv_width), jnp.bfloat16)], axis=0
    )
    rows = jnp.arange(tok_rows, dtype=jnp.int32)
    far = jnp.full((pad_rows,), 1 << 30, jnp.int32)
    key_pos = jnp.concatenate(
        [
            cycle_rank * tok_rows + rows,
            ((cycle_rank - 1) % cycle_size) * tok_rows + rows,
            suffix_pos[0],
            far,
        ]
    )
    earlier = key_pos[None, :] <= query_pos[:, None]
    kept = (key_pos[None, :] >= offset) | (key_pos[None, :] == query_pos[:, None])
    bias = jnp.where(earlier & kept, 0.0, masked_fill).astype(jnp.float32).T
    dq, dk_local, dv_local, dk_prev, dv_prev, dk_suffix, dv_suffix = attend(
        queries[0], out_grad[0], every_kv, bias, kv_heads, group, suffix_len
    )
    back_k = passed_along(dk_prev, "ctx", -1)
    back_v = passed_along(dv_prev, "ctx", -1)
    suffix_dkv = jnp.concatenate([dk_suffix, dv_suffix], axis=1)
    summed_dkv = suffix_dkv + swapped(suffix_dkv, "ctx")
    local_ids = jnp.arange(own_slots, dtype=jnp.int32)
    pair_ids = jnp.arange(2, dtype=jnp.int32)
    collected = None
    for step in range(owners // 2):
        target = (owner_rank + 2 * step) % owners
        wanted = picked == ((target ^ pair_ids)[:, None] * own_slots + local_ids[None, :])
        sent = jnp.where(wanted[:, :, None, None], summed_dkv[None, None], 0.0)
        if step:
            sent = shifted(sent, "dp", 2 * step)
        collected = sent if collected is None else collected + sent
    slot_total = collected[0] + swapped(collected[1], "dp")
    slot_rows = slot_total.reshape(own_slots * suffix_len, 2 * kv_width)
    high = slot_rows.astype(jnp.bfloat16)
    rest = slot_rows - high.astype(jnp.float32)
    middle = rest.astype(jnp.bfloat16)
    low = (rest - middle.astype(jnp.float32)).astype(jnp.bfloat16)
    split = jnp.concatenate([high, middle, low], axis=0)
    both = jnp.dot(split[:, :kv_width], key_weight.T, preferred_element_type=jnp.float32) + jnp.dot(
        split[:, kv_width:], value_weight.T, preferred_element_type=jnp.float32
    )
    rows = own_slots * suffix_len
    suffix_grad = (both[:rows] + both[rows : 2 * rows] + both[2 * rows :]).reshape(
        own_slots, suffix_len, key_weight.shape[0]
    )
    back_k = passed_along(dk_prev, "ctx", -1)
    back_v = passed_along(dv_prev, "ctx", -1)
    suffix_dkv = jnp.concatenate([dk_suffix, dv_suffix], axis=1)
    summed_dkv = suffix_dkv + swapped(suffix_dkv, "ctx")
    local_ids = jnp.arange(own_slots, dtype=jnp.int32)
    pair_ids = jnp.arange(2, dtype=jnp.int32)
    collected = None
    for step in range(owners // 2):
        target = (owner_rank + 2 * step) % owners
        wanted = picked == ((target ^ pair_ids)[:, None] * own_slots + local_ids[None, :])
        sent = jnp.where(wanted[:, :, None, None], summed_dkv[None, None], 0.0)
        if step:
            sent = shifted(sent, "dp", 2 * step)
        collected = sent if collected is None else collected + sent
    slot_total = collected[0] + swapped(collected[1], "dp")
    key_full = key_weight.astype(jnp.float32)
    value_full = value_weight.astype(jnp.float32)
    suffix_grad = jnp.einsum(
        "slk,dk->sld", slot_total[:, :, :kv_width], key_full, precision=lax.Precision.HIGHEST
    )
    suffix_grad = suffix_grad + jnp.einsum(
        "slk,dk->sld", slot_total[:, :, kv_width:], value_full, precision=lax.Precision.HIGHEST
    )
    key_grad = (dk_local + back_k).astype(jnp.bfloat16)[None]
    value_grad = (dv_local + back_v).astype(jnp.bfloat16)[None]
    return (dq[None], key_grad, value_grad, suffix_grad)


def solution(mesh):
    return jax.shard_map(
        per_device,
        mesh=mesh,
        in_specs=(
            P(("groups", "dp"), "ctx", None),
            P(("groups", "dp"), "ctx", None),
            P(("groups", "dp"), "ctx", None),
            P(("groups", "dp"), "ctx", None),
            P("ctx", None),
            P("ctx", None),
            P(("groups", "dp"), None, "ctx"),
            P(("groups", "dp")),
            P("groups"),
            P(("groups", "dp")),
            P(("groups", "dp"), None),
        ),
        out_specs=(
            P(("groups", "dp"), "ctx", None),
            P(("groups", "dp"), "ctx", None),
            P(("groups", "dp"), "ctx", None),
            P(("groups", "dp"), None, "ctx"),
        ),
        check_vma=False,
    )
```

```python
import functools
import jax
import jax.numpy as jnp
from jax import lax
from jax.experimental import pallas as pl
from jax.experimental.pallas import tpu as pltpu
from jax.sharding import PartitionSpec as P

HEAD_DIM = 128
masked_fill = -1e30


def passed_along(block, axis, distance):
    devices = range(lax.axis_size(axis))
    route = [(i - distance, i) for i in devices if i - distance in devices]
    return lax.ppermute(block, axis, route)


def swapped(block, axis):
    devices = range(lax.axis_size(axis))
    route = [(i, i ^ 1) for i in devices]
    return lax.ppermute(block, axis, route)


def shifted(block, axis, distance):
    devices = range(lax.axis_size(axis))
    route = [(i, (i + distance) % len(devices)) for i in devices]
    return lax.ppermute(block, axis, route)


def paired_gather(block, axis):
    size = lax.axis_size(axis)
    pair = jnp.stack([block, swapped(block, axis)])
    return jnp.stack([pair] + [shifted(pair, axis, 2 * step) for step in range(1, size // 2)])


def attention_kernel(
    q_ref, do_ref, k_ref, v_ref, bias_ref,
    dq_ref, local_ref, prev_ref, dk_suffix_ref, dv_suffix_ref,
    *, scale, tok_rows, suffix_len,
):
    member = pl.program_id(1)
    q = q_ref[...]
    grad = do_ref[...]
    k = k_ref[...]
    v = v_ref[...]
    nt = (((1,), (1,)), ((), ()))
    tn = (((0,), (0,)), ((), ()))
    scores = lax.dot_general(k, q, nt, preferred_element_type=jnp.float32) * scale + bias_ref[...]
    row_max = jnp.max(scores, axis=0, keepdims=True)
    expo = jnp.exp(scores - row_max)
    total = jnp.sum(expo, axis=0, keepdims=True)
    inverse = 1.0 / total
    mixed = lax.dot_general(v, expo.astype(jnp.bfloat16), tn, preferred_element_type=jnp.float32)
    attended = (mixed * inverse).astype(jnp.bfloat16)
    grad_t = grad.astype(jnp.float32).T
    delta = jnp.sum(grad_t * attended.astype(jnp.float32), axis=0, keepdims=True)
    probs = expo * inverse
    prob_grad = lax.dot_general(v, grad, nt, preferred_element_type=jnp.float32)
    score_grad = (probs * (prob_grad - delta)).astype(jnp.bfloat16)
    query_piece = lax.dot_general(k, score_grad, tn, preferred_element_type=jnp.float32)
    dq_ref[...] = (query_piece.T * scale).astype(dq_ref.dtype)
    key_piece = jnp.dot(score_grad, q, preferred_element_type=jnp.float32) * scale
    value_piece = jnp.dot(probs.astype(jnp.bfloat16), grad, preferred_element_type=jnp.float32)
    pieces = [
        (local_ref.at[0], key_piece[:tok_rows]),
        (local_ref.at[1], value_piece[:tok_rows]),
        (prev_ref.at[0], key_piece[tok_rows : 2 * tok_rows]),
        (prev_ref.at[1], value_piece[tok_rows : 2 * tok_rows]),
        (dk_suffix_ref, key_piece[2 * tok_rows : 2 * tok_rows + suffix_len]),
        (dv_suffix_ref, value_piece[2 * tok_rows : 2 * tok_rows + suffix_len]),
    ]

    @pl.when(member == 0)
    def _():
        for ref, piece in pieces:
            ref[...] = piece

    @pl.when(member > 0)
    def _():
        for ref, piece in pieces:
            ref[...] += piece


def attend(queries2d, grads2d, every_kv, bias, kv_heads, group, suffix_len):
    tok_rows = queries2d.shape[0]
    n_keys = every_kv.shape[0]
    scale = HEAD_DIM ** (-0.5)
    kernel = functools.partial(attention_kernel, scale=scale, tok_rows=tok_rows, suffix_len=suffix_len)
    row_spec = pl.BlockSpec((tok_rows, HEAD_DIM), lambda h, g: (0, h * group + g))
    head_spec = pl.BlockSpec((2, tok_rows, HEAD_DIM), lambda h, g: (0, 0, h))
    suffix_spec = pl.BlockSpec((suffix_len, HEAD_DIM), lambda h, g: (0, h))
    width = kv_heads * HEAD_DIM
    return pl.pallas_call(
        kernel,
        grid=(kv_heads, group),
        in_specs=[
            row_spec,
            row_spec,
            pl.BlockSpec((n_keys, HEAD_DIM), lambda h, g: (0, h)),
            pl.BlockSpec((n_keys, HEAD_DIM), lambda h, g: (0, kv_heads + h)),
            pl.BlockSpec((n_keys, tok_rows), lambda h, g: (0, 0)),
        ],
        out_specs=[row_spec, head_spec, head_spec, suffix_spec, suffix_spec],
        out_shape=[jax.ShapeDtypeStruct(queries2d.shape, jnp.bfloat16)]
        + [jax.ShapeDtypeStruct((2, tok_rows, width), jnp.float32)] * 2
        + [jax.ShapeDtypeStruct((suffix_len, width), jnp.float32)] * 2,
        compiler_params=pltpu.CompilerParams(dimension_semantics=("arbitrary", "arbitrary")),
        cost_estimate=pl.CostEstimate(
            flops=12 * tok_rows * n_keys * HEAD_DIM * kv_heads * group,
            transcendentals=tok_rows * n_keys * kv_heads * group,
            bytes_accessed=6 * queries2d.size + 2 * every_kv.size + 4 * bias.size + 16 * tok_rows * width,
        ),
    )(queries2d, grads2d, every_kv, every_kv, bias)


def per_device(
    queries,
    keys,
    values,
    out_grad,
    key_weight,
    value_weight,
    suffix_embed,
    class_ids,
    class_slot,
    pad_offset,
    suffix_pos,
):
    cycle_size = lax.axis_size("ctx")
    cycle_rank = lax.axis_index("ctx")
    owners = lax.axis_size("dp")
    owner_rank = lax.axis_index("dp")
    tok_rows = queries.shape[1]
    kv_width = keys.shape[2]
    kv_heads = kv_width // HEAD_DIM
    group = queries.shape[2] // kv_width
    own_slots = suffix_embed.shape[0]
    suffix_len = suffix_embed.shape[1]
    classes = class_slot.shape[0]
    slot_ids = jnp.arange(classes, dtype=jnp.int32)
    picked = jnp.sum(jnp.where(slot_ids == class_ids[0], class_slot, 0))
    owned_kv = jnp.concatenate(
        [
            jnp.einsum("sld,dk->slk", suffix_embed, key_weight, preferred_element_type=jnp.float32),
            jnp.einsum("sld,dk->slk", suffix_embed, value_weight, preferred_element_type=jnp.float32),
        ],
        axis=2,
    )
    owner = picked // own_slots
    partner = (owner_rank ^ owner) & 1
    source_step = ((owner_rank - (owner ^ partner)) % owners) // 2
    half_kv = paired_gather(owned_kv, "dp")[source_step, partner, picked % own_slots]
    suffix_kv = (half_kv + swapped(half_kv, "ctx")).astype(jnp.bfloat16)
    query_pos = cycle_rank * tok_rows + jnp.arange(tok_rows, dtype=jnp.int32)
    offset = pad_offset[0]
    local_kv = jnp.concatenate([keys[0], values[0]], axis=1)
    prev_kv = passed_along(local_kv, "ctx", 1)
    pad_rows = (-(2 * tok_rows + suffix_len)) % 128
    every_kv = jnp.concatenate(
        [local_kv, prev_kv, suffix_kv, jnp.zeros((pad_rows, 2 * kv_width), jnp.bfloat16)], axis=0
    )
    rows = jnp.arange(tok_rows, dtype=jnp.int32)
    far = jnp.full((pad_rows,), 1 << 30, jnp.int32)
    key_pos = jnp.concatenate(
        [
            cycle_rank * tok_rows + rows,
            ((cycle_rank - 1) % cycle_size) * tok_rows + rows,
            suffix_pos[0],
            far,
        ]
    )
    earlier = key_pos[None, :] <= query_pos[:, None]
    kept = (key_pos[None, :] >= offset) | (key_pos[None, :] == query_pos[:, None])
    bias = jnp.where(earlier & kept, 0.0, masked_fill).astype(jnp.float32).T
    dq, local_grad, prev_grad, dk_suffix, dv_suffix = attend(
        queries[0], out_grad[0], every_kv, bias, kv_heads, group, suffix_len
    )
    back = passed_along(prev_grad, "ctx", -1)
    suffix_dkv = jnp.concatenate([dk_suffix, dv_suffix], axis=1)
    summed_dkv = suffix_dkv + swapped(suffix_dkv, "ctx")
    local_ids = jnp.arange(own_slots, dtype=jnp.int32)
    pair_ids = jnp.arange(2, dtype=jnp.int32)
    collected = None
    for step in range(owners // 2):
        target = (owner_rank + 2 * step) % owners
        wanted = picked == ((target ^ pair_ids)[:, None] * own_slots + local_ids[None, :])
        sent = jnp.where(wanted[:, :, None, None], summed_dkv[None, None], 0.0)
        if step:
            sent = shifted(sent, "dp", 2 * step)
        collected = sent if collected is None else collected + sent
    slot_total = collected[0] + swapped(collected[1], "dp")
    slot_rows = slot_total.reshape(own_slots * suffix_len, 2 * kv_width)
    high = slot_rows.astype(jnp.bfloat16)
    rest = slot_rows - high.astype(jnp.float32)
    middle = rest.astype(jnp.bfloat16)
    low = (rest - middle.astype(jnp.float32)).astype(jnp.bfloat16)
    split = jnp.concatenate([high, middle, low], axis=0)
    both = jnp.dot(split[:, :kv_width], key_weight.T, preferred_element_type=jnp.float32) + jnp.dot(
        split[:, kv_width:], value_weight.T, preferred_element_type=jnp.float32
    )
    rows = own_slots * suffix_len
    suffix_grad = (both[:rows] + both[rows : 2 * rows] + both[2 * rows :]).reshape(
        own_slots, suffix_len, key_weight.shape[0]
    )
    back = passed_along(prev_grad, "ctx", -1)
    suffix_dkv = jnp.concatenate([dk_suffix, dv_suffix], axis=1)
    summed_dkv = suffix_dkv + swapped(suffix_dkv, "ctx")
    local_ids = jnp.arange(own_slots, dtype=jnp.int32)
    pair_ids = jnp.arange(2, dtype=jnp.int32)
    collected = None
    for step in range(owners // 2):
        target = (owner_rank + 2 * step) % owners
        wanted = picked == ((target ^ pair_ids)[:, None] * own_slots + local_ids[None, :])
        sent = jnp.where(wanted[:, :, None, None], summed_dkv[None, None], 0.0)
        if step:
            sent = shifted(sent, "dp", 2 * step)
        collected = sent if collected is None else collected + sent
    slot_total = collected[0] + swapped(collected[1], "dp")
    key_full = key_weight.astype(jnp.float32)
    value_full = value_weight.astype(jnp.float32)
    suffix_grad = jnp.einsum(
        "slk,dk->sld", slot_total[:, :, :kv_width], key_full, precision=lax.Precision.HIGHEST
    )
    suffix_grad = suffix_grad + jnp.einsum(
        "slk,dk->sld", slot_total[:, :, kv_width:], value_full, precision=lax.Precision.HIGHEST
    )
    key_grad = (local_grad[0] + back[0]).astype(jnp.bfloat16)[None]
    value_grad = (local_grad[1] + back[1]).astype(jnp.bfloat16)[None]
    return (dq[None], key_grad, value_grad, suffix_grad)


def solution(mesh):
    return jax.shard_map(
        per_device,
        mesh=mesh,
        in_specs=(
            P(("groups", "dp"), "ctx", None),
            P(("groups", "dp"), "ctx", None),
            P(("groups", "dp"), "ctx", None),
            P(("groups", "dp"), "ctx", None),
            P("ctx", None),
            P("ctx", None),
            P(("groups", "dp"), None, "ctx"),
            P(("groups", "dp")),
            P("groups"),
            P(("groups", "dp")),
            P(("groups", "dp"), None),
        ),
        out_specs=(
            P(("groups", "dp"), "ctx", None),
            P(("groups", "dp"), "ctx", None),
            P(("groups", "dp"), "ctx", None),
            P(("groups", "dp"), None, "ctx"),
        ),
        check_vma=False,
    )
```

```python
import functools
import jax
import jax.numpy as jnp
from jax import lax
from jax.experimental import pallas as pl
from jax.experimental.pallas import tpu as pltpu
from jax.sharding import PartitionSpec as P

HEAD_DIM = 128
masked_fill = -1e30


def passed_along(block, axis, distance):
    devices = range(lax.axis_size(axis))
    route = [(i - distance, i) for i in devices if i - distance in devices]
    return lax.ppermute(block, axis, route)


def swapped(block, axis):
    devices = range(lax.axis_size(axis))
    route = [(i, i ^ 1) for i in devices]
    return lax.ppermute(block, axis, route)


def shifted(block, axis, distance):
    devices = range(lax.axis_size(axis))
    route = [(i, (i + distance) % len(devices)) for i in devices]
    return lax.ppermute(block, axis, route)


def paired_gather(block, axis):
    size = lax.axis_size(axis)
    pair = jnp.stack([block, swapped(block, axis)])
    return jnp.stack([pair] + [shifted(pair, axis, 2 * step) for step in range(1, size // 2)])


def attention_kernel(
    q_ref, do_ref, k_ref, v_ref, bias_ref,
    dq_ref, dk_suffix_ref, dv_suffix_ref, dk_prev_ref, dv_prev_ref, dk_local_ref, dv_local_ref,
    dk_acc, dv_acc,
    *, scale, tok_rows, suffix_rows, suffix_len, tile,
):
    member = pl.program_id(1)
    nt = (((1,), (1,)), ((), ()))
    tn = (((0,), (0,)), ((), ()))

    @pl.when(member == 0)
    def _():
        dk_acc[...] = jnp.zeros_like(dk_acc)
        dv_acc[...] = jnp.zeros_like(dv_acc)

    for start in range(0, tok_rows, tile):
        seen = suffix_rows + tok_rows + start + tile
        q = q_ref[start : start + tile, :]
        grad = do_ref[start : start + tile, :]
        k = k_ref[:seen, :]
        v = v_ref[:seen, :]
        scores = lax.dot_general(k, q, nt, preferred_element_type=jnp.float32) * scale
        scores = scores + bias_ref[:seen, start : start + tile]
        row_max = jnp.max(scores, axis=0, keepdims=True)
        expo = jnp.exp(scores - row_max)
        total = jnp.sum(expo, axis=0, keepdims=True)
        inverse = 1.0 / total
        mixed = lax.dot_general(v, expo.astype(jnp.bfloat16), tn, preferred_element_type=jnp.float32)
        attended = (mixed * inverse).astype(jnp.bfloat16)
        grad_t = grad.astype(jnp.float32).T
        delta = jnp.sum(grad_t * attended.astype(jnp.float32), axis=0, keepdims=True)
        probs = expo * inverse
        prob_grad = lax.dot_general(v, grad, nt, preferred_element_type=jnp.float32)
        score_grad = (probs * (prob_grad - delta)).astype(jnp.bfloat16)
        query_piece = lax.dot_general(k, score_grad, tn, preferred_element_type=jnp.float32)
        dq_ref[start : start + tile, :] = (query_piece.T * scale).astype(dq_ref.dtype)
        dk_acc[:seen, :] += jnp.dot(score_grad, q, preferred_element_type=jnp.float32) * scale
        dv_acc[:seen, :] += jnp.dot(probs.astype(jnp.bfloat16), grad, preferred_element_type=jnp.float32)

    @pl.when(member == pl.num_programs(1) - 1)
    def _():
        dk_suffix_ref[...] = dk_acc[:suffix_len, :]
        dv_suffix_ref[...] = dv_acc[:suffix_len, :]
        dk_prev_ref[...] = dk_acc[suffix_rows : suffix_rows + tok_rows, :]
        dv_prev_ref[...] = dv_acc[suffix_rows : suffix_rows + tok_rows, :]
        dk_local_ref[...] = dk_acc[suffix_rows + tok_rows :, :]
        dv_local_ref[...] = dv_acc[suffix_rows + tok_rows :, :]


def attend(queries2d, grads2d, every_kv, bias, kv_heads, group, suffix_rows, suffix_len):
    tok_rows = queries2d.shape[0]
    n_keys = every_kv.shape[0]
    scale = HEAD_DIM ** (-0.5)
    tile = 128 if tok_rows % 128 == 0 else tok_rows
    kernel = functools.partial(
        attention_kernel, scale=scale, tok_rows=tok_rows, suffix_rows=suffix_rows,
        suffix_len=suffix_len, tile=tile,
    )
    row_spec = pl.BlockSpec((tok_rows, HEAD_DIM), lambda h, g: (0, h * group + g))
    head_spec = pl.BlockSpec((tok_rows, HEAD_DIM), lambda h, g: (0, h))
    suffix_spec = pl.BlockSpec((suffix_len, HEAD_DIM), lambda h, g: (0, h))
    width = kv_heads * HEAD_DIM
    return pl.pallas_call(
        kernel,
        grid=(kv_heads, group),
        in_specs=[
            row_spec,
            row_spec,
            pl.BlockSpec((n_keys, HEAD_DIM), lambda h, g: (0, h)),
            pl.BlockSpec((n_keys, HEAD_DIM), lambda h, g: (0, kv_heads + h)),
            pl.BlockSpec((n_keys, tok_rows), lambda h, g: (0, 0)),
        ],
        out_specs=[row_spec, suffix_spec, suffix_spec, head_spec, head_spec, head_spec, head_spec],
        out_shape=[jax.ShapeDtypeStruct(queries2d.shape, jnp.bfloat16)]
        + [jax.ShapeDtypeStruct((suffix_len, width), jnp.float32)] * 2
        + [jax.ShapeDtypeStruct((tok_rows, width), jnp.float32)] * 4,
        scratch_shapes=[pltpu.VMEM((n_keys, HEAD_DIM), jnp.float32)] * 2,
        compiler_params=pltpu.CompilerParams(dimension_semantics=("arbitrary", "arbitrary")),
        cost_estimate=pl.CostEstimate(
            flops=12 * tok_rows * n_keys * HEAD_DIM * kv_heads * group,
            transcendentals=tok_rows * n_keys * kv_heads * group,
            bytes_accessed=6 * queries2d.size + 2 * every_kv.size + 4 * bias.size + 16 * tok_rows * width,
        ),
    )(queries2d, grads2d, every_kv, every_kv, bias)


def per_device(
    queries,
    keys,
    values,
    out_grad,
    key_weight,
    value_weight,
    suffix_embed,
    class_ids,
    class_slot,
    pad_offset,
    suffix_pos,
):
    cycle_size = lax.axis_size("ctx")
    cycle_rank = lax.axis_index("ctx")
    owners = lax.axis_size("dp")
    owner_rank = lax.axis_index("dp")
    tok_rows = queries.shape[1]
    kv_width = keys.shape[2]
    kv_heads = kv_width // HEAD_DIM
    group = queries.shape[2] // kv_width
    own_slots = suffix_embed.shape[0]
    suffix_len = suffix_embed.shape[1]
    classes = class_slot.shape[0]
    slot_ids = jnp.arange(classes, dtype=jnp.int32)
    picked = jnp.sum(jnp.where(slot_ids == class_ids[0], class_slot, 0))
    owned_kv = jnp.concatenate(
        [
            jnp.einsum("sld,dk->slk", suffix_embed, key_weight, preferred_element_type=jnp.float32),
            jnp.einsum("sld,dk->slk", suffix_embed, value_weight, preferred_element_type=jnp.float32),
        ],
        axis=2,
    )
    owner = picked // own_slots
    partner = (owner_rank ^ owner) & 1
    source_step = ((owner_rank - (owner ^ partner)) % owners) // 2
    half_kv = paired_gather(owned_kv, "dp")[source_step, partner, picked % own_slots]
    suffix_kv = (half_kv + swapped(half_kv, "ctx")).astype(jnp.bfloat16)
    query_pos = cycle_rank * tok_rows + jnp.arange(tok_rows, dtype=jnp.int32)
    offset = pad_offset[0]
    local_kv = jnp.concatenate([keys[0], values[0]], axis=1)
    prev_kv = passed_along(local_kv, "ctx", 1)
    pad_rows = (-suffix_len) % 128
    suffix_rows = suffix_len + pad_rows
    every_kv = jnp.concatenate(
        [suffix_kv, jnp.zeros((pad_rows, 2 * kv_width), jnp.bfloat16), prev_kv, local_kv], axis=0
    )
    rows = jnp.arange(tok_rows, dtype=jnp.int32)
    far = jnp.full((pad_rows,), 1 << 30, jnp.int32)
    key_pos = jnp.concatenate(
        [
            suffix_pos[0],
            far,
            ((cycle_rank - 1) % cycle_size) * tok_rows + rows,
            cycle_rank * tok_rows + rows,
        ]
    )
    earlier = key_pos[None, :] <= query_pos[:, None]
    kept = (key_pos[None, :] >= offset) | (key_pos[None, :] == query_pos[:, None])
    bias = jnp.where(earlier & kept, 0.0, masked_fill).astype(jnp.float32).T
    dq, dk_suffix, dv_suffix, dk_prev, dv_prev, dk_local, dv_local = attend(
        queries[0], out_grad[0], every_kv, bias, kv_heads, group, suffix_rows, suffix_len
    )
    back_k = passed_along(dk_prev, "ctx", -1)
    back_v = passed_along(dv_prev, "ctx", -1)
    suffix_dkv = jnp.concatenate([dk_suffix, dv_suffix], axis=1)
    summed_dkv = suffix_dkv + swapped(suffix_dkv, "ctx")
    local_ids = jnp.arange(own_slots, dtype=jnp.int32)
    pair_ids = jnp.arange(2, dtype=jnp.int32)
    collected = None
    for step in range(owners // 2):
        target = (owner_rank + 2 * step) % owners
        wanted = picked == ((target ^ pair_ids)[:, None] * own_slots + local_ids[None, :])
        sent = jnp.where(wanted[:, :, None, None], summed_dkv[None, None], 0.0)
        if step:
            sent = shifted(sent, "dp", 2 * step)
        collected = sent if collected is None else collected + sent
    slot_total = collected[0] + swapped(collected[1], "dp")
    key_full = key_weight.astype(jnp.float32)
    value_full = value_weight.astype(jnp.float32)
    suffix_grad = jnp.einsum(
        "slk,dk->sld", slot_total[:, :, :kv_width], key_full, precision=lax.Precision.HIGHEST
    )
    suffix_grad = suffix_grad + jnp.einsum(
        "slk,dk->sld", slot_total[:, :, kv_width:], value_full, precision=lax.Precision.HIGHEST
    )
    key_grad = (dk_local + back_k).astype(jnp.bfloat16)[None]
    value_grad = (dv_local + back_v).astype(jnp.bfloat16)[None]
    return (dq[None], key_grad, value_grad, suffix_grad)


def solution(mesh):
    return jax.shard_map(
        per_device,
        mesh=mesh,
        in_specs=(
            P(("groups", "dp"), "ctx", None),
            P(("groups", "dp"), "ctx", None),
            P(("groups", "dp"), "ctx", None),
            P(("groups", "dp"), "ctx", None),
            P("ctx", None),
            P("ctx", None),
            P(("groups", "dp"), None, "ctx"),
            P(("groups", "dp")),
            P("groups"),
            P(("groups", "dp")),
            P(("groups", "dp"), None),
        ),
        out_specs=(
            P(("groups", "dp"), "ctx", None),
            P(("groups", "dp"), "ctx", None),
            P(("groups", "dp"), "ctx", None),
            P(("groups", "dp"), None, "ctx"),
        ),
        check_vma=False,
    )
```

```python
import functools
import jax
import jax.numpy as jnp
from jax import lax
from jax.experimental import pallas as pl
from jax.experimental.pallas import tpu as pltpu
from jax.sharding import PartitionSpec as P

HEAD_DIM = 128
masked_fill = -1e30


def passed_along(block, axis, distance):
    devices = range(lax.axis_size(axis))
    route = [(i - distance, i) for i in devices if i - distance in devices]
    return lax.ppermute(block, axis, route)


def swapped(block, axis):
    devices = range(lax.axis_size(axis))
    route = [(i, i ^ 1) for i in devices]
    return lax.ppermute(block, axis, route)


def shifted(block, axis, distance):
    devices = range(lax.axis_size(axis))
    route = [(i, (i + distance) % len(devices)) for i in devices]
    return lax.ppermute(block, axis, route)


def paired_gather(block, axis):
    size = lax.axis_size(axis)
    pair = jnp.stack([block, swapped(block, axis)])
    return jnp.stack([pair] + [shifted(pair, axis, 2 * step) for step in range(1, size // 2)])


def attention_kernel(
    q_ref, do_ref, k_ref, v_ref, bias_ref,
    dq_ref, dk_local_ref, dv_local_ref, dk_prev_ref, dv_prev_ref, dk_suffix_ref, dv_suffix_ref,
    *, scale, tok_rows, suffix_len, group,
):
    k = k_ref[...]
    v = v_ref[...]
    bias = bias_ref[...]
    nt = (((1,), (1,)), ((), ()))
    tn = (((0,), (0,)), ((), ()))
    key_total = None
    value_total = None
    for member in range(group):
        cols = slice(member * HEAD_DIM, (member + 1) * HEAD_DIM)
        q = q_ref[:, cols]
        grad = do_ref[:, cols]
        scores = lax.dot_general(k, q, nt, preferred_element_type=jnp.float32) * scale + bias
        row_max = jnp.max(scores, axis=0, keepdims=True)
        expo = jnp.exp(scores - row_max)
        total = jnp.sum(expo, axis=0, keepdims=True)
        inverse = 1.0 / total
        mixed = lax.dot_general(v, expo.astype(jnp.bfloat16), tn, preferred_element_type=jnp.float32)
        attended = (mixed * inverse).astype(jnp.bfloat16)
        grad_t = grad.astype(jnp.float32).T
        delta = jnp.sum(grad_t * attended.astype(jnp.float32), axis=0, keepdims=True)
        probs = expo * inverse
        prob_grad = lax.dot_general(v, grad, nt, preferred_element_type=jnp.float32)
        score_grad = (probs * (prob_grad - delta)).astype(jnp.bfloat16)
        query_piece = lax.dot_general(k, score_grad, tn, preferred_element_type=jnp.float32)
        dq_ref[:, cols] = (query_piece.T * scale).astype(dq_ref.dtype)
        key_piece = jnp.dot(score_grad, q, preferred_element_type=jnp.float32) * scale
        value_piece = jnp.dot(probs.astype(jnp.bfloat16), grad, preferred_element_type=jnp.float32)
        key_total = key_piece if key_total is None else key_total + key_piece
        value_total = value_piece if value_total is None else value_total + value_piece
    dk_local_ref[...] = key_total[:tok_rows]
    dv_local_ref[...] = value_total[:tok_rows]
    dk_prev_ref[...] = key_total[tok_rows : 2 * tok_rows]
    dv_prev_ref[...] = value_total[tok_rows : 2 * tok_rows]
    dk_suffix_ref[...] = key_total[2 * tok_rows : 2 * tok_rows + suffix_len]
    dv_suffix_ref[...] = value_total[2 * tok_rows : 2 * tok_rows + suffix_len]


def attend(queries2d, grads2d, every_kv, bias, kv_heads, group, suffix_len):
    tok_rows = queries2d.shape[0]
    n_keys = every_kv.shape[0]
    scale = HEAD_DIM ** (-0.5)
    kernel = functools.partial(
        attention_kernel, scale=scale, tok_rows=tok_rows, suffix_len=suffix_len, group=group
    )
    row_spec = pl.BlockSpec((tok_rows, group * HEAD_DIM), lambda h: (0, h))
    head_spec = pl.BlockSpec((tok_rows, HEAD_DIM), lambda h: (0, h))
    suffix_spec = pl.BlockSpec((suffix_len, HEAD_DIM), lambda h: (0, h))
    width = kv_heads * HEAD_DIM
    return pl.pallas_call(
        kernel,
        grid=(kv_heads,),
        in_specs=[
            row_spec,
            row_spec,
            pl.BlockSpec((n_keys, HEAD_DIM), lambda h: (0, h)),
            pl.BlockSpec((n_keys, HEAD_DIM), lambda h: (0, kv_heads + h)),
            pl.BlockSpec((n_keys, tok_rows), lambda h: (0, 0)),
        ],
        out_specs=[row_spec, head_spec, head_spec, head_spec, head_spec, suffix_spec, suffix_spec],
        out_shape=[jax.ShapeDtypeStruct(queries2d.shape, jnp.bfloat16)]
        + [jax.ShapeDtypeStruct((tok_rows, width), jnp.float32)] * 4
        + [jax.ShapeDtypeStruct((suffix_len, width), jnp.float32)] * 2,
        compiler_params=pltpu.CompilerParams(dimension_semantics=("arbitrary",)),
        cost_estimate=pl.CostEstimate(
            flops=12 * tok_rows * n_keys * HEAD_DIM * kv_heads * group,
            transcendentals=tok_rows * n_keys * kv_heads * group,
            bytes_accessed=6 * queries2d.size + 2 * every_kv.size + 4 * bias.size + 16 * tok_rows * width,
        ),
    )(queries2d, grads2d, every_kv, every_kv, bias)


def per_device(
    queries,
    keys,
    values,
    out_grad,
    key_weight,
    value_weight,
    suffix_embed,
    class_ids,
    class_slot,
    pad_offset,
    suffix_pos,
):
    cycle_size = lax.axis_size("ctx")
    cycle_rank = lax.axis_index("ctx")
    owners = lax.axis_size("dp")
    owner_rank = lax.axis_index("dp")
    tok_rows = queries.shape[1]
    kv_width = keys.shape[2]
    kv_heads = kv_width // HEAD_DIM
    group = queries.shape[2] // kv_width
    own_slots = suffix_embed.shape[0]
    suffix_len = suffix_embed.shape[1]
    classes = class_slot.shape[0]
    slot_ids = jnp.arange(classes, dtype=jnp.int32)
    picked = jnp.sum(jnp.where(slot_ids == class_ids[0], class_slot, 0))
    owned_kv = jnp.concatenate(
        [
            jnp.einsum("sld,dk->slk", suffix_embed, key_weight, preferred_element_type=jnp.float32),
            jnp.einsum("sld,dk->slk", suffix_embed, value_weight, preferred_element_type=jnp.float32),
        ],
        axis=2,
    )
    owner = picked // own_slots
    partner = (owner_rank ^ owner) & 1
    source_step = ((owner_rank - (owner ^ partner)) % owners) // 2
    half_kv = paired_gather(owned_kv, "dp")[source_step, partner, picked % own_slots]
    suffix_kv = (half_kv + swapped(half_kv, "ctx")).astype(jnp.bfloat16)
    query_pos = cycle_rank * tok_rows + jnp.arange(tok_rows, dtype=jnp.int32)
    offset = pad_offset[0]
    local_kv = jnp.concatenate([keys[0], values[0]], axis=1)
    prev_kv = passed_along(local_kv, "ctx", 1)
    pad_rows = (-(2 * tok_rows + suffix_len)) % 128
    every_kv = jnp.concatenate(
        [local_kv, prev_kv, suffix_kv, jnp.zeros((pad_rows, 2 * kv_width), jnp.bfloat16)], axis=0
    )
    rows = jnp.arange(tok_rows, dtype=jnp.int32)
    far = jnp.full((pad_rows,), 1 << 30, jnp.int32)
    key_pos = jnp.concatenate(
        [
            cycle_rank * tok_rows + rows,
            ((cycle_rank - 1) % cycle_size) * tok_rows + rows,
            suffix_pos[0],
            far,
        ]
    )
    earlier = key_pos[None, :] <= query_pos[:, None]
    kept = (key_pos[None, :] >= offset) | (key_pos[None, :] == query_pos[:, None])
    bias = jnp.where(earlier & kept, 0.0, masked_fill).astype(jnp.float32).T
    dq, dk_local, dv_local, dk_prev, dv_prev, dk_suffix, dv_suffix = attend(
        queries[0], out_grad[0], every_kv, bias, kv_heads, group, suffix_len
    )
    back_k = passed_along(dk_prev, "ctx", -1)
    back_v = passed_along(dv_prev, "ctx", -1)
    suffix_dkv = jnp.concatenate([dk_suffix, dv_suffix], axis=1)
    summed_dkv = suffix_dkv + swapped(suffix_dkv, "ctx")
    local_ids = jnp.arange(own_slots, dtype=jnp.int32)
    pair_ids = jnp.arange(2, dtype=jnp.int32)
    collected = None
    for step in range(owners // 2):
        target = (owner_rank + 2 * step) % owners
        wanted = picked == ((target ^ pair_ids)[:, None] * own_slots + local_ids[None, :])
        sent = jnp.where(wanted[:, :, None, None], summed_dkv[None, None], 0.0)
        if step:
            sent = shifted(sent, "dp", 2 * step)
        collected = sent if collected is None else collected + sent
    slot_total = collected[0] + swapped(collected[1], "dp")
    key_full = key_weight.astype(jnp.float32)
    value_full = value_weight.astype(jnp.float32)
    suffix_grad = jnp.einsum(
        "slk,dk->sld", slot_total[:, :, :kv_width], key_full, precision=lax.Precision.HIGHEST
    )
    suffix_grad = suffix_grad + jnp.einsum(
        "slk,dk->sld", slot_total[:, :, kv_width:], value_full, precision=lax.Precision.HIGHEST
    )
    key_grad = (dk_local + back_k).astype(jnp.bfloat16)[None]
    value_grad = (dv_local + back_v).astype(jnp.bfloat16)[None]
    return (dq[None], key_grad, value_grad, suffix_grad)


def solution(mesh):
    return jax.shard_map(
        per_device,
        mesh=mesh,
        in_specs=(
            P(("groups", "dp"), "ctx", None),
            P(("groups", "dp"), "ctx", None),
            P(("groups", "dp"), "ctx", None),
            P(("groups", "dp"), "ctx", None),
            P("ctx", None),
            P("ctx", None),
            P(("groups", "dp"), None, "ctx"),
            P(("groups", "dp")),
            P("groups"),
            P(("groups", "dp")),
            P(("groups", "dp"), None),
        ),
        out_specs=(
            P(("groups", "dp"), "ctx", None),
            P(("groups", "dp"), "ctx", None),
            P(("groups", "dp"), "ctx", None),
            P(("groups", "dp"), None, "ctx"),
        ),
        check_vma=False,
    )
```

```python
import functools
import jax
import jax.numpy as jnp
from jax import lax
from jax.experimental import pallas as pl
from jax.experimental.pallas import tpu as pltpu
from jax.sharding import PartitionSpec as P

HEAD_DIM = 128
masked_fill = -1e30


def passed_along(block, axis, distance):
    devices = range(lax.axis_size(axis))
    route = [(i - distance, i) for i in devices if i - distance in devices]
    return lax.ppermute(block, axis, route)


def swapped(block, axis):
    devices = range(lax.axis_size(axis))
    route = [(i, i ^ 1) for i in devices]
    return lax.ppermute(block, axis, route)


def shifted(block, axis, distance):
    devices = range(lax.axis_size(axis))
    route = [(i, (i + distance) % len(devices)) for i in devices]
    return lax.ppermute(block, axis, route)


def paired_gather(block, axis):
    size = lax.axis_size(axis)
    pair = jnp.stack([block, swapped(block, axis)])
    return jnp.stack([pair] + [shifted(pair, axis, 2 * step) for step in range(1, size // 2)])


def attention_kernel(
    q_ref, do_ref, k_ref, v_ref, bias_ref,
    dq_ref, dk_local_ref, dv_local_ref, dk_prev_ref, dv_prev_ref, dk_suffix_ref, dv_suffix_ref,
    *, scale, tok_rows, suffix_len, group,
):
    k = k_ref[...]
    v = v_ref[...]
    k_t = k.astype(jnp.float32).T.astype(jnp.bfloat16)
    v_t = v.astype(jnp.float32).T.astype(jnp.bfloat16)
    bias = bias_ref[...]
    nt = (((1,), (1,)), ((), ()))
    key_total = None
    value_total = None
    for member in range(group):
        cols = slice(member * HEAD_DIM, (member + 1) * HEAD_DIM)
        q = q_ref[:, cols]
        grad = do_ref[:, cols]
        scores = lax.dot_general(k, q, nt, preferred_element_type=jnp.float32) * scale + bias
        row_max = jnp.max(scores, axis=0, keepdims=True)
        expo = jnp.exp(scores - row_max)
        total = jnp.sum(expo, axis=0, keepdims=True)
        inverse = 1.0 / total
        mixed = jnp.dot(v_t, expo.astype(jnp.bfloat16), preferred_element_type=jnp.float32)
        attended = (mixed * inverse).astype(jnp.bfloat16)
        grad_t = grad.astype(jnp.float32).T
        delta = jnp.sum(grad_t * attended.astype(jnp.float32), axis=0, keepdims=True)
        probs = expo * inverse
        prob_grad = lax.dot_general(v, grad, nt, preferred_element_type=jnp.float32)
        score_grad = (probs * (prob_grad - delta)).astype(jnp.bfloat16)
        query_piece = jnp.dot(k_t, score_grad, preferred_element_type=jnp.float32)
        dq_ref[:, cols] = (query_piece.T * scale).astype(dq_ref.dtype)
        key_piece = jnp.dot(score_grad, q, preferred_element_type=jnp.float32) * scale
        value_piece = jnp.dot(probs.astype(jnp.bfloat16), grad, preferred_element_type=jnp.float32)
        key_total = key_piece if key_total is None else key_total + key_piece
        value_total = value_piece if value_total is None else value_total + value_piece
    dk_local_ref[...] = key_total[:tok_rows]
    dv_local_ref[...] = value_total[:tok_rows]
    dk_prev_ref[...] = key_total[tok_rows : 2 * tok_rows]
    dv_prev_ref[...] = value_total[tok_rows : 2 * tok_rows]
    dk_suffix_ref[...] = key_total[2 * tok_rows : 2 * tok_rows + suffix_len]
    dv_suffix_ref[...] = value_total[2 * tok_rows : 2 * tok_rows + suffix_len]


def attend(queries2d, grads2d, every_kv, bias, kv_heads, group, suffix_len):
    tok_rows = queries2d.shape[0]
    n_keys = every_kv.shape[0]
    scale = HEAD_DIM ** (-0.5)
    kernel = functools.partial(
        attention_kernel, scale=scale, tok_rows=tok_rows, suffix_len=suffix_len, group=group
    )
    row_spec = pl.BlockSpec((tok_rows, group * HEAD_DIM), lambda h: (0, h))
    head_spec = pl.BlockSpec((tok_rows, HEAD_DIM), lambda h: (0, h))
    suffix_spec = pl.BlockSpec((suffix_len, HEAD_DIM), lambda h: (0, h))
    width = kv_heads * HEAD_DIM
    return pl.pallas_call(
        kernel,
        grid=(kv_heads,),
        in_specs=[
            row_spec,
            row_spec,
            pl.BlockSpec((n_keys, HEAD_DIM), lambda h: (0, h)),
            pl.BlockSpec((n_keys, HEAD_DIM), lambda h: (0, kv_heads + h)),
            pl.BlockSpec((n_keys, tok_rows), lambda h: (0, 0)),
        ],
        out_specs=[row_spec, head_spec, head_spec, head_spec, head_spec, suffix_spec, suffix_spec],
        out_shape=[jax.ShapeDtypeStruct(queries2d.shape, jnp.bfloat16)]
        + [jax.ShapeDtypeStruct((tok_rows, width), jnp.float32)] * 4
        + [jax.ShapeDtypeStruct((suffix_len, width), jnp.float32)] * 2,
        compiler_params=pltpu.CompilerParams(dimension_semantics=("arbitrary",)),
        cost_estimate=pl.CostEstimate(
            flops=12 * tok_rows * n_keys * HEAD_DIM * kv_heads * group,
            transcendentals=tok_rows * n_keys * kv_heads * group,
            bytes_accessed=6 * queries2d.size + 2 * every_kv.size + 4 * bias.size + 16 * tok_rows * width,
        ),
    )(queries2d, grads2d, every_kv, every_kv, bias)


def per_device(
    queries,
    keys,
    values,
    out_grad,
    key_weight,
    value_weight,
    suffix_embed,
    class_ids,
    class_slot,
    pad_offset,
    suffix_pos,
):
    cycle_size = lax.axis_size("ctx")
    cycle_rank = lax.axis_index("ctx")
    owners = lax.axis_size("dp")
    owner_rank = lax.axis_index("dp")
    tok_rows = queries.shape[1]
    kv_width = keys.shape[2]
    kv_heads = kv_width // HEAD_DIM
    group = queries.shape[2] // kv_width
    own_slots = suffix_embed.shape[0]
    suffix_len = suffix_embed.shape[1]
    classes = class_slot.shape[0]
    slot_ids = jnp.arange(classes, dtype=jnp.int32)
    picked = jnp.sum(jnp.where(slot_ids == class_ids[0], class_slot, 0))
    owned_kv = jnp.concatenate(
        [
            jnp.einsum("sld,dk->slk", suffix_embed, key_weight, preferred_element_type=jnp.float32),
            jnp.einsum("sld,dk->slk", suffix_embed, value_weight, preferred_element_type=jnp.float32),
        ],
        axis=2,
    )
    owner = picked // own_slots
    partner = (owner_rank ^ owner) & 1
    source_step = ((owner_rank - (owner ^ partner)) % owners) // 2
    half_kv = paired_gather(owned_kv, "dp")[source_step, partner, picked % own_slots]
    suffix_kv = (half_kv + swapped(half_kv, "ctx")).astype(jnp.bfloat16)
    query_pos = cycle_rank * tok_rows + jnp.arange(tok_rows, dtype=jnp.int32)
    offset = pad_offset[0]
    local_kv = jnp.concatenate([keys[0], values[0]], axis=1)
    prev_kv = passed_along(local_kv, "ctx", 1)
    pad_rows = (-(2 * tok_rows + suffix_len)) % 128
    every_kv = jnp.concatenate(
        [local_kv, prev_kv, suffix_kv, jnp.zeros((pad_rows, 2 * kv_width), jnp.bfloat16)], axis=0
    )
    rows = jnp.arange(tok_rows, dtype=jnp.int32)
    far = jnp.full((pad_rows,), 1 << 30, jnp.int32)
    key_pos = jnp.concatenate(
        [
            cycle_rank * tok_rows + rows,
            ((cycle_rank - 1) % cycle_size) * tok_rows + rows,
            suffix_pos[0],
            far,
        ]
    )
    earlier = key_pos[None, :] <= query_pos[:, None]
    kept = (key_pos[None, :] >= offset) | (key_pos[None, :] == query_pos[:, None])
    bias = jnp.where(earlier & kept, 0.0, masked_fill).astype(jnp.float32).T
    dq, dk_local, dv_local, dk_prev, dv_prev, dk_suffix, dv_suffix = attend(
        queries[0], out_grad[0], every_kv, bias, kv_heads, group, suffix_len
    )
    back_k = passed_along(dk_prev, "ctx", -1)
    back_v = passed_along(dv_prev, "ctx", -1)
    suffix_dkv = jnp.concatenate([dk_suffix, dv_suffix], axis=1)
    summed_dkv = suffix_dkv + swapped(suffix_dkv, "ctx")
    local_ids = jnp.arange(own_slots, dtype=jnp.int32)
    pair_ids = jnp.arange(2, dtype=jnp.int32)
    collected = None
    for step in range(owners // 2):
        target = (owner_rank + 2 * step) % owners
        wanted = picked == ((target ^ pair_ids)[:, None] * own_slots + local_ids[None, :])
        sent = jnp.where(wanted[:, :, None, None], summed_dkv[None, None], 0.0)
        if step:
            sent = shifted(sent, "dp", 2 * step)
        collected = sent if collected is None else collected + sent
    slot_total = collected[0] + swapped(collected[1], "dp")
    key_full = key_weight.astype(jnp.float32)
    value_full = value_weight.astype(jnp.float32)
    suffix_grad = jnp.einsum(
        "slk,dk->sld", slot_total[:, :, :kv_width], key_full, precision=lax.Precision.HIGHEST
    )
    suffix_grad = suffix_grad + jnp.einsum(
        "slk,dk->sld", slot_total[:, :, kv_width:], value_full, precision=lax.Precision.HIGHEST
    )
    key_grad = (dk_local + back_k).astype(jnp.bfloat16)[None]
    value_grad = (dv_local + back_v).astype(jnp.bfloat16)[None]
    return (dq[None], key_grad, value_grad, suffix_grad)


def solution(mesh):
    return jax.shard_map(
        per_device,
        mesh=mesh,
        in_specs=(
            P(("groups", "dp"), "ctx", None),
            P(("groups", "dp"), "ctx", None),
            P(("groups", "dp"), "ctx", None),
            P(("groups", "dp"), "ctx", None),
            P("ctx", None),
            P("ctx", None),
            P(("groups", "dp"), None, "ctx"),
            P(("groups", "dp")),
            P("groups"),
            P(("groups", "dp")),
            P(("groups", "dp"), None),
        ),
        out_specs=(
            P(("groups", "dp"), "ctx", None),
            P(("groups", "dp"), "ctx", None),
            P(("groups", "dp"), "ctx", None),
            P(("groups", "dp"), None, "ctx"),
        ),
        check_vma=False,
    )
```

```python
import functools
import jax
import jax.numpy as jnp
from jax import lax
from jax.experimental import pallas as pl
from jax.experimental.pallas import tpu as pltpu
from jax.sharding import PartitionSpec as P

HEAD_DIM = 128
masked_fill = -1e30


def passed_along(block, axis, distance):
    devices = range(lax.axis_size(axis))
    route = [(i - distance, i) for i in devices if i - distance in devices]
    return lax.ppermute(block, axis, route)


def swapped(block, axis):
    devices = range(lax.axis_size(axis))
    route = [(i, i ^ 1) for i in devices]
    return lax.ppermute(block, axis, route)


def shifted(block, axis, distance):
    devices = range(lax.axis_size(axis))
    route = [(i, (i + distance) % len(devices)) for i in devices]
    return lax.ppermute(block, axis, route)


def paired_gather(block, axis):
    size = lax.axis_size(axis)
    pair = jnp.stack([block, swapped(block, axis)])
    return jnp.stack([pair] + [shifted(pair, axis, 2 * step) for step in range(1, size // 2)])


def attention_kernel(
    q_ref, do_ref, kl_ref, vl_ref, k_ref, v_ref, ks_ref, vs_ref, bias_ref,
    dq_ref, dk_local_ref, dv_local_ref, dk_prev_ref, dv_prev_ref, dk_suffix_ref, dv_suffix_ref,
    *, scale, tok_rows, suffix_len, group,
):
    k = jnp.concatenate([kl_ref[...], k_ref[...], ks_ref[...]], axis=0)
    v = jnp.concatenate([vl_ref[...], v_ref[...], vs_ref[...]], axis=0)
    k_t = k.astype(jnp.float32).T.astype(jnp.bfloat16)
    v_t = v.astype(jnp.float32).T.astype(jnp.bfloat16)
    bias = bias_ref[...]
    nt = (((1,), (1,)), ((), ()))
    key_total = None
    value_total = None
    for member in range(group):
        cols = slice(member * HEAD_DIM, (member + 1) * HEAD_DIM)
        q = q_ref[:, cols]
        grad = do_ref[:, cols]
        scores = lax.dot_general(k, q, nt, preferred_element_type=jnp.float32) * scale + bias
        row_max = jnp.max(scores, axis=0, keepdims=True)
        expo = jnp.exp(scores - row_max)
        total = jnp.sum(expo, axis=0, keepdims=True)
        inverse = 1.0 / total
        mixed = jnp.dot(v_t, expo.astype(jnp.bfloat16), preferred_element_type=jnp.float32)
        attended = (mixed * inverse).astype(jnp.bfloat16)
        grad_t = grad.astype(jnp.float32).T
        delta = jnp.sum(grad_t * attended.astype(jnp.float32), axis=0, keepdims=True)
        probs = expo * inverse
        prob_grad = lax.dot_general(v, grad, nt, preferred_element_type=jnp.float32)
        score_grad = (probs * (prob_grad - delta)).astype(jnp.bfloat16)
        query_piece = jnp.dot(k_t, score_grad, preferred_element_type=jnp.float32)
        dq_ref[:, cols] = (query_piece.T * scale).astype(dq_ref.dtype)
        key_piece = jnp.dot(score_grad, q, preferred_element_type=jnp.float32) * scale
        value_piece = jnp.dot(probs.astype(jnp.bfloat16), grad, preferred_element_type=jnp.float32)
        key_total = key_piece if key_total is None else key_total + key_piece
        value_total = value_piece if value_total is None else value_total + value_piece
    dk_local_ref[...] = key_total[:tok_rows]
    dv_local_ref[...] = value_total[:tok_rows]
    dk_prev_ref[...] = key_total[tok_rows : 2 * tok_rows]
    dv_prev_ref[...] = value_total[tok_rows : 2 * tok_rows]
    dk_suffix_ref[...] = key_total[2 * tok_rows : 2 * tok_rows + suffix_len]
    dv_suffix_ref[...] = value_total[2 * tok_rows : 2 * tok_rows + suffix_len]


def attend(queries2d, grads2d, keys2d, values2d, prev_kv, suffix_block, bias, kv_heads, group, suffix_len):
    tok_rows = queries2d.shape[0]
    n_keys = keys2d.shape[0] + prev_kv.shape[0] + suffix_block.shape[0]
    n_prompt = prev_kv.shape[0]
    n_suffix = suffix_block.shape[0]
    scale = HEAD_DIM ** (-0.5)
    kernel = functools.partial(
        attention_kernel, scale=scale, tok_rows=tok_rows, suffix_len=suffix_len, group=group
    )
    row_spec = pl.BlockSpec((tok_rows, group * HEAD_DIM), lambda h: (0, h))
    head_spec = pl.BlockSpec((tok_rows, HEAD_DIM), lambda h: (0, h))
    suffix_spec = pl.BlockSpec((suffix_len, HEAD_DIM), lambda h: (0, h))
    width = kv_heads * HEAD_DIM
    return pl.pallas_call(
        kernel,
        grid=(kv_heads,),
        in_specs=[
            row_spec,
            row_spec,
            pl.BlockSpec((tok_rows, HEAD_DIM), lambda h: (0, h)),
            pl.BlockSpec((tok_rows, HEAD_DIM), lambda h: (0, h)),
            pl.BlockSpec((n_prompt, HEAD_DIM), lambda h: (0, h)),
            pl.BlockSpec((n_prompt, HEAD_DIM), lambda h: (0, kv_heads + h)),
            pl.BlockSpec((n_suffix, HEAD_DIM), lambda h: (0, h)),
            pl.BlockSpec((n_suffix, HEAD_DIM), lambda h: (0, kv_heads + h)),
            pl.BlockSpec((n_keys, tok_rows), lambda h: (0, 0)),
        ],
        out_specs=[row_spec, head_spec, head_spec, head_spec, head_spec, suffix_spec, suffix_spec],
        out_shape=[jax.ShapeDtypeStruct(queries2d.shape, jnp.bfloat16)]
        + [jax.ShapeDtypeStruct((tok_rows, width), jnp.float32)] * 4
        + [jax.ShapeDtypeStruct((suffix_len, width), jnp.float32)] * 2,
        compiler_params=pltpu.CompilerParams(dimension_semantics=("arbitrary",)),
        cost_estimate=pl.CostEstimate(
            flops=12 * tok_rows * n_keys * HEAD_DIM * kv_heads * group,
            transcendentals=tok_rows * n_keys * kv_heads * group,
            bytes_accessed=6 * queries2d.size + 2 * n_keys * 2 * width + 4 * bias.size + 16 * tok_rows * width,
        ),
    )(queries2d, grads2d, keys2d, values2d, prev_kv, prev_kv, suffix_block, suffix_block, bias)


def per_device(
    queries,
    keys,
    values,
    out_grad,
    key_weight,
    value_weight,
    suffix_embed,
    class_ids,
    class_slot,
    pad_offset,
    suffix_pos,
):
    cycle_size = lax.axis_size("ctx")
    cycle_rank = lax.axis_index("ctx")
    owners = lax.axis_size("dp")
    owner_rank = lax.axis_index("dp")
    tok_rows = queries.shape[1]
    kv_width = keys.shape[2]
    kv_heads = kv_width // HEAD_DIM
    group = queries.shape[2] // kv_width
    own_slots = suffix_embed.shape[0]
    suffix_len = suffix_embed.shape[1]
    classes = class_slot.shape[0]
    slot_ids = jnp.arange(classes, dtype=jnp.int32)
    picked = jnp.sum(jnp.where(slot_ids == class_ids[0], class_slot, 0))
    owned_kv = jnp.concatenate(
        [
            jnp.einsum("sld,dk->slk", suffix_embed, key_weight, preferred_element_type=jnp.float32),
            jnp.einsum("sld,dk->slk", suffix_embed, value_weight, preferred_element_type=jnp.float32),
        ],
        axis=2,
    )
    owner = picked // own_slots
    partner = (owner_rank ^ owner) & 1
    source_step = ((owner_rank - (owner ^ partner)) % owners) // 2
    half_kv = paired_gather(owned_kv, "dp")[source_step, partner, picked % own_slots]
    suffix_kv = (half_kv + swapped(half_kv, "ctx")).astype(jnp.bfloat16)
    query_pos = cycle_rank * tok_rows + jnp.arange(tok_rows, dtype=jnp.int32)
    offset = pad_offset[0]
    local_kv = jnp.concatenate([keys[0], values[0]], axis=1)
    prev_kv = passed_along(local_kv, "ctx", 1)
    pad_rows = (-(2 * tok_rows + suffix_len)) % 128
    suffix_block = jnp.concatenate(
        [suffix_kv, jnp.zeros((pad_rows, 2 * kv_width), jnp.bfloat16)], axis=0
    )
    rows = jnp.arange(tok_rows, dtype=jnp.int32)
    far = jnp.full((pad_rows,), 1 << 30, jnp.int32)
    key_pos = jnp.concatenate(
        [
            cycle_rank * tok_rows + rows,
            ((cycle_rank - 1) % cycle_size) * tok_rows + rows,
            suffix_pos[0],
            far,
        ]
    )
    earlier = key_pos[None, :] <= query_pos[:, None]
    kept = (key_pos[None, :] >= offset) | (key_pos[None, :] == query_pos[:, None])
    bias = jnp.where(earlier & kept, 0.0, masked_fill).astype(jnp.float32).T
    dq, dk_local, dv_local, dk_prev, dv_prev, dk_suffix, dv_suffix = attend(
        queries[0], out_grad[0], keys[0], values[0], prev_kv, suffix_block, bias, kv_heads, group, suffix_len
    )
    back_k = passed_along(dk_prev, "ctx", -1)
    back_v = passed_along(dv_prev, "ctx", -1)
    suffix_dkv = jnp.concatenate([dk_suffix, dv_suffix], axis=1)
    summed_dkv = suffix_dkv + swapped(suffix_dkv, "ctx")
    local_ids = jnp.arange(own_slots, dtype=jnp.int32)
    pair_ids = jnp.arange(2, dtype=jnp.int32)
    collected = None
    for step in range(owners // 2):
        target = (owner_rank + 2 * step) % owners
        wanted = picked == ((target ^ pair_ids)[:, None] * own_slots + local_ids[None, :])
        sent = jnp.where(wanted[:, :, None, None], summed_dkv[None, None], 0.0)
        if step:
            sent = shifted(sent, "dp", 2 * step)
        collected = sent if collected is None else collected + sent
    slot_total = collected[0] + swapped(collected[1], "dp")
    key_full = key_weight.astype(jnp.float32)
    value_full = value_weight.astype(jnp.float32)
    suffix_grad = jnp.einsum(
        "slk,dk->sld", slot_total[:, :, :kv_width], key_full, precision=lax.Precision.HIGHEST
    )
    suffix_grad = suffix_grad + jnp.einsum(
        "slk,dk->sld", slot_total[:, :, kv_width:], value_full, precision=lax.Precision.HIGHEST
    )
    key_grad = (dk_local + back_k).astype(jnp.bfloat16)[None]
    value_grad = (dv_local + back_v).astype(jnp.bfloat16)[None]
    return (dq[None], key_grad, value_grad, suffix_grad)


def solution(mesh):
    return jax.shard_map(
        per_device,
        mesh=mesh,
        in_specs=(
            P(("groups", "dp"), "ctx", None),
            P(("groups", "dp"), "ctx", None),
            P(("groups", "dp"), "ctx", None),
            P(("groups", "dp"), "ctx", None),
            P("ctx", None),
            P("ctx", None),
            P(("groups", "dp"), None, "ctx"),
            P(("groups", "dp")),
            P("groups"),
            P(("groups", "dp")),
            P(("groups", "dp"), None),
        ),
        out_specs=(
            P(("groups", "dp"), "ctx", None),
            P(("groups", "dp"), "ctx", None),
            P(("groups", "dp"), "ctx", None),
            P(("groups", "dp"), None, "ctx"),
        ),
        check_vma=False,
    )
```

```python
import functools
import jax
import jax.numpy as jnp
from jax import lax
from jax.experimental import pallas as pl
from jax.experimental.pallas import tpu as pltpu
from jax.sharding import PartitionSpec as P

HEAD_DIM = 128
masked_fill = -1e30


def passed_along(block, axis, distance):
    devices = range(lax.axis_size(axis))
    route = [(i - distance, i) for i in devices if i - distance in devices]
    return lax.ppermute(block, axis, route)


def swapped(block, axis):
    devices = range(lax.axis_size(axis))
    route = [(i, i ^ 1) for i in devices]
    return lax.ppermute(block, axis, route)


def shifted(block, axis, distance):
    devices = range(lax.axis_size(axis))
    route = [(i, (i + distance) % len(devices)) for i in devices]
    return lax.ppermute(block, axis, route)


def paired_gather(block, axis):
    size = lax.axis_size(axis)
    pair = jnp.stack([block, swapped(block, axis)])
    return jnp.stack([pair] + [shifted(pair, axis, 2 * step) for step in range(1, size // 2)])


def attention_kernel(
    q_ref, do_ref, kl_ref, vl_ref, k_ref, v_ref, ks_ref, vs_ref, bias_ref,
    dq_ref, dk_local_ref, dv_local_ref, dk_prev_ref, dv_prev_ref, dk_suffix_ref, dv_suffix_ref,
    *, scale, tok_rows, suffix_len, group, pack,
):
    bias = bias_ref[...]
    nt = (((1,), (1,)), ((), ()))
    for sub in range(pack):
        lanes = slice(sub * HEAD_DIM, (sub + 1) * HEAD_DIM)
        k = jnp.concatenate([kl_ref[:, lanes], k_ref[:, lanes], ks_ref[:, lanes]], axis=0)
        v = jnp.concatenate([vl_ref[:, lanes], v_ref[:, lanes], vs_ref[:, lanes]], axis=0)
        k_t = k.astype(jnp.float32).T.astype(jnp.bfloat16)
        v_t = v.astype(jnp.float32).T.astype(jnp.bfloat16)
        key_total = None
        value_total = None
        for member in range(group):
            head = sub * group + member
            cols = slice(head * HEAD_DIM, (head + 1) * HEAD_DIM)
            q = q_ref[:, cols]
            grad = do_ref[:, cols]
            scores = lax.dot_general(k, q, nt, preferred_element_type=jnp.float32) * scale + bias
            row_max = jnp.max(scores, axis=0, keepdims=True)
            expo = jnp.exp(scores - row_max)
            total = jnp.sum(expo, axis=0, keepdims=True)
            inverse = 1.0 / total
            mixed = jnp.dot(v_t, expo.astype(jnp.bfloat16), preferred_element_type=jnp.float32)
            attended = (mixed * inverse).astype(jnp.bfloat16)
            grad_t = grad.astype(jnp.float32).T
            delta = jnp.sum(grad_t * attended.astype(jnp.float32), axis=0, keepdims=True)
            probs = expo * inverse
            prob_grad = lax.dot_general(v, grad, nt, preferred_element_type=jnp.float32)
            score_grad = (probs * (prob_grad - delta)).astype(jnp.bfloat16)
            query_piece = jnp.dot(k_t, score_grad, preferred_element_type=jnp.float32)
            dq_ref[:, cols] = (query_piece.T * scale).astype(dq_ref.dtype)
            key_piece = jnp.dot(score_grad, q, preferred_element_type=jnp.float32) * scale
            value_piece = jnp.dot(probs.astype(jnp.bfloat16), grad, preferred_element_type=jnp.float32)
            key_total = key_piece if key_total is None else key_total + key_piece
            value_total = value_piece if value_total is None else value_total + value_piece
        dk_local_ref[:, lanes] = key_total[:tok_rows]
        dv_local_ref[:, lanes] = value_total[:tok_rows]
        dk_prev_ref[:, lanes] = key_total[tok_rows : 2 * tok_rows]
        dv_prev_ref[:, lanes] = value_total[tok_rows : 2 * tok_rows]
        dk_suffix_ref[:, lanes] = key_total[2 * tok_rows : 2 * tok_rows + suffix_len]
        dv_suffix_ref[:, lanes] = value_total[2 * tok_rows : 2 * tok_rows + suffix_len]


def attend(queries2d, grads2d, keys2d, values2d, prev_kv, suffix_block, bias, kv_heads, group, suffix_len):
    tok_rows = queries2d.shape[0]
    n_keys = keys2d.shape[0] + prev_kv.shape[0] + suffix_block.shape[0]
    n_prompt = prev_kv.shape[0]
    n_suffix = suffix_block.shape[0]
    scale = HEAD_DIM ** (-0.5)
    pack = 2 if kv_heads % 2 == 0 else 1
    steps = kv_heads // pack
    lane = pack * HEAD_DIM
    kernel = functools.partial(
        attention_kernel, scale=scale, tok_rows=tok_rows, suffix_len=suffix_len, group=group, pack=pack
    )
    row_spec = pl.BlockSpec((tok_rows, group * lane), lambda h: (0, h))
    head_spec = pl.BlockSpec((tok_rows, lane), lambda h: (0, h))
    suffix_spec = pl.BlockSpec((suffix_len, lane), lambda h: (0, h))
    width = kv_heads * HEAD_DIM
    return pl.pallas_call(
        kernel,
        grid=(steps,),
        in_specs=[
            row_spec,
            row_spec,
            pl.BlockSpec((tok_rows, lane), lambda h: (0, h)),
            pl.BlockSpec((tok_rows, lane), lambda h: (0, h)),
            pl.BlockSpec((n_prompt, lane), lambda h: (0, h)),
            pl.BlockSpec((n_prompt, lane), lambda h: (0, steps + h)),
            pl.BlockSpec((n_suffix, lane), lambda h: (0, h)),
            pl.BlockSpec((n_suffix, lane), lambda h: (0, steps + h)),
            pl.BlockSpec((n_keys, tok_rows), lambda h: (0, 0)),
        ],
        out_specs=[row_spec, head_spec, head_spec, head_spec, head_spec, suffix_spec, suffix_spec],
        out_shape=[jax.ShapeDtypeStruct(queries2d.shape, jnp.bfloat16)]
        + [jax.ShapeDtypeStruct((tok_rows, width), jnp.float32)] * 4
        + [jax.ShapeDtypeStruct((suffix_len, width), jnp.float32)] * 2,
        compiler_params=pltpu.CompilerParams(dimension_semantics=("arbitrary",)),
        cost_estimate=pl.CostEstimate(
            flops=12 * tok_rows * n_keys * HEAD_DIM * kv_heads * group,
            transcendentals=tok_rows * n_keys * kv_heads * group,
            bytes_accessed=6 * queries2d.size + 2 * n_keys * 2 * width + 4 * bias.size + 16 * tok_rows * width,
        ),
    )(queries2d, grads2d, keys2d, values2d, prev_kv, prev_kv, suffix_block, suffix_block, bias)


def per_device(
    queries,
    keys,
    values,
    out_grad,
    key_weight,
    value_weight,
    suffix_embed,
    class_ids,
    class_slot,
    pad_offset,
    suffix_pos,
):
    cycle_size = lax.axis_size("ctx")
    cycle_rank = lax.axis_index("ctx")
    owners = lax.axis_size("dp")
    owner_rank = lax.axis_index("dp")
    tok_rows = queries.shape[1]
    kv_width = keys.shape[2]
    kv_heads = kv_width // HEAD_DIM
    group = queries.shape[2] // kv_width
    own_slots = suffix_embed.shape[0]
    suffix_len = suffix_embed.shape[1]
    classes = class_slot.shape[0]
    slot_ids = jnp.arange(classes, dtype=jnp.int32)
    picked = jnp.sum(jnp.where(slot_ids == class_ids[0], class_slot, 0))
    owned_kv = jnp.concatenate(
        [
            jnp.einsum("sld,dk->slk", suffix_embed, key_weight, preferred_element_type=jnp.float32),
            jnp.einsum("sld,dk->slk", suffix_embed, value_weight, preferred_element_type=jnp.float32),
        ],
        axis=2,
    )
    owner = picked // own_slots
    partner = (owner_rank ^ owner) & 1
    source_step = ((owner_rank - (owner ^ partner)) % owners) // 2
    half_kv = paired_gather(owned_kv, "dp")[source_step, partner, picked % own_slots]
    suffix_kv = (half_kv + swapped(half_kv, "ctx")).astype(jnp.bfloat16)
    query_pos = cycle_rank * tok_rows + jnp.arange(tok_rows, dtype=jnp.int32)
    offset = pad_offset[0]
    local_kv = jnp.concatenate([keys[0], values[0]], axis=1)
    prev_kv = passed_along(local_kv, "ctx", 1)
    pad_rows = (-(2 * tok_rows + suffix_len)) % 128
    suffix_block = jnp.concatenate(
        [suffix_kv, jnp.zeros((pad_rows, 2 * kv_width), jnp.bfloat16)], axis=0
    )
    rows = jnp.arange(tok_rows, dtype=jnp.int32)
    far = jnp.full((pad_rows,), 1 << 30, jnp.int32)
    key_pos = jnp.concatenate(
        [
            cycle_rank * tok_rows + rows,
            ((cycle_rank - 1) % cycle_size) * tok_rows + rows,
            suffix_pos[0],
            far,
        ]
    )
    earlier = key_pos[None, :] <= query_pos[:, None]
    kept = (key_pos[None, :] >= offset) | (key_pos[None, :] == query_pos[:, None])
    bias = jnp.where(earlier & kept, 0.0, masked_fill).astype(jnp.float32).T
    dq, dk_local, dv_local, dk_prev, dv_prev, dk_suffix, dv_suffix = attend(
        queries[0], out_grad[0], keys[0], values[0], prev_kv, suffix_block, bias, kv_heads, group, suffix_len
    )
    back_k = passed_along(dk_prev, "ctx", -1)
    back_v = passed_along(dv_prev, "ctx", -1)
    suffix_dkv = jnp.concatenate([dk_suffix, dv_suffix], axis=1)
    summed_dkv = suffix_dkv + swapped(suffix_dkv, "ctx")
    local_ids = jnp.arange(own_slots, dtype=jnp.int32)
    pair_ids = jnp.arange(2, dtype=jnp.int32)
    collected = None
    for step in range(owners // 2):
        target = (owner_rank + 2 * step) % owners
        wanted = picked == ((target ^ pair_ids)[:, None] * own_slots + local_ids[None, :])
        sent = jnp.where(wanted[:, :, None, None], summed_dkv[None, None], 0.0)
        if step:
            sent = shifted(sent, "dp", 2 * step)
        collected = sent if collected is None else collected + sent
    slot_total = collected[0] + swapped(collected[1], "dp")
    key_full = key_weight.astype(jnp.float32)
    value_full = value_weight.astype(jnp.float32)
    suffix_grad = jnp.einsum(
        "slk,dk->sld", slot_total[:, :, :kv_width], key_full, precision=lax.Precision.HIGHEST
    )
    suffix_grad = suffix_grad + jnp.einsum(
        "slk,dk->sld", slot_total[:, :, kv_width:], value_full, precision=lax.Precision.HIGHEST
    )
    key_grad = (dk_local + back_k).astype(jnp.bfloat16)[None]
    value_grad = (dv_local + back_v).astype(jnp.bfloat16)[None]
    return (dq[None], key_grad, value_grad, suffix_grad)


def solution(mesh):
    return jax.shard_map(
        per_device,
        mesh=mesh,
        in_specs=(
            P(("groups", "dp"), "ctx", None),
            P(("groups", "dp"), "ctx", None),
            P(("groups", "dp"), "ctx", None),
            P(("groups", "dp"), "ctx", None),
            P("ctx", None),
            P("ctx", None),
            P(("groups", "dp"), None, "ctx"),
            P(("groups", "dp")),
            P("groups"),
            P(("groups", "dp")),
            P(("groups", "dp"), None),
        ),
        out_specs=(
            P(("groups", "dp"), "ctx", None),
            P(("groups", "dp"), "ctx", None),
            P(("groups", "dp"), "ctx", None),
            P(("groups", "dp"), None, "ctx"),
        ),
        check_vma=False,
    )
```

```python
import functools
import jax
import jax.numpy as jnp
from jax import lax
from jax.experimental import pallas as pl
from jax.experimental.pallas import tpu as pltpu
from jax.sharding import PartitionSpec as P

HEAD_DIM = 128
masked_fill = -1e30


def passed_along(block, axis, distance):
    devices = range(lax.axis_size(axis))
    route = [(i - distance, i) for i in devices if i - distance in devices]
    return lax.ppermute(block, axis, route)


def swapped(block, axis):
    devices = range(lax.axis_size(axis))
    route = [(i, i ^ 1) for i in devices]
    return lax.ppermute(block, axis, route)


def shifted(block, axis, distance):
    devices = range(lax.axis_size(axis))
    route = [(i, (i + distance) % len(devices)) for i in devices]
    return lax.ppermute(block, axis, route)


def paired_gather(block, axis):
    size = lax.axis_size(axis)
    pair = jnp.stack([block, swapped(block, axis)])
    return jnp.stack([pair] + [shifted(pair, axis, 2 * step) for step in range(1, size // 2)])


def attention_kernel(
    q_ref, do_ref, kl_ref, vl_ref, k_ref, v_ref, ks_ref, vs_ref, bias_ref,
    dq_ref, dk_local_ref, dv_local_ref, dk_prev_ref, dv_prev_ref, dk_suffix_ref, dv_suffix_ref,
    *, scale, tok_rows, suffix_len, group,
):
    k = jnp.concatenate([kl_ref[...], k_ref[...], ks_ref[...]], axis=0)
    v = jnp.concatenate([vl_ref[...], v_ref[...], vs_ref[...]], axis=0)
    k_t = k.astype(jnp.float32).T.astype(jnp.bfloat16)
    v_t = v.astype(jnp.float32).T.astype(jnp.bfloat16)
    bias = bias_ref[...]
    nt = (((1,), (1,)), ((), ()))
    key_total = None
    value_total = None
    for member in range(group):
        cols = slice(member * HEAD_DIM, (member + 1) * HEAD_DIM)
        q = q_ref[:, cols]
        grad = do_ref[:, cols]
        scores = lax.dot_general(k, q, nt, preferred_element_type=jnp.float32) * scale + bias
        row_max = jnp.max(scores, axis=0, keepdims=True)
        expo = jnp.exp(scores - row_max)
        total = jnp.sum(expo, axis=0, keepdims=True)
        inverse = 1.0 / total
        mixed = jnp.dot(v_t, expo.astype(jnp.bfloat16), preferred_element_type=jnp.float32)
        attended = (mixed * inverse).astype(jnp.bfloat16)
        grad_t = grad.astype(jnp.float32).T
        delta = jnp.sum(grad_t * attended.astype(jnp.float32), axis=0, keepdims=True)
        probs = expo * inverse
        prob_grad = lax.dot_general(v, grad, nt, preferred_element_type=jnp.float32)
        score_grad = (probs * (prob_grad - delta)).astype(jnp.bfloat16)
        query_piece = jnp.dot(k_t, score_grad, preferred_element_type=jnp.float32)
        dq_ref[:, cols] = (query_piece.T * scale).astype(dq_ref.dtype)
        key_piece = jnp.dot(score_grad, q, preferred_element_type=jnp.float32) * scale
        value_piece = jnp.dot(probs.astype(jnp.bfloat16), grad, preferred_element_type=jnp.float32)
        key_total = key_piece if key_total is None else key_total + key_piece
        value_total = value_piece if value_total is None else value_total + value_piece
    dk_local_ref[...] = key_total[:tok_rows]
    dv_local_ref[...] = value_total[:tok_rows]
    dk_prev_ref[...] = key_total[tok_rows : 2 * tok_rows]
    dv_prev_ref[...] = value_total[tok_rows : 2 * tok_rows]
    dk_suffix_ref[...] = key_total[2 * tok_rows : 2 * tok_rows + suffix_len]
    dv_suffix_ref[...] = value_total[2 * tok_rows : 2 * tok_rows + suffix_len]


def attend(queries2d, grads2d, keys2d, values2d, prev_kv, suffix_block, bias, kv_heads, group, suffix_len):
    tok_rows = queries2d.shape[0]
    n_keys = keys2d.shape[0] + prev_kv.shape[0] + suffix_block.shape[0]
    n_prompt = prev_kv.shape[0]
    n_suffix = suffix_block.shape[0]
    scale = HEAD_DIM ** (-0.5)
    kernel = functools.partial(
        attention_kernel, scale=scale, tok_rows=tok_rows, suffix_len=suffix_len, group=group
    )
    row_spec = pl.BlockSpec((tok_rows, group * HEAD_DIM), lambda h: (0, h))
    head_spec = pl.BlockSpec((tok_rows, HEAD_DIM), lambda h: (0, h))
    suffix_spec = pl.BlockSpec((suffix_len, HEAD_DIM), lambda h: (0, h))
    width = kv_heads * HEAD_DIM
    return pl.pallas_call(
        kernel,
        grid=(kv_heads,),
        in_specs=[
            row_spec,
            row_spec,
            pl.BlockSpec((tok_rows, HEAD_DIM), lambda h: (0, h)),
            pl.BlockSpec((tok_rows, HEAD_DIM), lambda h: (0, h)),
            pl.BlockSpec((n_prompt, HEAD_DIM), lambda h: (0, h)),
            pl.BlockSpec((n_prompt, HEAD_DIM), lambda h: (0, kv_heads + h)),
            pl.BlockSpec((n_suffix, HEAD_DIM), lambda h: (0, h)),
            pl.BlockSpec((n_suffix, HEAD_DIM), lambda h: (0, kv_heads + h)),
            pl.BlockSpec((n_keys, tok_rows), lambda h: (0, 0)),
        ],
        out_specs=[row_spec, head_spec, head_spec, head_spec, head_spec, suffix_spec, suffix_spec],
        out_shape=[jax.ShapeDtypeStruct(queries2d.shape, jnp.bfloat16)]
        + [jax.ShapeDtypeStruct((tok_rows, width), jnp.float32)] * 4
        + [jax.ShapeDtypeStruct((suffix_len, width), jnp.float32)] * 2,
        compiler_params=pltpu.CompilerParams(dimension_semantics=("arbitrary",)),
        cost_estimate=pl.CostEstimate(
            flops=12 * tok_rows * n_keys * HEAD_DIM * kv_heads * group,
            transcendentals=tok_rows * n_keys * kv_heads * group,
            bytes_accessed=6 * queries2d.size + 2 * n_keys * 2 * width + 4 * bias.size + 16 * tok_rows * width,
        ),
    )(queries2d, grads2d, keys2d, values2d, prev_kv, prev_kv, suffix_block, suffix_block, bias)


def per_device(
    queries,
    keys,
    values,
    out_grad,
    key_weight,
    value_weight,
    suffix_embed,
    class_ids,
    class_slot,
    pad_offset,
    suffix_pos,
):
    cycle_size = lax.axis_size("ctx")
    cycle_rank = lax.axis_index("ctx")
    owners = lax.axis_size("dp")
    owner_rank = lax.axis_index("dp")
    tok_rows = queries.shape[1]
    kv_width = keys.shape[2]
    kv_heads = kv_width // HEAD_DIM
    group = queries.shape[2] // kv_width
    own_slots = suffix_embed.shape[0]
    suffix_len = suffix_embed.shape[1]
    classes = class_slot.shape[0]
    slot_ids = jnp.arange(classes, dtype=jnp.int32)
    picked = jnp.sum(jnp.where(slot_ids == class_ids[0], class_slot, 0))
    owned_kv = jnp.concatenate(
        [
            jnp.einsum("sld,dk->slk", suffix_embed, key_weight, preferred_element_type=jnp.float32),
            jnp.einsum("sld,dk->slk", suffix_embed, value_weight, preferred_element_type=jnp.float32),
        ],
        axis=2,
    )
    owner = picked // own_slots
    partner = (owner_rank ^ owner) & 1
    source_step = ((owner_rank - (owner ^ partner)) % owners) // 2
    pair = jnp.stack([owned_kv, swapped(owned_kv, "dp")])
    pair, keys, values, pad_offset, suffix_pos = lax.optimization_barrier(
        (pair, keys, values, pad_offset, suffix_pos)
    )
    gathered_pairs = jnp.stack(
        [pair] + [shifted(pair, "dp", 2 * step) for step in range(1, owners // 2)]
    )
    half_kv = gathered_pairs[source_step, partner, picked % own_slots]
    suffix_kv = (half_kv + swapped(half_kv, "ctx")).astype(jnp.bfloat16)
    query_pos = cycle_rank * tok_rows + jnp.arange(tok_rows, dtype=jnp.int32)
    offset = pad_offset[0]
    local_kv = jnp.concatenate([keys[0], values[0]], axis=1)
    prev_kv = passed_along(local_kv, "ctx", 1)
    pad_rows = (-(2 * tok_rows + suffix_len)) % 128
    suffix_block = jnp.concatenate(
        [suffix_kv, jnp.zeros((pad_rows, 2 * kv_width), jnp.bfloat16)], axis=0
    )
    rows = jnp.arange(tok_rows, dtype=jnp.int32)
    far = jnp.full((pad_rows,), 1 << 30, jnp.int32)
    key_pos = jnp.concatenate(
        [
            cycle_rank * tok_rows + rows,
            ((cycle_rank - 1) % cycle_size) * tok_rows + rows,
            suffix_pos[0],
            far,
        ]
    )
    earlier = key_pos[None, :] <= query_pos[:, None]
    kept = (key_pos[None, :] >= offset) | (key_pos[None, :] == query_pos[:, None])
    bias = jnp.where(earlier & kept, 0.0, masked_fill).astype(jnp.float32).T
    dq, dk_local, dv_local, dk_prev, dv_prev, dk_suffix, dv_suffix = attend(
        queries[0], out_grad[0], keys[0], values[0], prev_kv, suffix_block, bias, kv_heads, group, suffix_len
    )
    back_k = passed_along(dk_prev, "ctx", -1)
    back_v = passed_along(dv_prev, "ctx", -1)
    suffix_dkv = jnp.concatenate([dk_suffix, dv_suffix], axis=1)
    summed_dkv = suffix_dkv + swapped(suffix_dkv, "ctx")
    local_ids = jnp.arange(own_slots, dtype=jnp.int32)
    pair_ids = jnp.arange(2, dtype=jnp.int32)
    collected = None
    for step in range(owners // 2):
        target = (owner_rank + 2 * step) % owners
        wanted = picked == ((target ^ pair_ids)[:, None] * own_slots + local_ids[None, :])
        sent = jnp.where(wanted[:, :, None, None], summed_dkv[None, None], 0.0)
        if step:
            sent = shifted(sent, "dp", 2 * step)
        collected = sent if collected is None else collected + sent
    slot_total = collected[0] + swapped(collected[1], "dp")
    key_full = key_weight.astype(jnp.float32)
    value_full = value_weight.astype(jnp.float32)
    suffix_grad = jnp.einsum(
        "slk,dk->sld", slot_total[:, :, :kv_width], key_full, precision=lax.Precision.HIGHEST
    )
    suffix_grad = suffix_grad + jnp.einsum(
        "slk,dk->sld", slot_total[:, :, kv_width:], value_full, precision=lax.Precision.HIGHEST
    )
    key_grad = (dk_local + back_k).astype(jnp.bfloat16)[None]
    value_grad = (dv_local + back_v).astype(jnp.bfloat16)[None]
    return (dq[None], key_grad, value_grad, suffix_grad)


def solution(mesh):
    return jax.shard_map(
        per_device,
        mesh=mesh,
        in_specs=(
            P(("groups", "dp"), "ctx", None),
            P(("groups", "dp"), "ctx", None),
            P(("groups", "dp"), "ctx", None),
            P(("groups", "dp"), "ctx", None),
            P("ctx", None),
            P("ctx", None),
            P(("groups", "dp"), None, "ctx"),
            P(("groups", "dp")),
            P("groups"),
            P(("groups", "dp")),
            P(("groups", "dp"), None),
        ),
        out_specs=(
            P(("groups", "dp"), "ctx", None),
            P(("groups", "dp"), "ctx", None),
            P(("groups", "dp"), "ctx", None),
            P(("groups", "dp"), None, "ctx"),
        ),
        check_vma=False,
    )
```

```python
import functools
import jax
import jax.numpy as jnp
from jax import lax
from jax.experimental import pallas as pl
from jax.experimental.pallas import tpu as pltpu
from jax.sharding import PartitionSpec as P

HEAD_DIM = 128
masked_fill = -1e30


def passed_along(block, axis, distance):
    devices = range(lax.axis_size(axis))
    route = [(i - distance, i) for i in devices if i - distance in devices]
    return lax.ppermute(block, axis, route)


def swapped(block, axis):
    devices = range(lax.axis_size(axis))
    route = [(i, i ^ 1) for i in devices]
    return lax.ppermute(block, axis, route)


def shifted(block, axis, distance):
    devices = range(lax.axis_size(axis))
    route = [(i, (i + distance) % len(devices)) for i in devices]
    return lax.ppermute(block, axis, route)


def paired_gather(block, axis):
    size = lax.axis_size(axis)
    pair = jnp.stack([block, swapped(block, axis)])
    return jnp.stack([pair] + [shifted(pair, axis, 2 * step) for step in range(1, size // 2)])


def attention_kernel(
    q_ref, do_ref, kl_ref, vl_ref, k_ref, v_ref, ks_ref, vs_ref, bias_ref,
    dq_ref, dk_local_ref, dv_local_ref, dk_prev_ref, dv_prev_ref, dk_suffix_ref, dv_suffix_ref,
    *, scale, tok_rows, suffix_len, group,
):
    k = jnp.concatenate([kl_ref[...], k_ref[...], ks_ref[...]], axis=0)
    v = jnp.concatenate([vl_ref[...], v_ref[...], vs_ref[...]], axis=0)
    k_t = k.astype(jnp.float32).T.astype(jnp.bfloat16)
    v_t = v.astype(jnp.float32).T.astype(jnp.bfloat16)
    bias = bias_ref[...]
    nt = (((1,), (1,)), ((), ()))
    key_total = None
    value_total = None
    for member in range(group):
        cols = slice(member * HEAD_DIM, (member + 1) * HEAD_DIM)
        q = q_ref[:, cols]
        grad = do_ref[:, cols]
        scores = lax.dot_general(k, q, nt, preferred_element_type=jnp.float32) * scale + bias
        row_max = jnp.max(scores, axis=0, keepdims=True)
        expo = jnp.exp(scores - row_max)
        total = jnp.sum(expo, axis=0, keepdims=True)
        inverse = 1.0 / total
        mixed = jnp.dot(v_t, expo.astype(jnp.bfloat16), preferred_element_type=jnp.float32)
        attended = (mixed * inverse).astype(jnp.bfloat16)
        grad_t = grad.astype(jnp.float32).T
        delta = jnp.sum(grad_t * attended.astype(jnp.float32), axis=0, keepdims=True)
        probs = expo * inverse
        prob_grad = lax.dot_general(v, grad, nt, preferred_element_type=jnp.float32)
        score_grad = (probs * (prob_grad - delta)).astype(jnp.bfloat16)
        query_piece = jnp.dot(k_t, score_grad, preferred_element_type=jnp.float32)
        dq_ref[:, cols] = (query_piece.T * scale).astype(dq_ref.dtype)
        key_piece = jnp.dot(score_grad, q, preferred_element_type=jnp.float32) * scale
        value_piece = jnp.dot(probs.astype(jnp.bfloat16), grad, preferred_element_type=jnp.float32)
        key_total = key_piece if key_total is None else key_total + key_piece
        value_total = value_piece if value_total is None else value_total + value_piece
    dk_local_ref[...] = key_total[:tok_rows]
    dv_local_ref[...] = value_total[:tok_rows]
    dk_prev_ref[...] = key_total[tok_rows : 2 * tok_rows]
    dv_prev_ref[...] = value_total[tok_rows : 2 * tok_rows]
    dk_suffix_ref[...] = key_total[2 * tok_rows : 2 * tok_rows + suffix_len]
    dv_suffix_ref[...] = value_total[2 * tok_rows : 2 * tok_rows + suffix_len]


def attend(queries2d, grads2d, keys2d, values2d, prev_kv, suffix_block, bias, kv_heads, group, suffix_len):
    tok_rows = queries2d.shape[0]
    n_keys = keys2d.shape[0] + prev_kv.shape[0] + suffix_block.shape[0]
    n_prompt = prev_kv.shape[0]
    n_suffix = suffix_block.shape[0]
    scale = HEAD_DIM ** (-0.5)
    kernel = functools.partial(
        attention_kernel, scale=scale, tok_rows=tok_rows, suffix_len=suffix_len, group=group
    )
    row_spec = pl.BlockSpec((tok_rows, group * HEAD_DIM), lambda h: (0, h))
    head_spec = pl.BlockSpec((tok_rows, HEAD_DIM), lambda h: (0, h))
    suffix_spec = pl.BlockSpec((suffix_len, HEAD_DIM), lambda h: (0, h))
    width = kv_heads * HEAD_DIM
    return pl.pallas_call(
        kernel,
        grid=(kv_heads,),
        in_specs=[
            row_spec,
            row_spec,
            pl.BlockSpec((tok_rows, HEAD_DIM), lambda h: (0, h)),
            pl.BlockSpec((tok_rows, HEAD_DIM), lambda h: (0, h)),
            pl.BlockSpec((n_prompt, HEAD_DIM), lambda h: (0, h)),
            pl.BlockSpec((n_prompt, HEAD_DIM), lambda h: (0, kv_heads + h)),
            pl.BlockSpec((n_suffix, HEAD_DIM), lambda h: (0, h)),
            pl.BlockSpec((n_suffix, HEAD_DIM), lambda h: (0, kv_heads + h)),
            pl.BlockSpec((n_keys, tok_rows), lambda h: (0, 0)),
        ],
        out_specs=[row_spec, head_spec, head_spec, head_spec, head_spec, suffix_spec, suffix_spec],
        out_shape=[jax.ShapeDtypeStruct(queries2d.shape, jnp.bfloat16)]
        + [jax.ShapeDtypeStruct((tok_rows, width), jnp.float32)] * 4
        + [jax.ShapeDtypeStruct((suffix_len, width), jnp.float32)] * 2,
        compiler_params=pltpu.CompilerParams(dimension_semantics=("arbitrary",)),
        cost_estimate=pl.CostEstimate(
            flops=12 * tok_rows * n_keys * HEAD_DIM * kv_heads * group,
            transcendentals=tok_rows * n_keys * kv_heads * group,
            bytes_accessed=6 * queries2d.size + 2 * n_keys * 2 * width + 4 * bias.size + 16 * tok_rows * width,
        ),
    )(queries2d, grads2d, keys2d, values2d, prev_kv, prev_kv, suffix_block, suffix_block, bias)


def per_device(
    queries,
    keys,
    values,
    out_grad,
    key_weight,
    value_weight,
    suffix_embed,
    class_ids,
    class_slot,
    pad_offset,
    suffix_pos,
):
    cycle_size = lax.axis_size("ctx")
    cycle_rank = lax.axis_index("ctx")
    owners = lax.axis_size("dp")
    owner_rank = lax.axis_index("dp")
    tok_rows = queries.shape[1]
    kv_width = keys.shape[2]
    kv_heads = kv_width // HEAD_DIM
    group = queries.shape[2] // kv_width
    own_slots = suffix_embed.shape[0]
    suffix_len = suffix_embed.shape[1]
    classes = class_slot.shape[0]
    slot_ids = jnp.arange(classes, dtype=jnp.int32)
    picked = jnp.sum(jnp.where(slot_ids == class_ids[0], class_slot, 0))
    owned_kv = jnp.concatenate(
        [
            jnp.einsum("sld,dk->slk", suffix_embed, key_weight, preferred_element_type=jnp.float32),
            jnp.einsum("sld,dk->slk", suffix_embed, value_weight, preferred_element_type=jnp.float32),
        ],
        axis=2,
    )
    owner = picked // own_slots
    partner = (owner_rank ^ owner) & 1
    source_step = ((owner_rank - (owner ^ partner)) % owners) // 2
    pair = jnp.stack([owned_kv, swapped(owned_kv, "dp")])
    pair, keys, values, pad_offset, suffix_pos = lax.optimization_barrier(
        (pair, keys, values, pad_offset, suffix_pos)
    )
    gathered_pairs = jnp.stack(
        [pair] + [shifted(pair, "dp", 2 * step) for step in range(1, owners // 2)]
    )
    half_kv = gathered_pairs[source_step, partner, picked % own_slots]
    suffix_kv = (half_kv + swapped(half_kv, "ctx")).astype(jnp.bfloat16)
    query_pos = cycle_rank * tok_rows + jnp.arange(tok_rows, dtype=jnp.int32)
    offset = pad_offset[0]
    local_kv = jnp.concatenate([keys[0], values[0]], axis=1)
    prev_kv = passed_along(local_kv, "ctx", 1)
    pad_rows = (-suffix_len) % 16
    suffix_block = jnp.concatenate(
        [suffix_kv, jnp.zeros((pad_rows, 2 * kv_width), jnp.bfloat16)], axis=0
    )
    rows = jnp.arange(tok_rows, dtype=jnp.int32)
    far = jnp.full((pad_rows,), 1 << 30, jnp.int32)
    key_pos = jnp.concatenate(
        [
            cycle_rank * tok_rows + rows,
            ((cycle_rank - 1) % cycle_size) * tok_rows + rows,
            suffix_pos[0],
            far,
        ]
    )
    earlier = key_pos[None, :] <= query_pos[:, None]
    kept = (key_pos[None, :] >= offset) | (key_pos[None, :] == query_pos[:, None])
    bias = jnp.where(earlier & kept, 0.0, masked_fill).astype(jnp.float32).T
    dq, dk_local, dv_local, dk_prev, dv_prev, dk_suffix, dv_suffix = attend(
        queries[0], out_grad[0], keys[0], values[0], prev_kv, suffix_block, bias, kv_heads, group, suffix_len
    )
    back_k = passed_along(dk_prev, "ctx", -1)
    back_v = passed_along(dv_prev, "ctx", -1)
    suffix_dkv = jnp.concatenate([dk_suffix, dv_suffix], axis=1)
    summed_dkv = suffix_dkv + swapped(suffix_dkv, "ctx")
    local_ids = jnp.arange(own_slots, dtype=jnp.int32)
    pair_ids = jnp.arange(2, dtype=jnp.int32)
    collected = None
    for step in range(owners // 2):
        target = (owner_rank + 2 * step) % owners
        wanted = picked == ((target ^ pair_ids)[:, None] * own_slots + local_ids[None, :])
        sent = jnp.where(wanted[:, :, None, None], summed_dkv[None, None], 0.0)
        if step:
            sent = shifted(sent, "dp", 2 * step)
        collected = sent if collected is None else collected + sent
    slot_total = collected[0] + swapped(collected[1], "dp")
    key_full = key_weight.astype(jnp.float32)
    value_full = value_weight.astype(jnp.float32)
    suffix_grad = jnp.einsum(
        "slk,dk->sld", slot_total[:, :, :kv_width], key_full, precision=lax.Precision.HIGHEST
    )
    suffix_grad = suffix_grad + jnp.einsum(
        "slk,dk->sld", slot_total[:, :, kv_width:], value_full, precision=lax.Precision.HIGHEST
    )
    key_grad = (dk_local + back_k).astype(jnp.bfloat16)[None]
    value_grad = (dv_local + back_v).astype(jnp.bfloat16)[None]
    return (dq[None], key_grad, value_grad, suffix_grad)


def solution(mesh):
    return jax.shard_map(
        per_device,
        mesh=mesh,
        in_specs=(
            P(("groups", "dp"), "ctx", None),
            P(("groups", "dp"), "ctx", None),
            P(("groups", "dp"), "ctx", None),
            P(("groups", "dp"), "ctx", None),
            P("ctx", None),
            P("ctx", None),
            P(("groups", "dp"), None, "ctx"),
            P(("groups", "dp")),
            P("groups"),
            P(("groups", "dp")),
            P(("groups", "dp"), None),
        ),
        out_specs=(
            P(("groups", "dp"), "ctx", None),
            P(("groups", "dp"), "ctx", None),
            P(("groups", "dp"), "ctx", None),
            P(("groups", "dp"), None, "ctx"),
        ),
        check_vma=False,
    )
```

```python
import functools
import jax
import jax.numpy as jnp
from jax import lax
from jax.experimental import pallas as pl
from jax.experimental.pallas import tpu as pltpu
from jax.sharding import PartitionSpec as P

HEAD_DIM = 128
masked_fill = -1e30


def passed_along(block, axis, distance):
    devices = range(lax.axis_size(axis))
    route = [(i - distance, i) for i in devices if i - distance in devices]
    return lax.ppermute(block, axis, route)


def swapped(block, axis):
    devices = range(lax.axis_size(axis))
    route = [(i, i ^ 1) for i in devices]
    return lax.ppermute(block, axis, route)


def shifted(block, axis, distance):
    devices = range(lax.axis_size(axis))
    route = [(i, (i + distance) % len(devices)) for i in devices]
    return lax.ppermute(block, axis, route)


def paired_gather(block, axis):
    size = lax.axis_size(axis)
    pair = jnp.stack([block, swapped(block, axis)])
    return jnp.stack([pair] + [shifted(pair, axis, 2 * step) for step in range(1, size // 2)])


def attention_kernel(
    q_ref, do_ref, kl_ref, vl_ref, k_ref, v_ref, ks_ref, vs_ref, bias_ref,
    dq_ref, dk_local_ref, dv_local_ref, dk_prev_ref, dv_prev_ref, dk_suffix_ref, dv_suffix_ref,
    *, scale, tok_rows, suffix_len, group,
):
    k = jnp.concatenate([kl_ref[...], k_ref[...], ks_ref[...]], axis=0)
    v = jnp.concatenate([vl_ref[...], v_ref[...], vs_ref[...]], axis=0)
    k_t = k.astype(jnp.float32).T.astype(jnp.bfloat16)
    v_t = v.astype(jnp.float32).T.astype(jnp.bfloat16)
    bias = bias_ref[...]
    nt = (((1,), (1,)), ((), ()))
    key_total = None
    value_total = None
    for member in range(group):
        cols = slice(member * HEAD_DIM, (member + 1) * HEAD_DIM)
        q = q_ref[:, cols]
        grad = do_ref[:, cols]
        scores = lax.dot_general(k, q, nt, preferred_element_type=jnp.float32) * scale + bias
        row_max = jnp.max(scores, axis=0, keepdims=True)
        expo = jnp.exp(scores - row_max)
        total = jnp.sum(expo, axis=0, keepdims=True)
        inverse = 1.0 / total
        mixed = jnp.dot(v_t, expo.astype(jnp.bfloat16), preferred_element_type=jnp.float32)
        attended = (mixed * inverse).astype(jnp.bfloat16)
        grad_t = grad.astype(jnp.float32).T
        delta = jnp.sum(grad_t * attended.astype(jnp.float32), axis=0, keepdims=True)
        probs = expo * inverse
        prob_grad = lax.dot_general(v, grad, nt, preferred_element_type=jnp.float32)
        score_grad = (probs * (prob_grad - delta)).astype(jnp.bfloat16)
        query_piece = jnp.dot(k_t, score_grad, preferred_element_type=jnp.float32)
        dq_ref[:, cols] = (query_piece.T * scale).astype(dq_ref.dtype)
        key_piece = jnp.dot(score_grad, q, preferred_element_type=jnp.float32) * scale
        value_piece = jnp.dot(probs.astype(jnp.bfloat16), grad, preferred_element_type=jnp.float32)
        key_total = key_piece if key_total is None else key_total + key_piece
        value_total = value_piece if value_total is None else value_total + value_piece
    dk_local_ref[...] = key_total[:tok_rows]
    dv_local_ref[...] = value_total[:tok_rows]
    dk_prev_ref[...] = key_total[tok_rows : 2 * tok_rows]
    dv_prev_ref[...] = value_total[tok_rows : 2 * tok_rows]
    dk_suffix_ref[...] = key_total[2 * tok_rows : 2 * tok_rows + suffix_len]
    dv_suffix_ref[...] = value_total[2 * tok_rows : 2 * tok_rows + suffix_len]


def attend(queries2d, grads2d, keys2d, values2d, prev_kv, suffix_block, bias, kv_heads, group, suffix_len):
    tok_rows = queries2d.shape[0]
    n_keys = keys2d.shape[0] + prev_kv.shape[0] + suffix_block.shape[0]
    n_prompt = prev_kv.shape[0]
    n_suffix = suffix_block.shape[0]
    scale = HEAD_DIM ** (-0.5)
    kernel = functools.partial(
        attention_kernel, scale=scale, tok_rows=tok_rows, suffix_len=suffix_len, group=group
    )
    row_spec = pl.BlockSpec((tok_rows, group * HEAD_DIM), lambda h: (0, h))
    head_spec = pl.BlockSpec((tok_rows, HEAD_DIM), lambda h: (0, h))
    suffix_spec = pl.BlockSpec((suffix_len, HEAD_DIM), lambda h: (0, h))
    width = kv_heads * HEAD_DIM
    return pl.pallas_call(
        kernel,
        grid=(kv_heads,),
        in_specs=[
            row_spec,
            row_spec,
            pl.BlockSpec((tok_rows, HEAD_DIM), lambda h: (0, h)),
            pl.BlockSpec((tok_rows, HEAD_DIM), lambda h: (0, h)),
            pl.BlockSpec((n_prompt, HEAD_DIM), lambda h: (0, h)),
            pl.BlockSpec((n_prompt, HEAD_DIM), lambda h: (0, kv_heads + h)),
            pl.BlockSpec((n_suffix, HEAD_DIM), lambda h: (0, h)),
            pl.BlockSpec((n_suffix, HEAD_DIM), lambda h: (0, kv_heads + h)),
            pl.BlockSpec((n_keys, tok_rows), lambda h: (0, 0)),
        ],
        out_specs=[row_spec, head_spec, head_spec, head_spec, head_spec, suffix_spec, suffix_spec],
        out_shape=[jax.ShapeDtypeStruct(queries2d.shape, jnp.bfloat16)]
        + [jax.ShapeDtypeStruct((tok_rows, width), jnp.float32)] * 4
        + [jax.ShapeDtypeStruct((suffix_len, width), jnp.float32)] * 2,
        compiler_params=pltpu.CompilerParams(dimension_semantics=("arbitrary",)),
        cost_estimate=pl.CostEstimate(
            flops=12 * tok_rows * n_keys * HEAD_DIM * kv_heads * group,
            transcendentals=tok_rows * n_keys * kv_heads * group,
            bytes_accessed=6 * queries2d.size + 2 * n_keys * 2 * width + 4 * bias.size + 16 * tok_rows * width,
        ),
    )(queries2d, grads2d, keys2d, values2d, prev_kv, prev_kv, suffix_block, suffix_block, bias)


def per_device(
    queries,
    keys,
    values,
    out_grad,
    key_weight,
    value_weight,
    suffix_embed,
    class_ids,
    class_slot,
    pad_offset,
    suffix_pos,
):
    cycle_size = lax.axis_size("ctx")
    cycle_rank = lax.axis_index("ctx")
    owners = lax.axis_size("dp")
    owner_rank = lax.axis_index("dp")
    tok_rows = queries.shape[1]
    kv_width = keys.shape[2]
    kv_heads = kv_width // HEAD_DIM
    group = queries.shape[2] // kv_width
    own_slots = suffix_embed.shape[0]
    suffix_len = suffix_embed.shape[1]
    classes = class_slot.shape[0]
    slot_ids = jnp.arange(classes, dtype=jnp.int32)
    picked = jnp.sum(jnp.where(slot_ids == class_ids[0], class_slot, 0))
    owned_kv = jnp.concatenate(
        [
            jnp.einsum("sld,dk->slk", suffix_embed, key_weight, preferred_element_type=jnp.float32),
            jnp.einsum("sld,dk->slk", suffix_embed, value_weight, preferred_element_type=jnp.float32),
        ],
        axis=2,
    )
    owner = picked // own_slots
    partner = (owner_rank ^ owner) & 1
    source_step = ((owner_rank - (owner ^ partner)) % owners) // 2
    pair = jnp.stack([owned_kv, swapped(owned_kv, "dp")])
    pair, keys, values = lax.optimization_barrier((pair, keys, values))
    gathered_pairs = jnp.stack(
        [pair] + [shifted(pair, "dp", 2 * step) for step in range(1, owners // 2)]
    )
    half_kv = gathered_pairs[source_step, partner, picked % own_slots]
    suffix_kv = (half_kv + swapped(half_kv, "ctx")).astype(jnp.bfloat16)
    query_pos = cycle_rank * tok_rows + jnp.arange(tok_rows, dtype=jnp.int32)
    offset = pad_offset[0]
    local_kv = jnp.concatenate([keys[0], values[0]], axis=1)
    prev_kv = passed_along(local_kv, "ctx", 1)
    pad_rows = (-suffix_len) % 16
    suffix_block = jnp.concatenate(
        [suffix_kv, jnp.zeros((pad_rows, 2 * kv_width), jnp.bfloat16)], axis=0
    )
    rows = jnp.arange(tok_rows, dtype=jnp.int32)
    far = jnp.full((pad_rows,), 1 << 30, jnp.int32)
    key_pos = jnp.concatenate(
        [
            cycle_rank * tok_rows + rows,
            ((cycle_rank - 1) % cycle_size) * tok_rows + rows,
            suffix_pos[0],
            far,
        ]
    )
    earlier = key_pos[None, :] <= query_pos[:, None]
    kept = (key_pos[None, :] >= offset) | (key_pos[None, :] == query_pos[:, None])
    bias = jnp.where(earlier & kept, 0.0, masked_fill).astype(jnp.float32).T
    dq, dk_local, dv_local, dk_prev, dv_prev, dk_suffix, dv_suffix = attend(
        queries[0], out_grad[0], keys[0], values[0], prev_kv, suffix_block, bias, kv_heads, group, suffix_len
    )
    back_k = passed_along(dk_prev, "ctx", -1)
    back_v = passed_along(dv_prev, "ctx", -1)
    suffix_dkv = jnp.concatenate([dk_suffix, dv_suffix], axis=1)
    summed_dkv = suffix_dkv + swapped(suffix_dkv, "ctx")
    local_ids = jnp.arange(own_slots, dtype=jnp.int32)
    pair_ids = jnp.arange(2, dtype=jnp.int32)
    collected = None
    for step in range(owners // 2):
        target = (owner_rank + 2 * step) % owners
        wanted = picked == ((target ^ pair_ids)[:, None] * own_slots + local_ids[None, :])
        sent = jnp.where(wanted[:, :, None, None], summed_dkv[None, None], 0.0)
        if step:
            sent = shifted(sent, "dp", 2 * step)
        collected = sent if collected is None else collected + sent
    slot_total = collected[0] + swapped(collected[1], "dp")
    key_full = key_weight.astype(jnp.float32)
    value_full = value_weight.astype(jnp.float32)
    suffix_grad = jnp.einsum(
        "slk,dk->sld", slot_total[:, :, :kv_width], key_full, precision=lax.Precision.HIGHEST
    )
    suffix_grad = suffix_grad + jnp.einsum(
        "slk,dk->sld", slot_total[:, :, kv_width:], value_full, precision=lax.Precision.HIGHEST
    )
    key_grad = (dk_local + back_k).astype(jnp.bfloat16)[None]
    value_grad = (dv_local + back_v).astype(jnp.bfloat16)[None]
    return (dq[None], key_grad, value_grad, suffix_grad)


def solution(mesh):
    return jax.shard_map(
        per_device,
        mesh=mesh,
        in_specs=(
            P(("groups", "dp"), "ctx", None),
            P(("groups", "dp"), "ctx", None),
            P(("groups", "dp"), "ctx", None),
            P(("groups", "dp"), "ctx", None),
            P("ctx", None),
            P("ctx", None),
            P(("groups", "dp"), None, "ctx"),
            P(("groups", "dp")),
            P("groups"),
            P(("groups", "dp")),
            P(("groups", "dp"), None),
        ),
        out_specs=(
            P(("groups", "dp"), "ctx", None),
            P(("groups", "dp"), "ctx", None),
            P(("groups", "dp"), "ctx", None),
            P(("groups", "dp"), None, "ctx"),
        ),
        check_vma=False,
    )
```

```python
import functools
import jax
import jax.numpy as jnp
from jax import lax
from jax.experimental import pallas as pl
from jax.experimental.pallas import tpu as pltpu
from jax.sharding import PartitionSpec as P

HEAD_DIM = 128
masked_fill = -1e30


def passed_along(block, axis, distance):
    devices = range(lax.axis_size(axis))
    route = [(i - distance, i) for i in devices if i - distance in devices]
    return lax.ppermute(block, axis, route)


def swapped(block, axis):
    devices = range(lax.axis_size(axis))
    route = [(i, i ^ 1) for i in devices]
    return lax.ppermute(block, axis, route)


def shifted(block, axis, distance):
    devices = range(lax.axis_size(axis))
    route = [(i, (i + distance) % len(devices)) for i in devices]
    return lax.ppermute(block, axis, route)


def paired_gather(block, axis):
    size = lax.axis_size(axis)
    pair = jnp.stack([block, swapped(block, axis)])
    return jnp.stack([pair] + [shifted(pair, axis, 2 * step) for step in range(1, size // 2)])


def attention_kernel(
    q_ref, do_ref, kl_ref, vl_ref, k_ref, v_ref, ks_ref, vs_ref, bias_ref,
    dq_ref, dk_local_ref, dv_local_ref, dk_prev_ref, dv_prev_ref, dk_suffix_ref, dv_suffix_ref,
    *, scale, tok_rows, suffix_len, group,
):
    k = jnp.concatenate([kl_ref[...], k_ref[...], ks_ref[...]], axis=0)
    v = jnp.concatenate([vl_ref[...], v_ref[...], vs_ref[...]], axis=0)
    k_t = k.astype(jnp.float32).T.astype(jnp.bfloat16)
    v_t = v.astype(jnp.float32).T.astype(jnp.bfloat16)
    bias = bias_ref[...]
    nt = (((1,), (1,)), ((), ()))
    key_total = None
    value_total = None
    for member in range(group):
        cols = slice(member * HEAD_DIM, (member + 1) * HEAD_DIM)
        q = q_ref[:, cols]
        grad = do_ref[:, cols]
        scores = lax.dot_general(k, q, nt, preferred_element_type=jnp.float32) * scale + bias
        row_max = jnp.max(scores, axis=0, keepdims=True)
        expo = jnp.exp(scores - row_max)
        total = jnp.sum(expo, axis=0, keepdims=True)
        inverse = 1.0 / total
        mixed = jnp.dot(v_t, expo.astype(jnp.bfloat16), preferred_element_type=jnp.float32)
        attended = (mixed * inverse).astype(jnp.bfloat16)
        grad_t = grad.astype(jnp.float32).T
        delta = jnp.sum(grad_t * attended.astype(jnp.float32), axis=0, keepdims=True)
        probs = expo * inverse
        prob_grad = lax.dot_general(v, grad, nt, preferred_element_type=jnp.float32)
        score_grad = (probs * (prob_grad - delta)).astype(jnp.bfloat16)
        query_piece = jnp.dot(k_t, score_grad, preferred_element_type=jnp.float32)
        dq_ref[:, cols] = (query_piece.T * scale).astype(dq_ref.dtype)
        key_piece = jnp.dot(score_grad, q, preferred_element_type=jnp.float32) * scale
        value_piece = jnp.dot(probs.astype(jnp.bfloat16), grad, preferred_element_type=jnp.float32)
        key_total = key_piece if key_total is None else key_total + key_piece
        value_total = value_piece if value_total is None else value_total + value_piece
    dk_local_ref[...] = key_total[:tok_rows]
    dv_local_ref[...] = value_total[:tok_rows]
    dk_prev_ref[...] = key_total[tok_rows : 2 * tok_rows]
    dv_prev_ref[...] = value_total[tok_rows : 2 * tok_rows]
    dk_suffix_ref[...] = key_total[2 * tok_rows : 2 * tok_rows + suffix_len]
    dv_suffix_ref[...] = value_total[2 * tok_rows : 2 * tok_rows + suffix_len]


def attend(queries2d, grads2d, keys2d, values2d, prev_kv, suffix_block, bias, kv_heads, group, suffix_len):
    tok_rows = queries2d.shape[0]
    n_keys = keys2d.shape[0] + prev_kv.shape[0] + suffix_block.shape[0]
    n_prompt = prev_kv.shape[0]
    n_suffix = suffix_block.shape[0]
    scale = HEAD_DIM ** (-0.5)
    kernel = functools.partial(
        attention_kernel, scale=scale, tok_rows=tok_rows, suffix_len=suffix_len, group=group
    )
    row_spec = pl.BlockSpec((tok_rows, group * HEAD_DIM), lambda h: (0, h))
    head_spec = pl.BlockSpec((tok_rows, HEAD_DIM), lambda h: (0, h))
    suffix_spec = pl.BlockSpec((suffix_len, HEAD_DIM), lambda h: (0, h))
    width = kv_heads * HEAD_DIM
    return pl.pallas_call(
        kernel,
        grid=(kv_heads,),
        in_specs=[
            row_spec,
            row_spec,
            pl.BlockSpec((tok_rows, HEAD_DIM), lambda h: (0, h)),
            pl.BlockSpec((tok_rows, HEAD_DIM), lambda h: (0, h)),
            pl.BlockSpec((n_prompt, HEAD_DIM), lambda h: (0, h)),
            pl.BlockSpec((n_prompt, HEAD_DIM), lambda h: (0, kv_heads + h)),
            pl.BlockSpec((n_suffix, HEAD_DIM), lambda h: (0, h)),
            pl.BlockSpec((n_suffix, HEAD_DIM), lambda h: (0, kv_heads + h)),
            pl.BlockSpec((n_keys, tok_rows), lambda h: (0, 0)),
        ],
        out_specs=[row_spec, head_spec, head_spec, head_spec, head_spec, suffix_spec, suffix_spec],
        out_shape=[jax.ShapeDtypeStruct(queries2d.shape, jnp.bfloat16)]
        + [jax.ShapeDtypeStruct((tok_rows, width), jnp.float32)] * 4
        + [jax.ShapeDtypeStruct((suffix_len, width), jnp.float32)] * 2,
        compiler_params=pltpu.CompilerParams(dimension_semantics=("arbitrary",)),
        cost_estimate=pl.CostEstimate(
            flops=12 * tok_rows * n_keys * HEAD_DIM * kv_heads * group,
            transcendentals=tok_rows * n_keys * kv_heads * group,
            bytes_accessed=6 * queries2d.size + 2 * n_keys * 2 * width + 4 * bias.size + 16 * tok_rows * width,
        ),
    )(queries2d, grads2d, keys2d, values2d, prev_kv, prev_kv, suffix_block, suffix_block, bias)


def per_device(
    queries,
    keys,
    values,
    out_grad,
    key_weight,
    value_weight,
    suffix_embed,
    class_ids,
    class_slot,
    pad_offset,
    suffix_pos,
):
    cycle_size = lax.axis_size("ctx")
    cycle_rank = lax.axis_index("ctx")
    owners = lax.axis_size("dp")
    owner_rank = lax.axis_index("dp")
    tok_rows = queries.shape[1]
    kv_width = keys.shape[2]
    kv_heads = kv_width // HEAD_DIM
    group = queries.shape[2] // kv_width
    own_slots = suffix_embed.shape[0]
    suffix_len = suffix_embed.shape[1]
    classes = class_slot.shape[0]
    slot_ids = jnp.arange(classes, dtype=jnp.int32)
    picked = jnp.sum(jnp.where(slot_ids == class_ids[0], class_slot, 0))
    owned_kv = jnp.concatenate(
        [
            jnp.einsum("sld,dk->slk", suffix_embed, key_weight, preferred_element_type=jnp.float32),
            jnp.einsum("sld,dk->slk", suffix_embed, value_weight, preferred_element_type=jnp.float32),
        ],
        axis=2,
    )
    owner = picked // own_slots
    partner = (owner_rank ^ owner) & 1
    source_step = ((owner_rank - (owner ^ partner)) % owners) // 2
    pair = jnp.stack([owned_kv, swapped(owned_kv, "dp")])
    pair, keys, values, pad_offset, suffix_pos = lax.optimization_barrier(
        (pair, keys, values, pad_offset, suffix_pos)
    )
    gathered_pairs = jnp.stack(
        [pair] + [shifted(pair, "dp", 2 * step) for step in range(1, owners // 2)]
    )
    half_kv = gathered_pairs[source_step, partner, picked % own_slots]
    suffix_kv = (half_kv + swapped(half_kv, "ctx")).astype(jnp.bfloat16)
    query_pos = cycle_rank * tok_rows + jnp.arange(tok_rows, dtype=jnp.int32)
    offset = pad_offset[0]
    local_kv = jnp.concatenate([keys[0], values[0]], axis=1)
    prev_kv = passed_along(local_kv, "ctx", 1)
    pad_rows = (-suffix_len) % 8
    suffix_block = jnp.concatenate(
        [suffix_kv, jnp.zeros((pad_rows, 2 * kv_width), jnp.bfloat16)], axis=0
    )
    rows = jnp.arange(tok_rows, dtype=jnp.int32)
    far = jnp.full((pad_rows,), 1 << 30, jnp.int32)
    key_pos = jnp.concatenate(
        [
            cycle_rank * tok_rows + rows,
            ((cycle_rank - 1) % cycle_size) * tok_rows + rows,
            suffix_pos[0],
            far,
        ]
    )
    earlier = key_pos[None, :] <= query_pos[:, None]
    kept = (key_pos[None, :] >= offset) | (key_pos[None, :] == query_pos[:, None])
    bias = jnp.where(earlier & kept, 0.0, masked_fill).astype(jnp.float32).T
    dq, dk_local, dv_local, dk_prev, dv_prev, dk_suffix, dv_suffix = attend(
        queries[0], out_grad[0], keys[0], values[0], prev_kv, suffix_block, bias, kv_heads, group, suffix_len
    )
    back_k = passed_along(dk_prev, "ctx", -1)
    back_v = passed_along(dv_prev, "ctx", -1)
    suffix_dkv = jnp.concatenate([dk_suffix, dv_suffix], axis=1)
    summed_dkv = suffix_dkv + swapped(suffix_dkv, "ctx")
    local_ids = jnp.arange(own_slots, dtype=jnp.int32)
    pair_ids = jnp.arange(2, dtype=jnp.int32)
    collected = None
    for step in range(owners // 2):
        target = (owner_rank + 2 * step) % owners
        wanted = picked == ((target ^ pair_ids)[:, None] * own_slots + local_ids[None, :])
        sent = jnp.where(wanted[:, :, None, None], summed_dkv[None, None], 0.0)
        if step:
            sent = shifted(sent, "dp", 2 * step)
        collected = sent if collected is None else collected + sent
    slot_total = collected[0] + swapped(collected[1], "dp")
    key_full = key_weight.astype(jnp.float32)
    value_full = value_weight.astype(jnp.float32)
    suffix_grad = jnp.einsum(
        "slk,dk->sld", slot_total[:, :, :kv_width], key_full, precision=lax.Precision.HIGHEST
    )
    suffix_grad = suffix_grad + jnp.einsum(
        "slk,dk->sld", slot_total[:, :, kv_width:], value_full, precision=lax.Precision.HIGHEST
    )
    key_grad = (dk_local + back_k).astype(jnp.bfloat16)[None]
    value_grad = (dv_local + back_v).astype(jnp.bfloat16)[None]
    return (dq[None], key_grad, value_grad, suffix_grad)


def solution(mesh):
    return jax.shard_map(
        per_device,
        mesh=mesh,
        in_specs=(
            P(("groups", "dp"), "ctx", None),
            P(("groups", "dp"), "ctx", None),
            P(("groups", "dp"), "ctx", None),
            P(("groups", "dp"), "ctx", None),
            P("ctx", None),
            P("ctx", None),
            P(("groups", "dp"), None, "ctx"),
            P(("groups", "dp")),
            P("groups"),
            P(("groups", "dp")),
            P(("groups", "dp"), None),
        ),
        out_specs=(
            P(("groups", "dp"), "ctx", None),
            P(("groups", "dp"), "ctx", None),
            P(("groups", "dp"), "ctx", None),
            P(("groups", "dp"), None, "ctx"),
        ),
        check_vma=False,
    )
```

```python
import functools
import jax
import jax.numpy as jnp
from jax import lax
from jax.experimental import pallas as pl
from jax.experimental.pallas import tpu as pltpu
from jax.sharding import PartitionSpec as P

HEAD_DIM = 128
masked_fill = -1e30


def passed_along(block, axis, distance):
    devices = range(lax.axis_size(axis))
    route = [(i - distance, i) for i in devices if i - distance in devices]
    return lax.ppermute(block, axis, route)


def swapped(block, axis):
    devices = range(lax.axis_size(axis))
    route = [(i, i ^ 1) for i in devices]
    return lax.ppermute(block, axis, route)


def shifted(block, axis, distance):
    devices = range(lax.axis_size(axis))
    route = [(i, (i + distance) % len(devices)) for i in devices]
    return lax.ppermute(block, axis, route)


def paired_gather(block, axis):
    size = lax.axis_size(axis)
    pair = jnp.stack([block, swapped(block, axis)])
    return jnp.stack([pair] + [shifted(pair, axis, 2 * step) for step in range(1, size // 2)])


def attention_kernel(
    q_ref, do_ref, kl_ref, vl_ref, k_ref, v_ref, ks_ref, vs_ref, bias_ref,
    dq_ref, dk_local_ref, dv_local_ref, dk_prev_ref, dv_prev_ref, dk_suffix_ref, dv_suffix_ref,
    *, scale, tok_rows, suffix_len, group,
):
    k = jnp.concatenate([kl_ref[...], k_ref[...], ks_ref[...]], axis=0)
    v = jnp.concatenate([vl_ref[...], v_ref[...], vs_ref[...]], axis=0)
    k_t = k.astype(jnp.float32).T.astype(jnp.bfloat16)
    v_t = v.astype(jnp.float32).T.astype(jnp.bfloat16)
    bias = bias_ref[...].astype(jnp.float32)
    nt = (((1,), (1,)), ((), ()))
    key_total = None
    value_total = None
    for member in range(group):
        cols = slice(member * HEAD_DIM, (member + 1) * HEAD_DIM)
        q = q_ref[:, cols]
        grad = do_ref[:, cols]
        scores = lax.dot_general(k, q, nt, preferred_element_type=jnp.float32) * scale + bias
        row_max = jnp.max(scores, axis=0, keepdims=True)
        expo = jnp.exp(scores - row_max)
        total = jnp.sum(expo, axis=0, keepdims=True)
        inverse = 1.0 / total
        mixed = jnp.dot(v_t, expo.astype(jnp.bfloat16), preferred_element_type=jnp.float32)
        attended = (mixed * inverse).astype(jnp.bfloat16)
        grad_t = grad.astype(jnp.float32).T
        delta = jnp.sum(grad_t * attended.astype(jnp.float32), axis=0, keepdims=True)
        probs = expo * inverse
        prob_grad = lax.dot_general(v, grad, nt, preferred_element_type=jnp.float32)
        score_grad = (probs * (prob_grad - delta)).astype(jnp.bfloat16)
        query_piece = jnp.dot(k_t, score_grad, preferred_element_type=jnp.float32)
        dq_ref[:, cols] = (query_piece.T * scale).astype(dq_ref.dtype)
        key_piece = jnp.dot(score_grad, q, preferred_element_type=jnp.float32) * scale
        value_piece = jnp.dot(probs.astype(jnp.bfloat16), grad, preferred_element_type=jnp.float32)
        key_total = key_piece if key_total is None else key_total + key_piece
        value_total = value_piece if value_total is None else value_total + value_piece
    dk_local_ref[...] = key_total[:tok_rows]
    dv_local_ref[...] = value_total[:tok_rows]
    dk_prev_ref[...] = key_total[tok_rows : 2 * tok_rows]
    dv_prev_ref[...] = value_total[tok_rows : 2 * tok_rows]
    dk_suffix_ref[...] = key_total[2 * tok_rows : 2 * tok_rows + suffix_len]
    dv_suffix_ref[...] = value_total[2 * tok_rows : 2 * tok_rows + suffix_len]


def attend(queries2d, grads2d, keys2d, values2d, prev_kv, suffix_block, bias, kv_heads, group, suffix_len):
    tok_rows = queries2d.shape[0]
    n_keys = keys2d.shape[0] + prev_kv.shape[0] + suffix_block.shape[0]
    n_prompt = prev_kv.shape[0]
    n_suffix = suffix_block.shape[0]
    scale = HEAD_DIM ** (-0.5)
    kernel = functools.partial(
        attention_kernel, scale=scale, tok_rows=tok_rows, suffix_len=suffix_len, group=group
    )
    row_spec = pl.BlockSpec((tok_rows, group * HEAD_DIM), lambda h: (0, h))
    head_spec = pl.BlockSpec((tok_rows, HEAD_DIM), lambda h: (0, h))
    suffix_spec = pl.BlockSpec((suffix_len, HEAD_DIM), lambda h: (0, h))
    width = kv_heads * HEAD_DIM
    return pl.pallas_call(
        kernel,
        grid=(kv_heads,),
        in_specs=[
            row_spec,
            row_spec,
            pl.BlockSpec((tok_rows, HEAD_DIM), lambda h: (0, h)),
            pl.BlockSpec((tok_rows, HEAD_DIM), lambda h: (0, h)),
            pl.BlockSpec((n_prompt, HEAD_DIM), lambda h: (0, h)),
            pl.BlockSpec((n_prompt, HEAD_DIM), lambda h: (0, kv_heads + h)),
            pl.BlockSpec((n_suffix, HEAD_DIM), lambda h: (0, h)),
            pl.BlockSpec((n_suffix, HEAD_DIM), lambda h: (0, kv_heads + h)),
            pl.BlockSpec((n_keys, tok_rows), lambda h: (0, 0)),
        ],
        out_specs=[row_spec, head_spec, head_spec, head_spec, head_spec, suffix_spec, suffix_spec],
        out_shape=[jax.ShapeDtypeStruct(queries2d.shape, jnp.bfloat16)]
        + [jax.ShapeDtypeStruct((tok_rows, width), jnp.float32)] * 4
        + [jax.ShapeDtypeStruct((suffix_len, width), jnp.float32)] * 2,
        compiler_params=pltpu.CompilerParams(dimension_semantics=("arbitrary",)),
        cost_estimate=pl.CostEstimate(
            flops=12 * tok_rows * n_keys * HEAD_DIM * kv_heads * group,
            transcendentals=tok_rows * n_keys * kv_heads * group,
            bytes_accessed=6 * queries2d.size + 2 * n_keys * 2 * width + 4 * bias.size + 16 * tok_rows * width,
        ),
    )(queries2d, grads2d, keys2d, values2d, prev_kv, prev_kv, suffix_block, suffix_block, bias)


def per_device(
    queries,
    keys,
    values,
    out_grad,
    key_weight,
    value_weight,
    suffix_embed,
    class_ids,
    class_slot,
    pad_offset,
    suffix_pos,
):
    cycle_size = lax.axis_size("ctx")
    cycle_rank = lax.axis_index("ctx")
    owners = lax.axis_size("dp")
    owner_rank = lax.axis_index("dp")
    tok_rows = queries.shape[1]
    kv_width = keys.shape[2]
    kv_heads = kv_width // HEAD_DIM
    group = queries.shape[2] // kv_width
    own_slots = suffix_embed.shape[0]
    suffix_len = suffix_embed.shape[1]
    classes = class_slot.shape[0]
    slot_ids = jnp.arange(classes, dtype=jnp.int32)
    picked = jnp.sum(jnp.where(slot_ids == class_ids[0], class_slot, 0))
    owned_kv = jnp.concatenate(
        [
            jnp.einsum("sld,dk->slk", suffix_embed, key_weight, preferred_element_type=jnp.float32),
            jnp.einsum("sld,dk->slk", suffix_embed, value_weight, preferred_element_type=jnp.float32),
        ],
        axis=2,
    )
    owner = picked // own_slots
    partner = (owner_rank ^ owner) & 1
    source_step = ((owner_rank - (owner ^ partner)) % owners) // 2
    pair = jnp.stack([owned_kv, swapped(owned_kv, "dp")])
    pair, keys, values, pad_offset, suffix_pos = lax.optimization_barrier(
        (pair, keys, values, pad_offset, suffix_pos)
    )
    gathered_pairs = jnp.stack(
        [pair] + [shifted(pair, "dp", 2 * step) for step in range(1, owners // 2)]
    )
    half_kv = gathered_pairs[source_step, partner, picked % own_slots]
    suffix_kv = (half_kv + swapped(half_kv, "ctx")).astype(jnp.bfloat16)
    query_pos = cycle_rank * tok_rows + jnp.arange(tok_rows, dtype=jnp.int32)
    offset = pad_offset[0]
    local_kv = jnp.concatenate([keys[0], values[0]], axis=1)
    prev_kv = passed_along(local_kv, "ctx", 1)
    pad_rows = (-suffix_len) % 16
    suffix_block = jnp.concatenate(
        [suffix_kv, jnp.zeros((pad_rows, 2 * kv_width), jnp.bfloat16)], axis=0
    )
    rows = jnp.arange(tok_rows, dtype=jnp.int32)
    far = jnp.full((pad_rows,), 1 << 30, jnp.int32)
    key_pos = jnp.concatenate(
        [
            cycle_rank * tok_rows + rows,
            ((cycle_rank - 1) % cycle_size) * tok_rows + rows,
            suffix_pos[0],
            far,
        ]
    )
    earlier = key_pos[None, :] <= query_pos[:, None]
    kept = (key_pos[None, :] >= offset) | (key_pos[None, :] == query_pos[:, None])
    bias = jnp.where(earlier & kept, 0.0, masked_fill).astype(jnp.bfloat16).T
    dq, dk_local, dv_local, dk_prev, dv_prev, dk_suffix, dv_suffix = attend(
        queries[0], out_grad[0], keys[0], values[0], prev_kv, suffix_block, bias, kv_heads, group, suffix_len
    )
    back_k = passed_along(dk_prev, "ctx", -1)
    back_v = passed_along(dv_prev, "ctx", -1)
    suffix_dkv = jnp.concatenate([dk_suffix, dv_suffix], axis=1)
    summed_dkv = suffix_dkv + swapped(suffix_dkv, "ctx")
    local_ids = jnp.arange(own_slots, dtype=jnp.int32)
    pair_ids = jnp.arange(2, dtype=jnp.int32)
    collected = None
    for step in range(owners // 2):
        target = (owner_rank + 2 * step) % owners
        wanted = picked == ((target ^ pair_ids)[:, None] * own_slots + local_ids[None, :])
        sent = jnp.where(wanted[:, :, None, None], summed_dkv[None, None], 0.0)
        if step:
            sent = shifted(sent, "dp", 2 * step)
        collected = sent if collected is None else collected + sent
    slot_total = collected[0] + swapped(collected[1], "dp")
    key_full = key_weight.astype(jnp.float32)
    value_full = value_weight.astype(jnp.float32)
    suffix_grad = jnp.einsum(
        "slk,dk->sld", slot_total[:, :, :kv_width], key_full, precision=lax.Precision.HIGHEST
    )
    suffix_grad = suffix_grad + jnp.einsum(
        "slk,dk->sld", slot_total[:, :, kv_width:], value_full, precision=lax.Precision.HIGHEST
    )
    key_grad = (dk_local + back_k).astype(jnp.bfloat16)[None]
    value_grad = (dv_local + back_v).astype(jnp.bfloat16)[None]
    return (dq[None], key_grad, value_grad, suffix_grad)


def solution(mesh):
    return jax.shard_map(
        per_device,
        mesh=mesh,
        in_specs=(
            P(("groups", "dp"), "ctx", None),
            P(("groups", "dp"), "ctx", None),
            P(("groups", "dp"), "ctx", None),
            P(("groups", "dp"), "ctx", None),
            P("ctx", None),
            P("ctx", None),
            P(("groups", "dp"), None, "ctx"),
            P(("groups", "dp")),
            P("groups"),
            P(("groups", "dp")),
            P(("groups", "dp"), None),
        ),
        out_specs=(
            P(("groups", "dp"), "ctx", None),
            P(("groups", "dp"), "ctx", None),
            P(("groups", "dp"), "ctx", None),
            P(("groups", "dp"), None, "ctx"),
        ),
        check_vma=False,
    )
```
